32 devices in a mesh: gx: 8 (over z, core), gy: 4 (over y, x).
Axes of the slice: x: 2, y: 2, z: 4, core: 2. Of those that a mesh axis runs over, the one named last changes fastest.
Arguments:
- tokens_in: bfloat16 [2048, 8192], P('gy', 'gx'), may hold values from -230 to 230, as said below
- norm_gain: bfloat16 [8192], replicated, may hold values from 0.099609375 to 1.8984375
- query_weight: bfloat16 [8192, 2048], P('gy', 'gx'), may hold values from -0.044194174 to 0.044194174
- key_weight: bfloat16 [8192, 256], P('gy', 'gx'), may hold values from -1.08275726 to 1.08275726
- value_weight: bfloat16 [8192, 256], P('gy', 'gx'), may hold values from -0.0625 to 0.0625
- segment_ids: int32 [2048], P('gy'), may hold values from -1 to 389, as said below
- positions: int32 [2048], P('gy'), may hold values from 0 to 511, as said below
- page_owner: int32 [128, 1], P('gy'), may hold values from 0 to 3; in each aligned block of 32 rows (0 to 31, 32 to 63, ...) at most 16 rows name the same one
Outputs:
- context: bfloat16 [2048, 2048], P('gy', 'gx')
- key_cache: bfloat16 [256, 16, 256], P('gy', None, 'gx')
- value_cache: bfloat16 [256, 16, 256], P('gy', None, 'gx')
The draws below stay inside these ranges and needn't reach their ends.
Inputs may be any that keep to these rules, and one draw needn't show every extreme that they name: `tokens_in`: activations with row and column scales. `segment_ids`: two requests are prompts of exactly 512 tokens, one starting in the first half of the stream and one in the second; every other request has 16 to 64 consecutive tokens; padding tokens have -1. The tokens of a request are consecutive. Inside a request, positions rise by one from token to token; padding has 0. `page_owner`: among the 32 pages of one index of gy, at most 16 have the same owner.
All inputs are finite; a program needn't handle non-finite values.
Results may differ from the reference program's by a relative error of at most 0.006.
The reference program's roundings to bfloat16 on the way (of `normed`, `queries`, `rotated_keys` and `weights`) count: a program that leaves them out, or rounds other values in their place, can miss the bound.
Values may be sent and summed in bfloat16 or wider, within the bound.
No kernel may reach another device: no remote copies, remote signals or barrier semaphores. Data moves between devices by JAX's collectives and lax.ppermute only.
A program may use at most 64 MiB of HBM per device.

```python
import math
import jax
import jax.numpy as jnp
import numpy as np
from jax import lax

D = 8192
HD = 128
GROUP = 8
PAGE = 16
TOK_DEV = 512
NH = 16
KVH = 2
TOKENS = 2048
SPAN = 1
PROMPT = 512
PPD = 32
CAP = 16
SLOTS = 256
N_GY = 4


def draw_tokens_in(key, part):
    seed_key = jax.random.fold_in(key, 11)
    normal_key, row_key, column_key = jax.random.split(seed_key, 3)
    standard = jax.random.truncated_normal(normal_key, -4.0, 4.0, (TOKENS, D), jnp.float32)
    row_scale = jnp.exp(jax.random.uniform(row_key, (TOKENS, 1), jnp.float32) * math.log(10.0))
    column_scale = 0.5 * jnp.exp(jax.random.uniform(column_key, (1, D), jnp.float32) * math.log(10.0))
    return (standard * row_scale * column_scale).astype(jnp.bfloat16)


def weight_pair(key):
    pair_key = jax.random.fold_in(key, 23)
    query_key, other_key = jax.random.split(pair_key, 2)
    query_draw = jax.random.truncated_normal(query_key, -4.0, 4.0, (D, NH * HD), jnp.float32) * D ** (-0.5)
    key_draw = jax.random.truncated_normal(other_key, -4.0, 4.0, (D, KVH * HD), jnp.float32) * D ** (-0.5)
    return (query_draw, key_draw)


def draw_query_weight(key, part):
    return weight_pair(key)[0].astype(jnp.bfloat16)


def draw_key_weight(key, part):
    return weight_pair(key)[1].astype(jnp.bfloat16)


def stream_layout(key):
    layout_key = jax.random.fold_in(key, 37)
    device_key, offset_key, length_key, prior_key = jax.random.split(layout_key, 4)
    device_total = TOKENS // TOK_DEV
    half_devices = device_total // 2
    span_devices = PROMPT // TOK_DEV
    start_devices = jax.random.randint(device_key, (2,), 0, half_devices - span_devices)
    offsets = jax.random.randint(offset_key, (2,), 1, TOK_DEV)
    first_start = start_devices[0] * TOK_DEV + offsets[0]
    second_start = (half_devices + start_devices[1]) * TOK_DEV + offsets[1]
    first_end = first_start + PROMPT
    second_end = second_start + PROMPT
    request_most = TOKENS // 16 + 1
    lengths = jax.random.randint(length_key, (3, request_most), 16, 65)
    bounds = jnp.cumsum(lengths, axis=1)
    prior_len = jax.random.randint(prior_key, (3, request_most), 0, PROMPT - 63)
    places = jnp.arange(TOKENS, dtype=jnp.int32)
    in_first = (places >= first_start) & (places < first_end)
    in_second = (places >= second_start) & (places < second_end)
    gap_index = jnp.where(places < first_start, 0, jnp.where(places < second_start, 1, 2))
    gap_start = jnp.where(gap_index == 0, 0, jnp.where(gap_index == 1, first_end, second_end))
    gap_end = jnp.where(gap_index == 0, first_start, jnp.where(gap_index == 1, second_start, TOKENS))
    offset_in = places - gap_start
    gap_bounds = bounds[gap_index]
    request = jnp.sum((gap_bounds <= offset_in[:, None]).astype(jnp.int32), axis=1)
    request_end = jnp.take_along_axis(gap_bounds, request[:, None], axis=1)[:, 0]
    request_length = jnp.take_along_axis(lengths[gap_index], request[:, None], axis=1)[:, 0]
    request_start = request_end - request_length
    complete = gap_start + request_end <= gap_end
    second_id = 2 + 3 * request_most
    segment = jnp.where(in_first, 0, jnp.where(in_second, second_id, jnp.where(complete, 2 + gap_index * request_most + request, -1)))
    request_prior = jnp.take_along_axis(prior_len[gap_index], request[:, None], axis=1)[:, 0]
    position_of = jnp.where(in_first, places - first_start, jnp.where(in_second, places - second_start, jnp.where(complete, request_prior + offset_in - request_start, 0)))
    return (segment.astype(jnp.int32), position_of.astype(jnp.int32))


def draw_segment_ids(key, part):
    return stream_layout(key)[0]


def draw_positions(key, part):
    return stream_layout(key)[1]


def block_levels(stream_key, dims, shards, least, largest):
    gain, own = 1.0, jax.random.fold_in(stream_key, 6)
    for position, shards_of in shards:
        draws = jnp.exp(jax.random.uniform(jax.random.fold_in(own, position), (shards_of,), jnp.float32, least / len(shards), largest / len(shards)))
        gain = gain * jnp.repeat(draws, dims[position] // shards_of).reshape([-1 if axis == position else 1 for axis in range(len(dims))])
    return gain


def deal_out(stream_key, own, number, rows, count, top, reach, lean):
    sequence = jax.random.permutation(stream_key, count)
    heavy_load, ordinary = portions_of(count, rows * top, reach, lean, True), portions_of(count, rows * top, reach, lean, False)
    places = jnp.arange(count)

    def named(tallies, rotation):
        used = int((tallies > 0).sum())
        fixed = max(1, used // 4)
        moved = fixed + (places - fixed + rotation * (used - fixed)) % max(1, count - fixed)
        return jnp.zeros((count,), jnp.int32).at[sequence[jnp.where(places < fixed, places, moved)]].set(jnp.asarray(tallies, jnp.int32))

    tallies = jnp.where(number % 4 == 0, named(heavy_load, number // 4), named(ordinary, number - number // 4 - 1))
    mixed = jax.random.permutation(jax.random.fold_in(own, 3), count)
    giver, receiver = mixed[0:count // 2 * 2:2], mixed[1:count // 2 * 2:2]
    margin = jnp.minimum(tallies[giver] - 1, reach - tallies[receiver]) // 2
    margin = jnp.where((giver == sequence[0]) | (receiver == sequence[0]) | (tallies[receiver] == 0), 0, jnp.maximum(margin, 0))
    moved = jax.random.randint(jax.random.fold_in(own, 4), (count // 2,), 0, 1 << 20) % (margin + 1)
    tallies = tallies.at[giver].add(-moved).at[receiver].add(moved)
    members = jnp.searchsorted(jnp.cumsum(tallies), jnp.arange(rows * top), side="right").astype(jnp.int32)
    listing = members.reshape(top, rows).T
    listing = listing[jax.random.permutation(jax.random.fold_in(own, 1), rows)]
    rotation = jax.random.randint(jax.random.fold_in(own, 2), (rows, 1), 0, top)
    return jnp.take_along_axis(listing, (jnp.arange(top)[None, :] + rotation) % top, axis=1)


def portions_of(amount, total, most, slope, full):
    weights = [(1 << 20) // math.isqrt(grade ** slope) + 1 for grade in range(1, amount + 1)]
    largest = most if full else min(most, max(-(-total // amount), total * weights[0] // sum(weights)))
    least = 1 if total - largest >= amount - 1 else 0
    given, rest = [largest] + [least] * (amount - 1), total - largest - least * (amount - 1)
    while rest > 0:
        candidates = [i for i in range(1, amount) if given[i] < largest] or [i for i in range(1, amount) if given[i] < most]
        pool, left = sum([weights[i] for i in candidates]), rest
        for i in candidates:
            extra = min(most - given[i], max(1, left * weights[i] // pool), rest)
            given[i] = given[i] + extra
            rest = rest - extra
    return np.array(given)


def centred(key, extent, spread, limit, pieces=(), kind=jnp.bfloat16):
    entries = jax.random.normal(key, extent, jnp.float32) * spread
    if len(pieces) > 0:
        entries = block_levels(key, extent, pieces, -0.22, 0.18) * entries
    return jnp.clip(entries, min=-limit, max=limit).astype(kind)


def setup_inputs(seed: int = 0) -> dict:
    key_of = jax.random.split(jax.random.key(seed), 9)
    tokens_in = draw_tokens_in(jax.random.fold_in(key_of[8], 71), 0)
    norm_gain = jnp.clip(1.0 + 0.18 * jax.random.normal(key_of[1], (D,), jnp.float32), 0.099609375, 1.8984375).astype(jnp.bfloat16)
    query_weight = draw_query_weight(jax.random.fold_in(key_of[8], 71), 0)
    key_weight = draw_key_weight(jax.random.fold_in(key_of[8], 71), 0)
    value_weight = centred(key_of[4], (D, KVH * HD), D ** -0.5, 0.0625, ((0, 4), (1, 8)))
    segment_ids = draw_segment_ids(jax.random.fold_in(key_of[8], 71), 0)
    positions = draw_positions(jax.random.fold_in(key_of[8], 71), 0)
    page_owner_keys = jax.random.split(jax.random.fold_in(key_of[7], 1), (TOKENS // PAGE) // PPD)
    page_owner_turns = jax.random.permutation(jax.random.fold_in(key_of[7], 3), (TOKENS // PAGE) // PPD)
    page_owner = jax.vmap(lambda own, number: deal_out(jax.random.fold_in(key_of[7], 2), own, number, PPD, N_GY, 1, CAP, 2))(page_owner_keys, page_owner_turns).reshape((TOKENS // PAGE, 1))
    return dict(tokens_in=tokens_in, norm_gain=norm_gain, query_weight=query_weight, key_weight=key_weight, value_weight=value_weight, segment_ids=segment_ids, positions=positions, page_owner=page_owner)


EPSILON = 1e-05
THETA = 500000.0
MASKED = -1e+30

def rotate(matrix, places, group_width, first_pair):
    row_count = matrix.shape[0]
    pair_count = group_width // 2
    shaped = matrix.reshape(row_count, -1, pair_count, 2)
    pair_index = first_pair + jnp.arange(pair_count, dtype=jnp.int32)
    frequency = jnp.power(THETA, -(2.0 * pair_index.astype(jnp.float32)) / HD)
    angles = places.astype(jnp.float32)[:, None] * frequency[None, :]
    cosine = jnp.cos(angles)[:, None, :]
    sine_of = jnp.sin(angles)[:, None, :]
    even_part = shaped[..., 0]
    odd_part = shaped[..., 1]
    turned = jnp.stack([even_part * cosine - odd_part * sine_of, even_part * sine_of + odd_part * cosine], axis=-1)
    return turned.reshape(row_count, -1)

def reference(tokens_in, norm_gain, query_weight, key_weight, value_weight, segment_ids, positions, page_owner):
    inputs = tokens_in.astype(jnp.float32)
    scaling = 1.0 / jnp.sqrt(lax.optimization_barrier(jnp.mean(inputs * inputs, axis=1)) + EPSILON)
    normed = (inputs * norm_gain.astype(jnp.float32)[None, :]).astype(jnp.bfloat16)
    query_proj = jnp.dot(normed, query_weight, preferred_element_type=jnp.float32) * scaling[:, None]
    key_proj = jnp.dot(normed, key_weight, preferred_element_type=jnp.float32) * scaling[:, None]
    value_proj = jnp.dot(normed, value_weight, preferred_element_type=jnp.float32) * scaling[:, None]
    queries = rotate(query_proj, positions, HD, 0).astype(jnp.bfloat16)
    rotated_keys = rotate(key_proj, positions, HD, 0).astype(jnp.bfloat16)
    values = value_proj.astype(jnp.bfloat16)
    reach_rows = SPAN * TOK_DEV
    window = reach_rows + TOK_DEV
    padded_keys = jnp.concatenate([jnp.zeros((reach_rows, KVH * HD), jnp.bfloat16), rotated_keys], axis=0)
    padded_values = jnp.concatenate([jnp.zeros((reach_rows, KVH * HD), jnp.bfloat16), values], axis=0)
    padded_marks = jnp.concatenate([jnp.full((reach_rows,), -1, jnp.int32), segment_ids], axis=0)
    score_scale = HD ** (-0.5)

    def one_block(block_index):
        begin_at = (block_index * TOK_DEV).astype(jnp.int32)
        query_rows = lax.dynamic_slice_in_dim(queries, begin_at, TOK_DEV, 0).astype(jnp.float32)
        query_rows = query_rows.reshape(TOK_DEV, KVH, GROUP, HD)
        key_rows = lax.dynamic_slice_in_dim(padded_keys, begin_at, window, 0).astype(jnp.float32).reshape(window, KVH, HD)
        value_rows = lax.dynamic_slice_in_dim(padded_values, begin_at, window, 0).astype(jnp.float32).reshape(window, KVH, HD)
        query_marks = lax.dynamic_slice_in_dim(segment_ids, begin_at, TOK_DEV, 0)
        key_marks = lax.dynamic_slice_in_dim(padded_marks, begin_at, window, 0)
        scores = jnp.einsum('tgrd,ugd->grtu', query_rows, key_rows) * score_scale
        allowed = (query_marks[:, None] == key_marks[None, :]) & (key_marks[None, :] >= 0)
        allowed = allowed & (jnp.arange(window, dtype=jnp.int32)[None, :] <= jnp.arange(TOK_DEV, dtype=jnp.int32)[:, None] + reach_rows)
        masked = jnp.where(allowed[None, None], scores, MASKED)
        highest = lax.optimization_barrier(jnp.max(masked, axis=-1, keepdims=True))
        exponent = jnp.exp(masked - highest)
        totals = lax.optimization_barrier(jnp.sum(exponent, axis=-1))
        weights = lax.optimization_barrier(exponent.astype(jnp.bfloat16)).astype(jnp.float32)
        summed = jnp.einsum('grtu,ugd->grtd', weights, value_rows)
        result = summed / totals[..., None]
        result = jnp.where((query_marks >= 0)[None, None, :, None], result, 0.0)
        return result.transpose(2, 0, 1, 3).reshape(TOK_DEV, NH * HD).astype(jnp.bfloat16)
    blocks = lax.map(one_block, jnp.arange(N_GY, dtype=jnp.int32))
    context = blocks.reshape(TOKENS, NH * HD)
    page_count = TOKENS // PAGE
    owner_of = page_owner[:, 0]
    source = jnp.arange(page_count, dtype=jnp.int32) // PPD
    one_hot = (owner_of[:, None] == jnp.arange(N_GY, dtype=jnp.int32)[None, :]).astype(jnp.int32)
    one_hot = one_hot.reshape(N_GY, PPD, N_GY)
    earlier = jnp.cumsum(one_hot, axis=1) - one_hot
    rank_in = lax.optimization_barrier(jnp.sum(earlier * one_hot, axis=2)).reshape(page_count)
    slot_of = (owner_of * N_GY + source) * CAP + rank_in
    key_pages = rotated_keys.reshape(page_count, PAGE, KVH * HD)
    value_pages = values.reshape(page_count, PAGE, KVH * HD)
    key_cache = jnp.zeros((SLOTS, PAGE, KVH * HD), jnp.bfloat16).at[slot_of].set(key_pages)
    value_cache = jnp.zeros((SLOTS, PAGE, KVH * HD), jnp.bfloat16).at[slot_of].set(value_pages)
    return (context, key_cache, value_cache)
```

```python
import jax
import jax.numpy as jnp
from jax import lax
from jax.sharding import PartitionSpec as P

D = 8192
HD = 128
PAGE = 16


EPSILON = 1e-05
THETA = 500000.0
MASKED = -1e30


def shifted(value, axis, by):
    count = lax.axis_size(axis)
    pairs = [(i, i + by) for i in range(count) if 0 <= i + by < count]
    return lax.ppermute(value, axis, pairs)


def partner_route(count, group, k):
    route = []
    for i in range(count):
        base = i - i % group
        route.append((i, base + ((i % group) ^ k)))
    return route


def rotate(matrix, places, group_width, first_pair):
    row_count = matrix.shape[0]
    pair_count = group_width // 2
    shaped = matrix.reshape(row_count, -1, pair_count, 2)
    all_pairs = jnp.arange(HD // 2, dtype=jnp.int32)
    all_freq = jnp.power(THETA, -(2.0 * all_pairs.astype(jnp.float32)) / HD)
    frequency = lax.dynamic_slice_in_dim(all_freq, first_pair, pair_count, 0)
    angles = places.astype(jnp.float32)[:, None] * frequency[None, :]
    cosine = jnp.cos(angles)[:, None, :]
    sine_of = jnp.sin(angles)[:, None, :]
    even_part = shaped[..., 0]
    odd_part = shaped[..., 1]
    turned = jnp.stack(
        [even_part * cosine - odd_part * sine_of, even_part * sine_of + odd_part * cosine], axis=-1
    )
    return turned.reshape(row_count, -1)


def shards(
    tokens_in, norm_gain, query_weight, key_weight, value_weight, segment_ids, positions, page_owner
):
    token_count = tokens_in.shape[0]
    quarter = key_weight.shape[1]
    head_local = query_weight.shape[1] // HD
    quarters = HD // quarter
    gx_count = lax.axis_size("gx")
    gy_count = lax.axis_size("gy")
    spot = lax.axis_index("gx") % quarters
    my_gy = lax.axis_index("gy")
    row_block = query_weight.shape[0]

    local_weights = jnp.concatenate([query_weight, key_weight, value_weight], axis=1)
    pieces = [(my_gy, local_weights)]
    for k in range(1, gy_count):
        got = lax.ppermute(local_weights, "gy", partner_route(gy_count, gy_count, k))
        pieces.append((my_gy ^ k, got))

    gain_part = norm_gain.astype(jnp.float32)
    piece_float = lax.all_gather(tokens_in, "gx", axis=1, tiled=True).astype(jnp.float32)
    normed = (piece_float * gain_part[None, :]).astype(jnp.bfloat16)
    squares = jnp.sum(piece_float * piece_float, axis=1)
    products = None
    for source, block in pieces:
        rows = lax.dynamic_slice_in_dim(normed, source * row_block, row_block, 1)
        part = jnp.dot(rows, block, preferred_element_type=jnp.float32)
        products = part if products is None else products + part
    scaling = 1.0 / jnp.sqrt(squares / D + EPSILON)
    projected = products * scaling[:, None]
    query_cols = head_local * HD
    queries = rotate(projected[:, :query_cols], positions, HD, 0).astype(jnp.bfloat16)
    key_proj = projected[:, query_cols : query_cols + quarter]
    value_proj = projected[:, query_cols + quarter :]
    key_piece = rotate(key_proj, positions, quarter, spot * (quarter // 2)).astype(jnp.bfloat16)
    value_piece = value_proj.astype(jnp.bfloat16)

    own_kv = jnp.stack([key_piece, value_piece])
    kv_parts = [own_kv]
    for k in range(1, quarters):
        kv_parts.append(lax.ppermute(own_kv, "gx", partner_route(gx_count, quarters, k)))
    kv_stack = jnp.stack(kv_parts)
    order = jnp.arange(quarters, dtype=jnp.int32) ^ spot
    kv_full = jnp.take(kv_stack, order, axis=0)
    kv_full = kv_full.transpose(1, 2, 0, 3).reshape(2, token_count, HD)
    full_keys = kv_full[0]
    full_values = kv_full[1]

    span_count = gy_count // 4
    marks = segment_ids + 1
    key_list = [full_keys]
    value_list = [full_values]
    mark_list = [marks]
    for shift_by in range(1, span_count + 1):
        moved_keys, moved_values, moved_marks = shifted(
            (full_keys, full_values, marks), "gy", shift_by
        )
        key_list.insert(0, moved_keys)
        value_list.insert(0, moved_values)
        mark_list.insert(0, moved_marks)
    window_keys = jnp.concatenate(key_list, axis=0)
    window_values = jnp.concatenate(value_list, axis=0)
    window_marks = jnp.concatenate(mark_list, axis=0)
    reach_rows = span_count * token_count
    query_rows = (
        queries.reshape(token_count, head_local, HD)
        .transpose(1, 0, 2)
        .reshape(head_local * token_count, HD)
    )
    scores = lax.dot_general(
        query_rows, window_keys, (((1,), (1,)), ((), ())), preferred_element_type=jnp.float32
    ) * HD ** (-0.5)
    query_marks = jnp.tile(segment_ids, head_local)
    query_place = jnp.tile(jnp.arange(token_count, dtype=jnp.int32), head_local)
    key_place = jnp.arange(window_keys.shape[0], dtype=jnp.int32)
    allowed = (window_marks[None, :] == query_marks[:, None] + 1) & (window_marks[None, :] > 0)
    allowed = allowed & (key_place[None, :] <= query_place[:, None] + reach_rows)
    masked = jnp.where(allowed, scores, MASKED)
    highest = jnp.max(masked, axis=1, keepdims=True)
    exponent = jnp.exp(masked - highest)
    totals = jnp.sum(exponent, axis=1)
    weights = exponent.astype(jnp.bfloat16)
    summed = jnp.dot(weights, window_values, preferred_element_type=jnp.float32)
    result = summed / totals[:, None]
    result = jnp.where((query_marks >= 0)[:, None], result, 0.0)
    context = (
        result.reshape(head_local, token_count, HD)
        .transpose(1, 0, 2)
        .reshape(token_count, head_local * HD)
        .astype(jnp.bfloat16)
    )
    owner_count = gy_count
    page_rows = token_count // PAGE
    capacity = max(2, 2 * page_rows // owner_count)
    owner_of = page_owner[:, 0]
    one_hot = (owner_of[:, None] == jnp.arange(owner_count, dtype=jnp.int32)[None, :]).astype(
        jnp.int32
    )
    earlier = jnp.cumsum(one_hot, axis=0) - one_hot
    rank_in = jnp.sum(earlier * one_hot, axis=1)
    slot_of = owner_of * capacity + rank_in
    key_pages = key_piece.reshape(page_rows, PAGE * quarter)
    value_pages = value_piece.reshape(page_rows, PAGE * quarter)
    send_keys = (
        jnp.zeros((owner_count * capacity, PAGE * quarter), jnp.bfloat16).at[slot_of].set(key_pages)
    )
    send_values = (
        jnp.zeros((owner_count * capacity, PAGE * quarter), jnp.bfloat16)
        .at[slot_of]
        .set(value_pages)
    )
    send_keys = send_keys.reshape(owner_count, capacity, PAGE * quarter)
    send_values = send_values.reshape(owner_count, capacity, PAGE * quarter)
    got_keys, got_values = (
        lax.all_to_all(send_keys, "gy", split_axis=0, concat_axis=0, tiled=True),
        lax.all_to_all(send_values, "gy", split_axis=0, concat_axis=0, tiled=True),
    )
    key_cache = got_keys.reshape(owner_count * capacity, PAGE, quarter)
    value_cache = got_values.reshape(owner_count * capacity, PAGE, quarter)
    return (context, key_cache, value_cache)


def solution(mesh):
    placed = (
        P("gy", "gx"),
        P(),
        P("gy", "gx"),
        P("gy", "gx"),
        P("gy", "gx"),
        P("gy"),
        P("gy"),
        P("gy", None),
    )
    return jax.shard_map(
        shards,
        mesh=mesh,
        in_specs=placed,
        out_specs=(P("gy", "gx"), P("gy", None, "gx"), P("gy", None, "gx")),
        check_vma=False,
    )
```

```python
import jax
import jax.numpy as jnp
from jax import lax
from jax.sharding import PartitionSpec as P

D = 8192
HD = 128
PAGE = 16


EPSILON = 1e-05
THETA = 500000.0
MASKED = -1e30


def shifted(value, axis, by):
    count = lax.axis_size(axis)
    pairs = [(i, i + by) for i in range(count) if 0 <= i + by < count]
    return lax.ppermute(value, axis, pairs)


def partner_route(count, group, k):
    route = []
    for i in range(count):
        base = i - i % group
        route.append((i, base + ((i % group) ^ k)))
    return route


def rotate(matrix, places, group_width, first_pair):
    row_count = matrix.shape[0]
    pair_count = group_width // 2
    shaped = matrix.reshape(row_count, -1, pair_count, 2)
    all_pairs = jnp.arange(HD // 2, dtype=jnp.int32)
    all_freq = jnp.power(THETA, -(2.0 * all_pairs.astype(jnp.float32)) / HD)
    frequency = lax.dynamic_slice_in_dim(all_freq, first_pair, pair_count, 0)
    angles = places.astype(jnp.float32)[:, None] * frequency[None, :]
    cosine = jnp.cos(angles)[:, None, :]
    sine_of = jnp.sin(angles)[:, None, :]
    even_part = shaped[..., 0]
    odd_part = shaped[..., 1]
    turned = jnp.stack(
        [even_part * cosine - odd_part * sine_of, even_part * sine_of + odd_part * cosine], axis=-1
    )
    return turned.reshape(row_count, -1)


def shards(
    tokens_in, norm_gain, query_weight, key_weight, value_weight, segment_ids, positions, page_owner
):
    token_count = tokens_in.shape[0]
    quarter = key_weight.shape[1]
    head_local = query_weight.shape[1] // HD
    quarters = HD // quarter
    gx_count = lax.axis_size("gx")
    gy_count = lax.axis_size("gy")
    spot = lax.axis_index("gx") % quarters
    my_gy = lax.axis_index("gy")
    row_block = query_weight.shape[0]

    local_weights = jnp.concatenate([query_weight, key_weight, value_weight], axis=1)
    pieces = [(my_gy, local_weights)]
    for k in range(1, gy_count):
        got = lax.ppermute(local_weights, "gy", partner_route(gy_count, gy_count, k))
        pieces.append((my_gy ^ k, got))

    local_float = tokens_in.astype(jnp.float32)
    my_gx = lax.axis_index("gx")
    feature_block = tokens_in.shape[1]
    local_gain = lax.dynamic_slice_in_dim(norm_gain, my_gx * feature_block, feature_block, 0)
    local_normed = (local_float * local_gain.astype(jnp.float32)[None, :]).astype(jnp.bfloat16)
    local_squares = jnp.sum(local_float * local_float, axis=1)
    square_parts = [local_squares]
    for k in range(1, gx_count):
        square_parts.append(lax.ppermute(local_squares, "gx", partner_route(gx_count, gx_count, k)))
    square_order = jnp.arange(gx_count, dtype=jnp.int32) ^ my_gx
    squares = jnp.sum(jnp.take(jnp.stack(square_parts), square_order, axis=0), axis=0)
    normed = lax.all_gather(local_normed, "gx", axis=1, tiled=True)
    products = None
    for source, block in pieces:
        rows = lax.dynamic_slice_in_dim(normed, source * row_block, row_block, 1)
        part = jnp.dot(rows, block, preferred_element_type=jnp.float32)
        products = part if products is None else products + part
    scaling = 1.0 / jnp.sqrt(squares / D + EPSILON)
    projected = products * scaling[:, None]
    query_cols = head_local * HD
    queries = rotate(projected[:, :query_cols], positions, HD, 0).astype(jnp.bfloat16)
    key_proj = projected[:, query_cols : query_cols + quarter]
    value_proj = projected[:, query_cols + quarter :]
    key_piece = rotate(key_proj, positions, quarter, spot * (quarter // 2)).astype(jnp.bfloat16)
    value_piece = value_proj.astype(jnp.bfloat16)

    span_count = gy_count // 4
    marks = segment_ids + 1
    own_kv = jnp.stack([key_piece, value_piece])
    order = jnp.arange(quarters, dtype=jnp.int32) ^ spot

    def assembled(parts):
        stack = jnp.take(jnp.stack(parts), order, axis=0)
        return stack.transpose(1, 2, 0, 3).reshape(2, token_count, HD)

    here = [own_kv]
    for k in range(1, quarters):
        here.append(lax.ppermute(own_kv, "gx", partner_route(gx_count, quarters, k)))
    kv_blocks = [assembled(here)]
    mark_list = [marks]
    for shift_by in range(1, span_count + 1):
        earlier_parts = []
        for k in range(quarters):
            route = []
            for i in range(gx_count):
                peer = i - i % quarters + ((i % quarters) ^ k)
                for j in range(gy_count - shift_by):
                    route.append((i * gy_count + j, peer * gy_count + j + shift_by))
            earlier_parts.append(lax.ppermute(own_kv, ("gx", "gy"), route))
        kv_blocks.insert(0, assembled(earlier_parts))
        mark_list.insert(0, shifted(marks, "gy", shift_by))
    window_kv = jnp.concatenate(kv_blocks, axis=1)
    window_keys = window_kv[0]
    window_values = window_kv[1]
    window_marks = jnp.concatenate(mark_list, axis=0)
    reach_rows = span_count * token_count
    query_rows = (
        queries.reshape(token_count, head_local, HD)
        .transpose(1, 0, 2)
        .reshape(head_local * token_count, HD)
    )
    scores = lax.dot_general(
        query_rows, window_keys, (((1,), (1,)), ((), ())), preferred_element_type=jnp.float32
    ) * HD ** (-0.5)
    query_marks = jnp.tile(segment_ids, head_local)
    query_place = jnp.tile(jnp.arange(token_count, dtype=jnp.int32), head_local)
    key_place = jnp.arange(window_keys.shape[0], dtype=jnp.int32)
    allowed = (window_marks[None, :] == query_marks[:, None] + 1) & (window_marks[None, :] > 0)
    allowed = allowed & (key_place[None, :] <= query_place[:, None] + reach_rows)
    masked = jnp.where(allowed, scores, MASKED)
    highest = jnp.max(masked, axis=1, keepdims=True)
    exponent = jnp.exp(masked - highest)
    totals = jnp.sum(exponent, axis=1)
    weights = exponent.astype(jnp.bfloat16)
    summed = jnp.dot(weights, window_values, preferred_element_type=jnp.float32)
    result = summed / totals[:, None]
    result = jnp.where((query_marks >= 0)[:, None], result, 0.0)
    context = (
        result.reshape(head_local, token_count, HD)
        .transpose(1, 0, 2)
        .reshape(token_count, head_local * HD)
        .astype(jnp.bfloat16)
    )
    owner_count = gy_count
    page_rows = token_count // PAGE
    capacity = max(2, 2 * page_rows // owner_count)
    owner_of = page_owner[:, 0]
    one_hot = (owner_of[:, None] == jnp.arange(owner_count, dtype=jnp.int32)[None, :]).astype(
        jnp.int32
    )
    earlier = jnp.cumsum(one_hot, axis=0) - one_hot
    rank_in = jnp.sum(earlier * one_hot, axis=1)
    slot_of = owner_of * capacity + rank_in
    kv_pages = own_kv.reshape(2, page_rows, PAGE * quarter).transpose(1, 0, 2)
    send_kv = (
        jnp.zeros((owner_count * capacity, 2, PAGE * quarter), jnp.bfloat16)
        .at[slot_of]
        .set(kv_pages)
    )
    send_kv = send_kv.reshape(owner_count, capacity, 2, PAGE * quarter)
    got_kv = lax.all_to_all(send_kv, "gy", split_axis=0, concat_axis=0, tiled=True)
    got_kv = got_kv.reshape(owner_count * capacity, 2, PAGE, quarter)
    key_cache = got_kv[:, 0]
    value_cache = got_kv[:, 1]
    return (context, key_cache, value_cache)


def solution(mesh):
    placed = (
        P("gy", "gx"),
        P(),
        P("gy", "gx"),
        P("gy", "gx"),
        P("gy", "gx"),
        P("gy"),
        P("gy"),
        P("gy", None),
    )
    return jax.shard_map(
        shards,
        mesh=mesh,
        in_specs=placed,
        out_specs=(P("gy", "gx"), P("gy", None, "gx"), P("gy", None, "gx")),
        check_vma=False,
    )
```

```python
import jax
import jax.numpy as jnp
from jax import lax
from jax.sharding import PartitionSpec as P

D = 8192
HD = 128
PAGE = 16


EPSILON = 1e-05
THETA = 500000.0
MASKED = -1e30


def shifted(value, axis, by):
    count = lax.axis_size(axis)
    pairs = [(i, i + by) for i in range(count) if 0 <= i + by < count]
    return lax.ppermute(value, axis, pairs)


def partner_route(count, group, k):
    route = []
    for i in range(count):
        base = i - i % group
        route.append((i, base + ((i % group) ^ k)))
    return route


def rotate(matrix, places, group_width, first_pair):
    row_count = matrix.shape[0]
    pair_count = group_width // 2
    shaped = matrix.reshape(row_count, -1, pair_count, 2)
    all_pairs = jnp.arange(HD // 2, dtype=jnp.int32)
    all_freq = jnp.power(THETA, -(2.0 * all_pairs.astype(jnp.float32)) / HD)
    frequency = lax.dynamic_slice_in_dim(all_freq, first_pair, pair_count, 0)
    angles = places.astype(jnp.float32)[:, None] * frequency[None, :]
    cosine = jnp.cos(angles)[:, None, :]
    sine_of = jnp.sin(angles)[:, None, :]
    even_part = shaped[..., 0]
    odd_part = shaped[..., 1]
    turned = jnp.stack(
        [even_part * cosine - odd_part * sine_of, even_part * sine_of + odd_part * cosine], axis=-1
    )
    return turned.reshape(row_count, -1)


def shards(
    tokens_in, norm_gain, query_weight, key_weight, value_weight, segment_ids, positions, page_owner
):
    token_count = tokens_in.shape[0]
    quarter = key_weight.shape[1]
    head_local = query_weight.shape[1] // HD
    quarters = HD // quarter
    gx_count = lax.axis_size("gx")
    gy_count = lax.axis_size("gy")
    spot = lax.axis_index("gx") % quarters
    my_gy = lax.axis_index("gy")
    row_block = query_weight.shape[0]

    kv_weights = jnp.stack([key_weight, value_weight])
    kv_order = jnp.arange(quarters, dtype=jnp.int32) ^ spot
    kv_parts = [kv_weights]
    for k in range(1, quarters):
        kv_parts.append(lax.ppermute(kv_weights, "gx", partner_route(gx_count, quarters, k)))
    kv_full = jnp.take(jnp.stack(kv_parts), kv_order, axis=0)
    kv_full = kv_full.transpose(1, 2, 0, 3).reshape(2, row_block, HD)
    local_weights = jnp.concatenate([query_weight, kv_full[0], kv_full[1]], axis=1)

    pieces = [(my_gy, local_weights)]
    if gy_count == 4:
        from_one = lax.ppermute(local_weights, "gy", partner_route(4, 4, 1))
        from_two = lax.ppermute(local_weights, "gy", partner_route(4, 4, 2))
        half = row_block // 2
        far_low = lax.ppermute(from_two[:half], "gy", partner_route(4, 4, 1))
        far_high = lax.ppermute(from_one[half:], "gy", partner_route(4, 4, 2))
        pieces += [(my_gy ^ 1, from_one), (my_gy ^ 2, from_two)]
        pieces.append((my_gy ^ 3, jnp.concatenate([far_low, far_high], axis=0)))
    else:
        for k in range(1, gy_count):
            got = lax.ppermute(local_weights, "gy", partner_route(gy_count, gy_count, k))
            pieces.append((my_gy ^ k, got))
    all_rows = jnp.zeros((gy_count * row_block, local_weights.shape[1]), local_weights.dtype)
    for source, block in pieces:
        all_rows = lax.dynamic_update_slice_in_dim(all_rows, block, source * row_block, 0)

    local_float = tokens_in.astype(jnp.float32)
    my_gx = lax.axis_index("gx")
    feature_block = tokens_in.shape[1]
    local_gain = lax.dynamic_slice_in_dim(norm_gain, my_gx * feature_block, feature_block, 0)
    local_normed = (local_float * local_gain.astype(jnp.float32)[None, :]).astype(jnp.bfloat16)
    local_squares = jnp.sum(local_float * local_float, axis=1)
    square_parts = [local_squares]
    for k in range(1, gx_count):
        square_parts.append(lax.ppermute(local_squares, "gx", partner_route(gx_count, gx_count, k)))
    square_order = jnp.arange(gx_count, dtype=jnp.int32) ^ my_gx
    squares = jnp.sum(jnp.take(jnp.stack(square_parts), square_order, axis=0), axis=0)
    normed = lax.all_gather(local_normed, "gx", axis=1, tiled=True)
    products = jnp.dot(normed, all_rows, preferred_element_type=jnp.float32)
    scaling = 1.0 / jnp.sqrt(squares / D + EPSILON)
    projected = products * scaling[:, None]
    query_cols = head_local * HD
    queries = rotate(projected[:, :query_cols], positions, HD, 0).astype(jnp.bfloat16)
    key_proj = projected[:, query_cols : query_cols + HD]
    value_proj = projected[:, query_cols + HD :]
    full_keys = rotate(key_proj, positions, HD, 0).astype(jnp.bfloat16)
    full_values = value_proj.astype(jnp.bfloat16)
    key_piece = lax.dynamic_slice_in_dim(full_keys, spot * quarter, quarter, 1)
    value_piece = lax.dynamic_slice_in_dim(full_values, spot * quarter, quarter, 1)
    own_kv = jnp.stack([key_piece, value_piece])

    span_count = gy_count // 4
    marks = segment_ids + 1
    head_kv = jnp.stack([full_keys, full_values])
    kv_blocks = [head_kv]
    mark_list = [marks]
    for shift_by in range(1, span_count + 1):
        kv_blocks.insert(0, shifted(head_kv, "gy", shift_by))
        mark_list.insert(0, shifted(marks, "gy", shift_by))
    window_kv = jnp.concatenate(kv_blocks, axis=1)
    window_keys = window_kv[0]
    window_values = window_kv[1]
    window_marks = jnp.concatenate(mark_list, axis=0)
    reach_rows = span_count * token_count
    query_rows = (
        queries.reshape(token_count, head_local, HD)
        .transpose(1, 0, 2)
        .reshape(head_local * token_count, HD)
    )
    scores = lax.dot_general(
        query_rows, window_keys, (((1,), (1,)), ((), ())), preferred_element_type=jnp.float32
    ) * HD ** (-0.5)
    query_marks = jnp.tile(segment_ids, head_local)
    query_place = jnp.tile(jnp.arange(token_count, dtype=jnp.int32), head_local)
    key_place = jnp.arange(window_keys.shape[0], dtype=jnp.int32)
    allowed = (window_marks[None, :] == query_marks[:, None] + 1) & (window_marks[None, :] > 0)
    allowed = allowed & (key_place[None, :] <= query_place[:, None] + reach_rows)
    masked = jnp.where(allowed, scores, MASKED)
    highest = jnp.max(masked, axis=1, keepdims=True)
    exponent = jnp.exp(masked - highest)
    totals = jnp.sum(exponent, axis=1)
    weights = exponent.astype(jnp.bfloat16)
    summed = jnp.dot(weights, window_values, preferred_element_type=jnp.float32)
    result = summed / totals[:, None]
    result = jnp.where((query_marks >= 0)[:, None], result, 0.0)
    context = (
        result.reshape(head_local, token_count, HD)
        .transpose(1, 0, 2)
        .reshape(token_count, head_local * HD)
        .astype(jnp.bfloat16)
    )
    owner_count = gy_count
    page_rows = token_count // PAGE
    capacity = max(2, 2 * page_rows // owner_count)
    owner_of = page_owner[:, 0]
    one_hot = (owner_of[:, None] == jnp.arange(owner_count, dtype=jnp.int32)[None, :]).astype(
        jnp.int32
    )
    earlier = jnp.cumsum(one_hot, axis=0) - one_hot
    rank_in = jnp.sum(earlier * one_hot, axis=1)
    slot_of = owner_of * capacity + rank_in
    kv_pages = own_kv.reshape(2, page_rows, PAGE * quarter).transpose(1, 0, 2)
    send_kv = (
        jnp.zeros((owner_count * capacity, 2, PAGE * quarter), jnp.bfloat16)
        .at[slot_of]
        .set(kv_pages)
    )
    send_kv = send_kv.reshape(owner_count, capacity, 2, PAGE * quarter)
    got_kv = lax.all_to_all(send_kv, "gy", split_axis=0, concat_axis=0, tiled=True)
    got_kv = got_kv.reshape(owner_count * capacity, 2, PAGE, quarter)
    key_cache = got_kv[:, 0]
    value_cache = got_kv[:, 1]
    return (context, key_cache, value_cache)


def solution(mesh):
    placed = (
        P("gy", "gx"),
        P(),
        P("gy", "gx"),
        P("gy", "gx"),
        P("gy", "gx"),
        P("gy"),
        P("gy"),
        P("gy", None),
    )
    return jax.shard_map(
        shards,
        mesh=mesh,
        in_specs=placed,
        out_specs=(P("gy", "gx"), P("gy", None, "gx"), P("gy", None, "gx")),
        check_vma=False,
    )
```

```python
import jax
import jax.numpy as jnp
from jax import lax
from jax.sharding import PartitionSpec as P

D = 8192
HD = 128
PAGE = 16


EPSILON = 1e-05
THETA = 500000.0
MASKED = -1e30


def shifted(value, axis, by):
    count = lax.axis_size(axis)
    pairs = [(i, i + by) for i in range(count) if 0 <= i + by < count]
    return lax.ppermute(value, axis, pairs)


def partner_route(count, group, k):
    route = []
    for i in range(count):
        base = i - i % group
        route.append((i, base + ((i % group) ^ k)))
    return route


def rope(matrix, places, width, first_pair):
    cols = jnp.arange(matrix.shape[1], dtype=jnp.int32)
    pair_index = first_pair + (cols % width) // 2
    frequency = jnp.power(THETA, -(2.0 * pair_index.astype(jnp.float32)) / HD)
    angles = places.astype(jnp.float32)[:, None] * frequency[None, :]
    cosine = jnp.cos(angles)
    sine_of = jnp.sin(angles)
    following = jnp.roll(matrix, -1, axis=1)
    preceding = jnp.roll(matrix, 1, axis=1)
    even = (cols % 2 == 0)[None, :]
    return jnp.where(
        even, matrix * cosine - following * sine_of, matrix * cosine + preceding * sine_of
    )


def shards(
    tokens_in, norm_gain, query_weight, key_weight, value_weight, segment_ids, positions, page_owner
):
    token_count = tokens_in.shape[0]
    quarter = key_weight.shape[1]
    head_local = query_weight.shape[1] // HD
    quarters = HD // quarter
    gx_count = lax.axis_size("gx")
    gy_count = lax.axis_size("gy")
    my_gx = lax.axis_index("gx")
    my_gy = lax.axis_index("gy")
    spot = my_gx % quarters
    row_block = query_weight.shape[0]

    local_weights = jnp.concatenate([query_weight, key_weight, value_weight], axis=1)
    all_rows = jnp.zeros((gy_count * row_block, local_weights.shape[1]), local_weights.dtype)
    all_rows = lax.dynamic_update_slice_in_dim(all_rows, local_weights, my_gy * row_block, 0)
    for k in range(1, gy_count):
        got = lax.ppermute(local_weights, "gy", partner_route(gy_count, gy_count, k))
        all_rows = lax.dynamic_update_slice_in_dim(all_rows, got, (my_gy ^ k) * row_block, 0)

    local_float = tokens_in.astype(jnp.float32)
    feature_block = tokens_in.shape[1]
    local_gain = lax.dynamic_slice_in_dim(norm_gain, my_gx * feature_block, feature_block, 0)
    local_normed = (local_float * local_gain.astype(jnp.float32)[None, :]).astype(jnp.bfloat16)
    local_squares = jnp.sum(local_float * local_float, axis=1)
    square_parts = [local_squares]
    for k in range(1, gx_count):
        square_parts.append(lax.ppermute(local_squares, "gx", partner_route(gx_count, gx_count, k)))
    square_order = jnp.arange(gx_count, dtype=jnp.int32) ^ my_gx
    squares = jnp.sum(jnp.take(jnp.stack(square_parts), square_order, axis=0), axis=0)
    normed = lax.all_gather(local_normed, "gx", axis=1, tiled=True)
    products = jnp.dot(normed, all_rows, preferred_element_type=jnp.float32)
    scaling = 1.0 / jnp.sqrt(squares / D + EPSILON)
    projected = products * scaling[:, None]
    query_cols = head_local * HD
    key_piece = rope(
        projected[:, query_cols : query_cols + quarter], positions, quarter, spot * (quarter // 2)
    ).astype(jnp.bfloat16)
    value_piece = projected[:, query_cols + quarter :].astype(jnp.bfloat16)
    queries = rope(projected[:, :query_cols], positions, HD, 0).astype(jnp.bfloat16)
    own_kv = jnp.stack([key_piece, value_piece])

    span_count = gy_count // 4
    marks = segment_ids + 1
    kv_list = [own_kv]
    mark_list = [marks]
    for shift_by in range(1, span_count + 1):
        kv_list.insert(0, shifted(own_kv, "gy", shift_by))
        mark_list.insert(0, shifted(marks, "gy", shift_by))
    window_quarter = jnp.concatenate(kv_list, axis=1)
    window_rows = window_quarter.shape[1]
    sent = jnp.broadcast_to(window_quarter[None], (gx_count,) + window_quarter.shape)
    got = lax.all_to_all(sent, "gx", split_axis=0, concat_axis=0, tiled=True)
    group_start = my_gx - spot
    head_parts = lax.dynamic_slice_in_dim(got, group_start, quarters, 0)
    window_kv = head_parts.transpose(1, 2, 0, 3).reshape(2, window_rows, HD)
    window_keys = window_kv[0]
    window_values = window_kv[1]
    window_marks = jnp.concatenate(mark_list, axis=0)

    reach_rows = span_count * token_count
    query_rows = (
        queries.reshape(token_count, head_local, HD)
        .transpose(1, 0, 2)
        .reshape(head_local * token_count, HD)
    )
    scores = lax.dot_general(
        query_rows, window_keys, (((1,), (1,)), ((), ())), preferred_element_type=jnp.float32
    ) * HD ** (-0.5)
    query_marks = jnp.tile(segment_ids, head_local)
    query_place = jnp.tile(jnp.arange(token_count, dtype=jnp.int32), head_local)
    key_place = jnp.arange(window_rows, dtype=jnp.int32)
    allowed = (window_marks[None, :] == query_marks[:, None] + 1) & (window_marks[None, :] > 0)
    allowed = allowed & (key_place[None, :] <= query_place[:, None] + reach_rows)
    masked = jnp.where(allowed, scores, MASKED)
    highest = jnp.max(masked, axis=1, keepdims=True)
    exponent = jnp.exp(masked - highest)
    totals = jnp.sum(exponent, axis=1)
    weights = exponent.astype(jnp.bfloat16)
    summed = jnp.dot(weights, window_values, preferred_element_type=jnp.float32)
    result = summed / totals[:, None]
    result = jnp.where((query_marks >= 0)[:, None], result, 0.0)
    context = (
        result.reshape(head_local, token_count, HD)
        .transpose(1, 0, 2)
        .reshape(token_count, head_local * HD)
        .astype(jnp.bfloat16)
    )

    owner_count = gy_count
    page_rows = token_count // PAGE
    capacity = max(2, 2 * page_rows // owner_count)
    owner_of = page_owner[:, 0]
    one_hot = (owner_of[:, None] == jnp.arange(owner_count, dtype=jnp.int32)[None, :]).astype(
        jnp.int32
    )
    earlier = jnp.cumsum(one_hot, axis=0) - one_hot
    rank_in = jnp.sum(earlier * one_hot, axis=1)
    slot_of = owner_of * capacity + rank_in
    kv_pages = own_kv.reshape(2, page_rows, PAGE * quarter).transpose(1, 0, 2)
    send_kv = (
        jnp.zeros((owner_count * capacity, 2, PAGE * quarter), jnp.bfloat16)
        .at[slot_of]
        .set(kv_pages)
    )
    send_kv = send_kv.reshape(owner_count, capacity, 2, PAGE * quarter)
    got_kv = lax.all_to_all(send_kv, "gy", split_axis=0, concat_axis=0, tiled=True)
    got_kv = got_kv.reshape(owner_count * capacity, 2, PAGE, quarter)
    key_cache = got_kv[:, 0]
    value_cache = got_kv[:, 1]
    return (context, key_cache, value_cache)


def solution(mesh):
    placed = (
        P("gy", "gx"),
        P(),
        P("gy", "gx"),
        P("gy", "gx"),
        P("gy", "gx"),
        P("gy"),
        P("gy"),
        P("gy", None),
    )
    return jax.shard_map(
        shards,
        mesh=mesh,
        in_specs=placed,
        out_specs=(P("gy", "gx"), P("gy", None, "gx"), P("gy", None, "gx")),
        check_vma=False,
    )
```

```python
import jax
import jax.numpy as jnp
from jax import lax
from jax.sharding import PartitionSpec as P

D = 8192
HD = 128
PAGE = 16


EPSILON = 1e-05
THETA = 500000.0
MASKED = -1e30


def shifted(value, axis, by):
    count = lax.axis_size(axis)
    pairs = [(i, i + by) for i in range(count) if 0 <= i + by < count]
    return lax.ppermute(value, axis, pairs)


def partner_route(count, group, k):
    route = []
    for i in range(count):
        base = i - i % group
        route.append((i, base + ((i % group) ^ k)))
    return route


def rope(matrix, places, width, first_pair):
    cols = jnp.arange(matrix.shape[1], dtype=jnp.int32)
    pair_index = first_pair + (cols % width) // 2
    frequency = jnp.power(THETA, -(2.0 * pair_index.astype(jnp.float32)) / HD)
    angles = places.astype(jnp.float32)[:, None] * frequency[None, :]
    cosine = jnp.cos(angles)
    sine_of = jnp.sin(angles)
    following = jnp.roll(matrix, -1, axis=1)
    preceding = jnp.roll(matrix, 1, axis=1)
    even = (cols % 2 == 0)[None, :]
    return jnp.where(
        even, matrix * cosine - following * sine_of, matrix * cosine + preceding * sine_of
    )


def joined(mine, theirs, mine_first):
    return jnp.where(
        mine_first,
        jnp.concatenate([mine, theirs], axis=-1),
        jnp.concatenate([theirs, mine], axis=-1),
    )


def shards(
    tokens_in, norm_gain, query_weight, key_weight, value_weight, segment_ids, positions, page_owner
):
    token_count = tokens_in.shape[0]
    quarter = key_weight.shape[1]
    head_local = query_weight.shape[1] // HD
    quarters = HD // quarter
    gx_count = lax.axis_size("gx")
    gy_count = lax.axis_size("gy")
    spot = lax.axis_index("gx") % quarters
    my_gy = lax.axis_index("gy")
    row_block = query_weight.shape[0]

    local_weights = jnp.concatenate([query_weight, key_weight, value_weight], axis=1)
    pieces = [(my_gy, local_weights)]
    for k in range(1, gy_count):
        got = lax.ppermute(local_weights, "gy", partner_route(gy_count, gy_count, k))
        pieces.append((my_gy ^ k, got))

    local_float = tokens_in.astype(jnp.float32)
    my_gx = lax.axis_index("gx")
    feature_block = tokens_in.shape[1]
    local_gain = lax.dynamic_slice_in_dim(norm_gain, my_gx * feature_block, feature_block, 0)
    local_normed = (local_float * local_gain.astype(jnp.float32)[None, :]).astype(jnp.bfloat16)
    local_squares = jnp.sum(local_float * local_float, axis=1)
    square_parts = [local_squares]
    for k in range(1, gx_count):
        square_parts.append(lax.ppermute(local_squares, "gx", partner_route(gx_count, gx_count, k)))
    square_order = jnp.arange(gx_count, dtype=jnp.int32) ^ my_gx
    squares = jnp.sum(jnp.take(jnp.stack(square_parts), square_order, axis=0), axis=0)
    span_count = gy_count // 4
    marks = segment_ids + 1
    mark_list = [marks]
    for shift_by in range(1, span_count + 1):
        mark_list.insert(0, shifted(marks, "gy", shift_by))
    scaling = 1.0 / jnp.sqrt(squares / D + EPSILON)
    query_cols = head_local * HD
    halves = 2
    half_rows = token_count // halves
    query_halves, kv_halves, head_halves = [], [], []
    for h in range(halves):
        rows_of = slice(h * half_rows, (h + 1) * half_rows)
        normed = lax.all_gather(local_normed[rows_of], "gx", axis=1, tiled=True)
        if head_halves:
            normed, head_halves[-1] = lax.optimization_barrier((normed, head_halves[-1]))
        products = None
        for source, block in pieces:
            rows = lax.dynamic_slice_in_dim(normed, source * row_block, row_block, 1)
            part = jnp.dot(rows, block, preferred_element_type=jnp.float32)
            products = part if products is None else products + part
        projected = products * scaling[rows_of, None]
        places = positions[rows_of]
        key_piece = rope(
            projected[:, query_cols : query_cols + quarter], places, quarter, spot * (quarter // 2)
        ).astype(jnp.bfloat16)
        value_piece = projected[:, query_cols + quarter :].astype(jnp.bfloat16)
        query_halves.append(rope(projected[:, :query_cols], places, HD, 0).astype(jnp.bfloat16))
        own_kv = jnp.stack([key_piece, value_piece])
        kv_halves.append(own_kv)
        window_list = [own_kv]
        for shift_by in range(1, span_count + 1):
            window_list.insert(0, shifted(own_kv, "gy", shift_by))
        held = jnp.concatenate(window_list, axis=1)
        step = 1
        while step < quarters:
            theirs = lax.ppermute(held, "gx", partner_route(gx_count, quarters, step))
            held = joined(held, theirs, (spot // step) % 2 == 0)
            step *= 2
        head_halves.append(held.reshape(2, span_count + 1, half_rows, HD))
    queries = jnp.concatenate(query_halves, axis=0)
    own_kv = jnp.concatenate(kv_halves, axis=1)
    key_piece = own_kv[0]
    value_piece = own_kv[1]
    window_kv = jnp.stack(head_halves, axis=2).reshape(2, (span_count + 1) * token_count, HD)
    window_keys = window_kv[0]
    window_values = window_kv[1]
    window_marks = jnp.concatenate(mark_list, axis=0)
    reach_rows = span_count * token_count
    query_rows = (
        queries.reshape(token_count, head_local, HD)
        .transpose(1, 0, 2)
        .reshape(head_local * token_count, HD)
    )
    scores = lax.dot_general(
        query_rows, window_keys, (((1,), (1,)), ((), ())), preferred_element_type=jnp.float32
    ) * HD ** (-0.5)
    query_marks = jnp.tile(segment_ids, head_local)
    query_place = jnp.tile(jnp.arange(token_count, dtype=jnp.int32), head_local)
    key_place = jnp.arange(window_keys.shape[0], dtype=jnp.int32)
    allowed = (window_marks[None, :] == query_marks[:, None] + 1) & (window_marks[None, :] > 0)
    allowed = allowed & (key_place[None, :] <= query_place[:, None] + reach_rows)
    masked = jnp.where(allowed, scores, MASKED)
    highest = jnp.max(masked, axis=1, keepdims=True)
    exponent = jnp.exp(masked - highest)
    totals = jnp.sum(exponent, axis=1)
    weights = exponent.astype(jnp.bfloat16)
    summed = jnp.dot(weights, window_values, preferred_element_type=jnp.float32)
    result = summed / totals[:, None]
    result = jnp.where((query_marks >= 0)[:, None], result, 0.0)
    context = (
        result.reshape(head_local, token_count, HD)
        .transpose(1, 0, 2)
        .reshape(token_count, head_local * HD)
        .astype(jnp.bfloat16)
    )
    owner_count = gy_count
    page_rows = token_count // PAGE
    capacity = max(2, 2 * page_rows // owner_count)
    owner_of = page_owner[:, 0]
    one_hot = (owner_of[:, None] == jnp.arange(owner_count, dtype=jnp.int32)[None, :]).astype(
        jnp.int32
    )
    earlier = jnp.cumsum(one_hot, axis=0) - one_hot
    rank_in = jnp.sum(earlier * one_hot, axis=1)
    slot_of = owner_of * capacity + rank_in
    kv_pages = own_kv.reshape(2, page_rows, PAGE * quarter).transpose(1, 0, 2)
    send_kv = (
        jnp.zeros((owner_count * capacity, 2, PAGE * quarter), jnp.bfloat16)
        .at[slot_of]
        .set(kv_pages)
    )
    send_kv = send_kv.reshape(owner_count, capacity, 2, PAGE * quarter)
    got_kv = lax.all_to_all(send_kv, "gy", split_axis=0, concat_axis=0, tiled=True)
    got_kv = got_kv.reshape(owner_count * capacity, 2, PAGE, quarter)
    key_cache = got_kv[:, 0]
    value_cache = got_kv[:, 1]
    return (context, key_cache, value_cache)


def solution(mesh):
    placed = (
        P("gy", "gx"),
        P(),
        P("gy", "gx"),
        P("gy", "gx"),
        P("gy", "gx"),
        P("gy"),
        P("gy"),
        P("gy", None),
    )
    return jax.shard_map(
        shards,
        mesh=mesh,
        in_specs=placed,
        out_specs=(P("gy", "gx"), P("gy", None, "gx"), P("gy", None, "gx")),
        check_vma=False,
    )
```

```python
import jax
import jax.numpy as jnp
from jax import lax
from jax.sharding import PartitionSpec as P

D = 8192
HD = 128
PAGE = 16


EPSILON = 1e-05
THETA = 500000.0
MASKED = -1e30


def shifted(value, axis, by):
    count = lax.axis_size(axis)
    pairs = [(i, i + by) for i in range(count) if 0 <= i + by < count]
    return lax.ppermute(value, axis, pairs)


def partner_route(count, group, k):
    route = []
    for i in range(count):
        base = i - i % group
        route.append((i, base + ((i % group) ^ k)))
    return route


def rope(matrix, places, width, first_pair):
    cols = jnp.arange(matrix.shape[1], dtype=jnp.int32)
    pair_index = first_pair + (cols % width) // 2
    frequency = jnp.power(THETA, -(2.0 * pair_index.astype(jnp.float32)) / HD)
    angles = places.astype(jnp.float32)[:, None] * frequency[None, :]
    cosine = jnp.cos(angles)
    sine_of = jnp.sin(angles)
    following = jnp.roll(matrix, -1, axis=1)
    preceding = jnp.roll(matrix, 1, axis=1)
    even = (cols % 2 == 0)[None, :]
    return jnp.where(
        even, matrix * cosine - following * sine_of, matrix * cosine + preceding * sine_of
    )


def joined(mine, theirs, mine_first):
    return jnp.where(
        mine_first,
        jnp.concatenate([mine, theirs], axis=-1),
        jnp.concatenate([theirs, mine], axis=-1),
    )


def shards(
    tokens_in, norm_gain, query_weight, key_weight, value_weight, segment_ids, positions, page_owner
):
    token_count = tokens_in.shape[0]
    quarter = key_weight.shape[1]
    head_local = query_weight.shape[1] // HD
    quarters = HD // quarter
    gx_count = lax.axis_size("gx")
    gy_count = lax.axis_size("gy")
    spot = lax.axis_index("gx") % quarters
    my_gy = lax.axis_index("gy")
    row_block = query_weight.shape[0]

    kv_weights = jnp.stack([key_weight, value_weight])
    sibling = lax.ppermute(kv_weights, "gx", partner_route(gx_count, quarters, 1))
    half_weights = joined(kv_weights, sibling, spot % 2 == 0)
    local_weights = jnp.concatenate([query_weight, half_weights[0], half_weights[1]], axis=1)
    half_cols = 2 * quarter
    pieces = [(my_gy, local_weights)]
    for k in range(1, gy_count):
        got = lax.ppermute(local_weights, "gy", partner_route(gy_count, gy_count, k))
        pieces.append((my_gy ^ k, got))

    local_float = tokens_in.astype(jnp.float32)
    my_gx = lax.axis_index("gx")
    feature_block = tokens_in.shape[1]
    local_gain = lax.dynamic_slice_in_dim(norm_gain, my_gx * feature_block, feature_block, 0)
    local_normed = (local_float * local_gain.astype(jnp.float32)[None, :]).astype(jnp.bfloat16)
    local_squares = jnp.sum(local_float * local_float, axis=1)
    square_parts = [local_squares]
    for k in range(1, gx_count):
        square_parts.append(lax.ppermute(local_squares, "gx", partner_route(gx_count, gx_count, k)))
    square_order = jnp.arange(gx_count, dtype=jnp.int32) ^ my_gx
    squares = jnp.sum(jnp.take(jnp.stack(square_parts), square_order, axis=0), axis=0)
    span_count = gy_count // 4
    marks = segment_ids + 1
    mark_list = [marks]
    for shift_by in range(1, span_count + 1):
        mark_list.insert(0, shifted(marks, "gy", shift_by))
    scaling = 1.0 / jnp.sqrt(squares / D + EPSILON)
    query_cols = head_local * HD
    halves = 2
    half_rows = token_count // halves
    query_halves, kv_halves, head_halves = [], [], []
    for h in range(halves):
        rows_of = slice(h * half_rows, (h + 1) * half_rows)
        normed = lax.all_gather(local_normed[rows_of], "gx", axis=1, tiled=True)
        if head_halves:
            normed, head_halves[-1] = lax.optimization_barrier((normed, head_halves[-1]))
        products = None
        for source, block in pieces:
            rows = lax.dynamic_slice_in_dim(normed, source * row_block, row_block, 1)
            part = jnp.dot(rows, block, preferred_element_type=jnp.float32)
            products = part if products is None else products + part
        projected = products * scaling[rows_of, None]
        places = positions[rows_of]
        key_half = rope(
            projected[:, query_cols : query_cols + half_cols],
            places,
            half_cols,
            (spot // 2) * quarter,
        ).astype(jnp.bfloat16)
        value_half = projected[:, query_cols + half_cols :].astype(jnp.bfloat16)
        query_halves.append(rope(projected[:, :query_cols], places, HD, 0).astype(jnp.bfloat16))
        half_kv = jnp.stack([key_half, value_half])
        kv_halves.append(lax.dynamic_slice_in_dim(half_kv, (spot % 2) * quarter, quarter, 2))
        low_half = (spot // 2) % 2 == 0
        window_list = [
            joined(half_kv, lax.ppermute(half_kv, "gx", partner_route(gx_count, quarters, 2)), low_half)
        ]
        for shift_by in range(1, span_count + 1):
            route = []
            for i in range(gx_count):
                peer = i - i % quarters + ((i % quarters) ^ 2)
                for j in range(gy_count - shift_by):
                    route.append((i * gy_count + j, peer * gy_count + j + shift_by))
            same = shifted(half_kv, "gy", shift_by)
            other = lax.ppermute(half_kv, ("gx", "gy"), route)
            window_list.insert(0, joined(same, other, low_half))
        held = jnp.concatenate(window_list, axis=1)
        head_halves.append(held.reshape(2, span_count + 1, half_rows, HD))
    queries = jnp.concatenate(query_halves, axis=0)
    own_kv = jnp.concatenate(kv_halves, axis=1)
    key_piece = own_kv[0]
    value_piece = own_kv[1]
    window_kv = jnp.stack(head_halves, axis=2).reshape(2, (span_count + 1) * token_count, HD)
    window_keys = window_kv[0]
    window_values = window_kv[1]
    window_marks = jnp.concatenate(mark_list, axis=0)
    reach_rows = span_count * token_count
    query_rows = (
        queries.reshape(token_count, head_local, HD)
        .transpose(1, 0, 2)
        .reshape(head_local * token_count, HD)
    )
    scores = lax.dot_general(
        query_rows, window_keys, (((1,), (1,)), ((), ())), preferred_element_type=jnp.float32
    ) * HD ** (-0.5)
    query_marks = jnp.tile(segment_ids, head_local)
    query_place = jnp.tile(jnp.arange(token_count, dtype=jnp.int32), head_local)
    key_place = jnp.arange(window_keys.shape[0], dtype=jnp.int32)
    allowed = (window_marks[None, :] == query_marks[:, None] + 1) & (window_marks[None, :] > 0)
    allowed = allowed & (key_place[None, :] <= query_place[:, None] + reach_rows)
    masked = jnp.where(allowed, scores, MASKED)
    highest = jnp.max(masked, axis=1, keepdims=True)
    exponent = jnp.exp(masked - highest)
    totals = jnp.sum(exponent, axis=1)
    weights = exponent.astype(jnp.bfloat16)
    summed = jnp.dot(weights, window_values, preferred_element_type=jnp.float32)
    result = summed / totals[:, None]
    result = jnp.where((query_marks >= 0)[:, None], result, 0.0)
    context = (
        result.reshape(head_local, token_count, HD)
        .transpose(1, 0, 2)
        .reshape(token_count, head_local * HD)
        .astype(jnp.bfloat16)
    )
    owner_count = gy_count
    page_rows = token_count // PAGE
    capacity = max(2, 2 * page_rows // owner_count)
    owner_of = page_owner[:, 0]
    one_hot = (owner_of[:, None] == jnp.arange(owner_count, dtype=jnp.int32)[None, :]).astype(
        jnp.int32
    )
    earlier = jnp.cumsum(one_hot, axis=0) - one_hot
    rank_in = jnp.sum(earlier * one_hot, axis=1)
    slot_of = owner_of * capacity + rank_in
    kv_pages = own_kv.reshape(2, page_rows, PAGE * quarter).transpose(1, 0, 2)
    send_kv = (
        jnp.zeros((owner_count * capacity, 2, PAGE * quarter), jnp.bfloat16)
        .at[slot_of]
        .set(kv_pages)
    )
    send_kv = send_kv.reshape(owner_count, capacity, 2, PAGE * quarter)
    got_kv = lax.all_to_all(send_kv, "gy", split_axis=0, concat_axis=0, tiled=True)
    got_kv = got_kv.reshape(owner_count * capacity, 2, PAGE, quarter)
    key_cache = got_kv[:, 0]
    value_cache = got_kv[:, 1]
    return (context, key_cache, value_cache)


def solution(mesh):
    placed = (
        P("gy", "gx"),
        P(),
        P("gy", "gx"),
        P("gy", "gx"),
        P("gy", "gx"),
        P("gy"),
        P("gy"),
        P("gy", None),
    )
    return jax.shard_map(
        shards,
        mesh=mesh,
        in_specs=placed,
        out_specs=(P("gy", "gx"), P("gy", None, "gx"), P("gy", None, "gx")),
        check_vma=False,
    )
```

```python
import jax
import jax.numpy as jnp
from jax import lax
from jax.sharding import PartitionSpec as P

D = 8192
HD = 128
PAGE = 16


EPSILON = 1e-05
THETA = 500000.0
MASKED = -1e30


def shifted(value, axis, by):
    count = lax.axis_size(axis)
    pairs = [(i, i + by) for i in range(count) if 0 <= i + by < count]
    return lax.ppermute(value, axis, pairs)


def partner_route(count, group, k):
    route = []
    for i in range(count):
        base = i - i % group
        route.append((i, base + ((i % group) ^ k)))
    return route


def rope(matrix, places, width, first_pair):
    cols = jnp.arange(matrix.shape[1], dtype=jnp.int32)
    pair_index = first_pair + (cols % width) // 2
    frequency = jnp.power(THETA, -(2.0 * pair_index.astype(jnp.float32)) / HD)
    angles = places.astype(jnp.float32)[:, None] * frequency[None, :]
    cosine = jnp.cos(angles)
    sine_of = jnp.sin(angles)
    following = jnp.roll(matrix, -1, axis=1)
    preceding = jnp.roll(matrix, 1, axis=1)
    even = (cols % 2 == 0)[None, :]
    return jnp.where(
        even, matrix * cosine - following * sine_of, matrix * cosine + preceding * sine_of
    )


def joined(mine, theirs, mine_first):
    return jnp.where(
        mine_first,
        jnp.concatenate([mine, theirs], axis=-1),
        jnp.concatenate([theirs, mine], axis=-1),
    )


def shards(
    tokens_in, norm_gain, query_weight, key_weight, value_weight, segment_ids, positions, page_owner
):
    token_count = tokens_in.shape[0]
    quarter = key_weight.shape[1]
    head_local = query_weight.shape[1] // HD
    quarters = HD // quarter
    gx_count = lax.axis_size("gx")
    gy_count = lax.axis_size("gy")
    spot = lax.axis_index("gx") % quarters
    my_gy = lax.axis_index("gy")
    row_block = query_weight.shape[0]

    local_weights = jnp.concatenate([query_weight, key_weight, value_weight], axis=1)
    pieces = [(my_gy, local_weights)]
    for k in range(1, gy_count):
        got = lax.ppermute(local_weights, "gy", partner_route(gy_count, gy_count, k))
        pieces.append((my_gy ^ k, got))

    local_float = tokens_in.astype(jnp.float32)
    my_gx = lax.axis_index("gx")
    feature_block = tokens_in.shape[1]
    local_gain = lax.dynamic_slice_in_dim(norm_gain, my_gx * feature_block, feature_block, 0)
    local_normed = (local_float * local_gain.astype(jnp.float32)[None, :]).astype(jnp.bfloat16)
    local_squares = jnp.sum(local_float * local_float, axis=1)
    square_parts = [local_squares]
    for k in range(1, gx_count):
        square_parts.append(lax.ppermute(local_squares, "gx", partner_route(gx_count, gx_count, k)))
    square_order = jnp.arange(gx_count, dtype=jnp.int32) ^ my_gx
    squares = jnp.sum(jnp.take(jnp.stack(square_parts), square_order, axis=0), axis=0)
    span_count = gy_count // 4
    marks = segment_ids + 1
    mark_list = [marks]
    for shift_by in range(1, span_count + 1):
        mark_list.insert(0, shifted(marks, "gy", shift_by))
    scaling = 1.0 / jnp.sqrt(squares / D + EPSILON)
    query_cols = head_local * HD
    first_rows = token_count * 3 // 4
    cuts = [(0, first_rows), (first_rows, token_count)]
    query_halves, kv_halves, head_halves = [], [], []
    for begin, finish in cuts:
        rows_of = slice(begin, finish)
        half_rows = finish - begin
        normed = lax.all_gather(local_normed[rows_of], "gx", axis=1, tiled=True)
        if head_halves:
            normed, head_halves[-1] = lax.optimization_barrier((normed, head_halves[-1]))
        products = None
        for source, block in pieces:
            rows = lax.dynamic_slice_in_dim(normed, source * row_block, row_block, 1)
            part = jnp.dot(rows, block, preferred_element_type=jnp.float32)
            products = part if products is None else products + part
        projected = products * scaling[rows_of, None]
        places = positions[rows_of]
        key_piece = rope(
            projected[:, query_cols : query_cols + quarter], places, quarter, spot * (quarter // 2)
        ).astype(jnp.bfloat16)
        value_piece = projected[:, query_cols + quarter :].astype(jnp.bfloat16)
        query_halves.append(rope(projected[:, :query_cols], places, HD, 0).astype(jnp.bfloat16))
        own_kv = jnp.stack([key_piece, value_piece])
        kv_halves.append(own_kv)
        window_list = [own_kv]
        for shift_by in range(1, span_count + 1):
            window_list.insert(0, shifted(own_kv, "gy", shift_by))
        held = jnp.concatenate(window_list, axis=1)
        step = 1
        while step < quarters:
            theirs = lax.ppermute(held, "gx", partner_route(gx_count, quarters, step))
            held = joined(held, theirs, (spot // step) % 2 == 0)
            step *= 2
        head_halves.append(held.reshape(2, span_count + 1, half_rows, HD))
    queries = jnp.concatenate(query_halves, axis=0)
    own_kv = jnp.concatenate(kv_halves, axis=1)
    key_piece = own_kv[0]
    value_piece = own_kv[1]
    window_kv = jnp.concatenate(head_halves, axis=2).reshape(2, (span_count + 1) * token_count, HD)
    window_keys = window_kv[0]
    window_values = window_kv[1]
    window_marks = jnp.concatenate(mark_list, axis=0)
    reach_rows = span_count * token_count
    query_rows = (
        queries.reshape(token_count, head_local, HD)
        .transpose(1, 0, 2)
        .reshape(head_local * token_count, HD)
    )
    scores = lax.dot_general(
        query_rows, window_keys, (((1,), (1,)), ((), ())), preferred_element_type=jnp.float32
    ) * HD ** (-0.5)
    query_marks = jnp.tile(segment_ids, head_local)
    query_place = jnp.tile(jnp.arange(token_count, dtype=jnp.int32), head_local)
    key_place = jnp.arange(window_keys.shape[0], dtype=jnp.int32)
    allowed = (window_marks[None, :] == query_marks[:, None] + 1) & (window_marks[None, :] > 0)
    allowed = allowed & (key_place[None, :] <= query_place[:, None] + reach_rows)
    masked = jnp.where(allowed, scores, MASKED)
    highest = jnp.max(masked, axis=1, keepdims=True)
    exponent = jnp.exp(masked - highest)
    totals = jnp.sum(exponent, axis=1)
    weights = exponent.astype(jnp.bfloat16)
    summed = jnp.dot(weights, window_values, preferred_element_type=jnp.float32)
    result = summed / totals[:, None]
    result = jnp.where((query_marks >= 0)[:, None], result, 0.0)
    context = (
        result.reshape(head_local, token_count, HD)
        .transpose(1, 0, 2)
        .reshape(token_count, head_local * HD)
        .astype(jnp.bfloat16)
    )
    owner_count = gy_count
    page_rows = token_count // PAGE
    capacity = max(2, 2 * page_rows // owner_count)
    owner_of = page_owner[:, 0]
    one_hot = (owner_of[:, None] == jnp.arange(owner_count, dtype=jnp.int32)[None, :]).astype(
        jnp.int32
    )
    earlier = jnp.cumsum(one_hot, axis=0) - one_hot
    rank_in = jnp.sum(earlier * one_hot, axis=1)
    slot_of = owner_of * capacity + rank_in
    kv_pages = own_kv.reshape(2, page_rows, PAGE * quarter).transpose(1, 0, 2)
    send_kv = (
        jnp.zeros((owner_count * capacity, 2, PAGE * quarter), jnp.bfloat16)
        .at[slot_of]
        .set(kv_pages)
    )
    send_kv = send_kv.reshape(owner_count, capacity, 2, PAGE * quarter)
    got_kv = lax.all_to_all(send_kv, "gy", split_axis=0, concat_axis=0, tiled=True)
    got_kv = got_kv.reshape(owner_count * capacity, 2, PAGE, quarter)
    key_cache = got_kv[:, 0]
    value_cache = got_kv[:, 1]
    return (context, key_cache, value_cache)


def solution(mesh):
    placed = (
        P("gy", "gx"),
        P(),
        P("gy", "gx"),
        P("gy", "gx"),
        P("gy", "gx"),
        P("gy"),
        P("gy"),
        P("gy", None),
    )
    return jax.shard_map(
        shards,
        mesh=mesh,
        in_specs=placed,
        out_specs=(P("gy", "gx"), P("gy", None, "gx"), P("gy", None, "gx")),
        check_vma=False,
    )
```

```python
import jax
import jax.numpy as jnp
from jax import lax
from jax.sharding import PartitionSpec as P

D = 8192
HD = 128
PAGE = 16


EPSILON = 1e-05
THETA = 500000.0
MASKED = -1e30


def shifted(value, axis, by):
    count = lax.axis_size(axis)
    pairs = [(i, i + by) for i in range(count) if 0 <= i + by < count]
    return lax.ppermute(value, axis, pairs)


def partner_route(count, group, k):
    route = []
    for i in range(count):
        base = i - i % group
        route.append((i, base + ((i % group) ^ k)))
    return route


def rope(matrix, places, width, first_pair):
    cols = jnp.arange(matrix.shape[1], dtype=jnp.int32)
    pair_index = first_pair + (cols % width) // 2
    frequency = jnp.power(THETA, -(2.0 * pair_index.astype(jnp.float32)) / HD)
    angles = places.astype(jnp.float32)[:, None] * frequency[None, :]
    cosine = jnp.cos(angles)
    sine_of = jnp.sin(angles)
    following = jnp.roll(matrix, -1, axis=1)
    preceding = jnp.roll(matrix, 1, axis=1)
    even = (cols % 2 == 0)[None, :]
    return jnp.where(
        even, matrix * cosine - following * sine_of, matrix * cosine + preceding * sine_of
    )


def joined(mine, theirs, mine_first):
    return jnp.where(
        mine_first,
        jnp.concatenate([mine, theirs], axis=-1),
        jnp.concatenate([theirs, mine], axis=-1),
    )


def shards(
    tokens_in, norm_gain, query_weight, key_weight, value_weight, segment_ids, positions, page_owner
):
    token_count = tokens_in.shape[0]
    quarter = key_weight.shape[1]
    head_local = query_weight.shape[1] // HD
    quarters = HD // quarter
    gx_count = lax.axis_size("gx")
    gy_count = lax.axis_size("gy")
    spot = lax.axis_index("gx") % quarters
    my_gy = lax.axis_index("gy")
    row_block = query_weight.shape[0]

    kv_weights = jnp.stack([key_weight, value_weight])
    sibling = lax.ppermute(kv_weights, "gx", partner_route(gx_count, quarters, 1))
    half_weights = joined(kv_weights, sibling, spot % 2 == 0)
    local_weights = jnp.concatenate([query_weight, half_weights[0], half_weights[1]], axis=1)
    half_cols = 2 * quarter
    pieces = [(my_gy, local_weights)]
    for k in range(1, gy_count):
        got = lax.ppermute(local_weights, "gy", partner_route(gy_count, gy_count, k))
        pieces.append((my_gy ^ k, got))

    local_float = tokens_in.astype(jnp.float32)
    my_gx = lax.axis_index("gx")
    feature_block = tokens_in.shape[1]
    local_gain = lax.dynamic_slice_in_dim(norm_gain, my_gx * feature_block, feature_block, 0)
    local_normed = (local_float * local_gain.astype(jnp.float32)[None, :]).astype(jnp.bfloat16)
    local_squares = jnp.sum(local_float * local_float, axis=1)
    square_parts = [local_squares]
    for k in range(1, gx_count):
        square_parts.append(lax.ppermute(local_squares, "gx", partner_route(gx_count, gx_count, k)))
    square_order = jnp.arange(gx_count, dtype=jnp.int32) ^ my_gx
    squares = jnp.sum(jnp.take(jnp.stack(square_parts), square_order, axis=0), axis=0)
    span_count = gy_count // 4
    marks = segment_ids + 1
    mark_list = [marks]
    for shift_by in range(1, span_count + 1):
        mark_list.insert(0, shifted(marks, "gy", shift_by))
    scaling = 1.0 / jnp.sqrt(squares / D + EPSILON)
    query_cols = head_local * HD
    halves = 1
    half_rows = token_count // halves
    query_halves, kv_halves, head_halves = [], [], []
    for h in range(halves):
        rows_of = slice(h * half_rows, (h + 1) * half_rows)
        normed = lax.all_gather(local_normed[rows_of], "gx", axis=1, tiled=True)
        if head_halves:
            normed, head_halves[-1] = lax.optimization_barrier((normed, head_halves[-1]))
        products = None
        for source, block in pieces:
            rows = lax.dynamic_slice_in_dim(normed, source * row_block, row_block, 1)
            part = jnp.dot(rows, block, preferred_element_type=jnp.float32)
            products = part if products is None else products + part
        projected = products * scaling[rows_of, None]
        places = positions[rows_of]
        key_half = rope(
            projected[:, query_cols : query_cols + half_cols],
            places,
            half_cols,
            (spot // 2) * quarter,
        ).astype(jnp.bfloat16)
        value_half = projected[:, query_cols + half_cols :].astype(jnp.bfloat16)
        query_halves.append(rope(projected[:, :query_cols], places, HD, 0).astype(jnp.bfloat16))
        half_kv = jnp.stack([key_half, value_half])
        kv_halves.append(lax.dynamic_slice_in_dim(half_kv, (spot % 2) * quarter, quarter, 2))
        low_half = (spot // 2) % 2 == 0
        window_list = [
            joined(half_kv, lax.ppermute(half_kv, "gx", partner_route(gx_count, quarters, 2)), low_half)
        ]
        for shift_by in range(1, span_count + 1):
            route = []
            for i in range(gx_count):
                peer = i - i % quarters + ((i % quarters) ^ 2)
                for j in range(gy_count - shift_by):
                    route.append((i * gy_count + j, peer * gy_count + j + shift_by))
            same = shifted(half_kv, "gy", shift_by)
            other = lax.ppermute(half_kv, ("gx", "gy"), route)
            window_list.insert(0, joined(same, other, low_half))
        held = jnp.concatenate(window_list, axis=1)
        head_halves.append(held.reshape(2, span_count + 1, half_rows, HD))
    queries = jnp.concatenate(query_halves, axis=0)
    own_kv = jnp.concatenate(kv_halves, axis=1)
    key_piece = own_kv[0]
    value_piece = own_kv[1]
    window_kv = jnp.stack(head_halves, axis=2).reshape(2, (span_count + 1) * token_count, HD)
    window_keys = window_kv[0]
    window_values = window_kv[1]
    window_marks = jnp.concatenate(mark_list, axis=0)
    reach_rows = span_count * token_count
    query_rows = (
        queries.reshape(token_count, head_local, HD)
        .transpose(1, 0, 2)
        .reshape(head_local * token_count, HD)
    )
    scores = lax.dot_general(
        query_rows, window_keys, (((1,), (1,)), ((), ())), preferred_element_type=jnp.float32
    ) * HD ** (-0.5)
    query_marks = jnp.tile(segment_ids, head_local)
    query_place = jnp.tile(jnp.arange(token_count, dtype=jnp.int32), head_local)
    key_place = jnp.arange(window_keys.shape[0], dtype=jnp.int32)
    allowed = (window_marks[None, :] == query_marks[:, None] + 1) & (window_marks[None, :] > 0)
    allowed = allowed & (key_place[None, :] <= query_place[:, None] + reach_rows)
    masked = jnp.where(allowed, scores, MASKED)
    highest = jnp.max(masked, axis=1, keepdims=True)
    exponent = jnp.exp(masked - highest)
    totals = jnp.sum(exponent, axis=1)
    weights = exponent.astype(jnp.bfloat16)
    summed = jnp.dot(weights, window_values, preferred_element_type=jnp.float32)
    result = summed / totals[:, None]
    result = jnp.where((query_marks >= 0)[:, None], result, 0.0)
    context = (
        result.reshape(head_local, token_count, HD)
        .transpose(1, 0, 2)
        .reshape(token_count, head_local * HD)
        .astype(jnp.bfloat16)
    )
    owner_count = gy_count
    page_rows = token_count // PAGE
    capacity = max(2, 2 * page_rows // owner_count)
    owner_of = page_owner[:, 0]
    one_hot = (owner_of[:, None] == jnp.arange(owner_count, dtype=jnp.int32)[None, :]).astype(
        jnp.int32
    )
    earlier = jnp.cumsum(one_hot, axis=0) - one_hot
    rank_in = jnp.sum(earlier * one_hot, axis=1)
    slot_of = owner_of * capacity + rank_in
    kv_pages = own_kv.reshape(2, page_rows, PAGE * quarter).transpose(1, 0, 2)
    send_kv = (
        jnp.zeros((owner_count * capacity, 2, PAGE * quarter), jnp.bfloat16)
        .at[slot_of]
        .set(kv_pages)
    )
    send_kv = send_kv.reshape(owner_count, capacity, 2, PAGE * quarter)
    got_kv = lax.all_to_all(send_kv, "gy", split_axis=0, concat_axis=0, tiled=True)
    got_kv = got_kv.reshape(owner_count * capacity, 2, PAGE, quarter)
    key_cache = got_kv[:, 0]
    value_cache = got_kv[:, 1]
    return (context, key_cache, value_cache)


def solution(mesh):
    placed = (
        P("gy", "gx"),
        P(),
        P("gy", "gx"),
        P("gy", "gx"),
        P("gy", "gx"),
        P("gy"),
        P("gy"),
        P("gy", None),
    )
    return jax.shard_map(
        shards,
        mesh=mesh,
        in_specs=placed,
        out_specs=(P("gy", "gx"), P("gy", None, "gx"), P("gy", None, "gx")),
        check_vma=False,
    )
```

```python
import jax
import jax.numpy as jnp
from jax import lax
from jax.sharding import PartitionSpec as P

D = 8192
HD = 128
PAGE = 16


EPSILON = 1e-05
THETA = 500000.0
MASKED = -1e30


def shifted(value, axis, by):
    count = lax.axis_size(axis)
    pairs = [(i, i + by) for i in range(count) if 0 <= i + by < count]
    return lax.ppermute(value, axis, pairs)


def partner_route(count, group, k):
    route = []
    for i in range(count):
        base = i - i % group
        route.append((i, base + ((i % group) ^ k)))
    return route


def rope(matrix, places, width, first_pair):
    cols = jnp.arange(matrix.shape[1], dtype=jnp.int32)
    pair_index = first_pair + (cols % width) // 2
    frequency = jnp.power(THETA, -(2.0 * pair_index.astype(jnp.float32)) / HD)
    angles = places.astype(jnp.float32)[:, None] * frequency[None, :]
    cosine = jnp.cos(angles)
    sine_of = jnp.sin(angles)
    following = jnp.roll(matrix, -1, axis=1)
    preceding = jnp.roll(matrix, 1, axis=1)
    even = (cols % 2 == 0)[None, :]
    return jnp.where(
        even, matrix * cosine - following * sine_of, matrix * cosine + preceding * sine_of
    )


def joined(mine, theirs, mine_first):
    return jnp.where(
        mine_first,
        jnp.concatenate([mine, theirs], axis=-1),
        jnp.concatenate([theirs, mine], axis=-1),
    )


def shards(
    tokens_in, norm_gain, query_weight, key_weight, value_weight, segment_ids, positions, page_owner
):
    token_count = tokens_in.shape[0]
    quarter = key_weight.shape[1]
    head_local = query_weight.shape[1] // HD
    quarters = HD // quarter
    gx_count = lax.axis_size("gx")
    gy_count = lax.axis_size("gy")
    spot = lax.axis_index("gx") % quarters
    my_gy = lax.axis_index("gy")
    row_block = query_weight.shape[0]

    kv_weights = jnp.stack([key_weight, value_weight])
    sibling = lax.ppermute(kv_weights, "gx", partner_route(gx_count, quarters, 1))
    half_weights = joined(kv_weights, sibling, spot % 2 == 0)
    local_weights = jnp.concatenate([query_weight, half_weights[0], half_weights[1]], axis=1)
    half_cols = 2 * quarter
    pieces = [(my_gy, local_weights)]
    for k in range(1, gy_count):
        got = lax.ppermute(local_weights, "gy", partner_route(gy_count, gy_count, k))
        pieces.append((my_gy ^ k, got))

    local_float = tokens_in.astype(jnp.float32)
    my_gx = lax.axis_index("gx")
    feature_block = tokens_in.shape[1]
    local_gain = lax.dynamic_slice_in_dim(norm_gain, my_gx * feature_block, feature_block, 0)
    local_normed = (local_float * local_gain.astype(jnp.float32)[None, :]).astype(jnp.bfloat16)
    local_squares = jnp.sum(local_float * local_float, axis=1)
    square_parts = [local_squares]
    for k in range(1, gx_count):
        square_parts.append(lax.ppermute(local_squares, "gx", partner_route(gx_count, gx_count, k)))
    square_order = jnp.arange(gx_count, dtype=jnp.int32) ^ my_gx
    squares = jnp.sum(jnp.take(jnp.stack(square_parts), square_order, axis=0), axis=0)
    span_count = gy_count // 4
    marks = segment_ids + 1
    mark_list = [marks]
    for shift_by in range(1, span_count + 1):
        mark_list.insert(0, shifted(marks, "gy", shift_by))
    scaling = 1.0 / jnp.sqrt(squares / D + EPSILON)
    query_cols = head_local * HD
    halves = 1
    half_rows = token_count // halves
    query_halves, kv_halves, head_halves = [], [], []
    for h in range(halves):
        rows_of = slice(h * half_rows, (h + 1) * half_rows)
        normed = lax.all_gather(local_normed[rows_of], "gx", axis=1, tiled=True)
        if head_halves:
            normed, head_halves[-1] = lax.optimization_barrier((normed, head_halves[-1]))
        query_cols = head_local * HD
        kv_products = None
        q_products = None
        for source, block in pieces:
            rows = lax.dynamic_slice_in_dim(normed, source * row_block, row_block, 1)
            kv_part = jnp.dot(rows, block[:, query_cols:], preferred_element_type=jnp.float32)
            kv_products = kv_part if kv_products is None else kv_products + kv_part
        places = positions[rows_of]
        kv_projected = kv_products * scaling[rows_of, None]
        key_half = rope(kv_projected[:, :half_cols], places, half_cols, (spot // 2) * quarter)
        key_half = key_half.astype(jnp.bfloat16)
        value_half = kv_projected[:, half_cols:].astype(jnp.bfloat16)
        half_kv = jnp.stack([key_half, value_half])
        normed, half_kv = lax.optimization_barrier((normed, half_kv))
        received = [lax.ppermute(half_kv, "gx", partner_route(gx_count, quarters, 2))]
        for shift_by in range(1, span_count + 1):
            route = []
            for i in range(gx_count):
                peer = i - i % quarters + ((i % quarters) ^ 2)
                for j in range(gy_count - shift_by):
                    route.append((i * gy_count + j, peer * gy_count + j + shift_by))
            received.append(shifted(half_kv, "gy", shift_by))
            received.append(lax.ppermute(half_kv, ("gx", "gy"), route))
        for source, block in pieces:
            rows = lax.dynamic_slice_in_dim(normed, source * row_block, row_block, 1)
            q_part = jnp.dot(rows, block[:, :query_cols], preferred_element_type=jnp.float32)
            q_products = q_part if q_products is None else q_products + q_part
        received, q_products = lax.optimization_barrier((received, q_products))
        low_half = (spot // 2) % 2 == 0
        window_list = [joined(half_kv, received[0], low_half)]
        for shift_by in range(1, span_count + 1):
            same, other = received[2 * shift_by - 1], received[2 * shift_by]
            window_list.insert(0, joined(same, other, low_half))
        held = jnp.concatenate(window_list, axis=1)
        projected = q_products * scaling[rows_of, None]
        query_halves.append(rope(projected, places, HD, 0).astype(jnp.bfloat16))
        kv_halves.append(lax.dynamic_slice_in_dim(half_kv, (spot % 2) * quarter, quarter, 2))
        head_halves.append(held.reshape(2, span_count + 1, half_rows, HD))
    queries = jnp.concatenate(query_halves, axis=0)
    own_kv = jnp.concatenate(kv_halves, axis=1)
    key_piece = own_kv[0]
    value_piece = own_kv[1]
    window_kv = jnp.stack(head_halves, axis=2).reshape(2, (span_count + 1) * token_count, HD)
    window_keys = window_kv[0]
    window_values = window_kv[1]
    window_marks = jnp.concatenate(mark_list, axis=0)
    reach_rows = span_count * token_count
    query_rows = (
        queries.reshape(token_count, head_local, HD)
        .transpose(1, 0, 2)
        .reshape(head_local * token_count, HD)
    )
    scores = lax.dot_general(
        query_rows, window_keys, (((1,), (1,)), ((), ())), preferred_element_type=jnp.float32
    ) * HD ** (-0.5)
    query_marks = jnp.tile(segment_ids, head_local)
    query_place = jnp.tile(jnp.arange(token_count, dtype=jnp.int32), head_local)
    key_place = jnp.arange(window_keys.shape[0], dtype=jnp.int32)
    allowed = (window_marks[None, :] == query_marks[:, None] + 1) & (window_marks[None, :] > 0)
    allowed = allowed & (key_place[None, :] <= query_place[:, None] + reach_rows)
    masked = jnp.where(allowed, scores, MASKED)
    highest = jnp.max(masked, axis=1, keepdims=True)
    exponent = jnp.exp(masked - highest)
    totals = jnp.sum(exponent, axis=1)
    weights = exponent.astype(jnp.bfloat16)
    summed = jnp.dot(weights, window_values, preferred_element_type=jnp.float32)
    result = summed / totals[:, None]
    result = jnp.where((query_marks >= 0)[:, None], result, 0.0)
    context = (
        result.reshape(head_local, token_count, HD)
        .transpose(1, 0, 2)
        .reshape(token_count, head_local * HD)
        .astype(jnp.bfloat16)
    )
    owner_count = gy_count
    page_rows = token_count // PAGE
    capacity = max(2, 2 * page_rows // owner_count)
    owner_of = page_owner[:, 0]
    one_hot = (owner_of[:, None] == jnp.arange(owner_count, dtype=jnp.int32)[None, :]).astype(
        jnp.int32
    )
    earlier = jnp.cumsum(one_hot, axis=0) - one_hot
    rank_in = jnp.sum(earlier * one_hot, axis=1)
    slot_of = owner_of * capacity + rank_in
    kv_pages = own_kv.reshape(2, page_rows, PAGE * quarter).transpose(1, 0, 2)
    send_kv = (
        jnp.zeros((owner_count * capacity, 2, PAGE * quarter), jnp.bfloat16)
        .at[slot_of]
        .set(kv_pages)
    )
    send_kv = send_kv.reshape(owner_count, capacity, 2, PAGE * quarter)
    got_kv = lax.all_to_all(send_kv, "gy", split_axis=0, concat_axis=0, tiled=True)
    got_kv = got_kv.reshape(owner_count * capacity, 2, PAGE, quarter)
    key_cache = got_kv[:, 0]
    value_cache = got_kv[:, 1]
    return (context, key_cache, value_cache)


def solution(mesh):
    placed = (
        P("gy", "gx"),
        P(),
        P("gy", "gx"),
        P("gy", "gx"),
        P("gy", "gx"),
        P("gy"),
        P("gy"),
        P("gy", None),
    )
    return jax.shard_map(
        shards,
        mesh=mesh,
        in_specs=placed,
        out_specs=(P("gy", "gx"), P("gy", None, "gx"), P("gy", None, "gx")),
        check_vma=False,
    )
```

```python
import jax
import jax.numpy as jnp
from jax import lax
from jax.sharding import PartitionSpec as P

D = 8192
HD = 128
PAGE = 16


EPSILON = 1e-05
THETA = 500000.0
MASKED = -1e30


def shifted(value, axis, by):
    count = lax.axis_size(axis)
    pairs = [(i, i + by) for i in range(count) if 0 <= i + by < count]
    return lax.ppermute(value, axis, pairs)


def partner_route(count, group, k):
    route = []
    for i in range(count):
        base = i - i % group
        route.append((i, base + ((i % group) ^ k)))
    return route


def rope(matrix, places, width, first_pair):
    cols = jnp.arange(matrix.shape[1], dtype=jnp.int32)
    pair_index = first_pair + (cols % width) // 2
    frequency = jnp.power(THETA, -(2.0 * pair_index.astype(jnp.float32)) / HD)
    angles = places.astype(jnp.float32)[:, None] * frequency[None, :]
    cosine = jnp.cos(angles)
    sine_of = jnp.sin(angles)
    following = jnp.roll(matrix, -1, axis=1)
    preceding = jnp.roll(matrix, 1, axis=1)
    even = (cols % 2 == 0)[None, :]
    return jnp.where(
        even, matrix * cosine - following * sine_of, matrix * cosine + preceding * sine_of
    )


def joined(mine, theirs, mine_first):
    return jnp.where(
        mine_first,
        jnp.concatenate([mine, theirs], axis=-1),
        jnp.concatenate([theirs, mine], axis=-1),
    )


def shards(
    tokens_in, norm_gain, query_weight, key_weight, value_weight, segment_ids, positions, page_owner
):
    token_count = tokens_in.shape[0]
    quarter = key_weight.shape[1]
    head_local = query_weight.shape[1] // HD
    quarters = HD // quarter
    gx_count = lax.axis_size("gx")
    gy_count = lax.axis_size("gy")
    spot = lax.axis_index("gx") % quarters
    my_gy = lax.axis_index("gy")
    row_block = query_weight.shape[0]

    kv_weights = jnp.stack([key_weight, value_weight])
    sibling = lax.ppermute(kv_weights, "gx", partner_route(gx_count, quarters, 1))
    half_weights = joined(kv_weights, sibling, spot % 2 == 0)
    local_weights = jnp.concatenate([query_weight, half_weights[0], half_weights[1]], axis=1)
    half_cols = 2 * quarter
    pieces = [(my_gy, local_weights)]
    for k in range(1, gy_count):
        got = lax.ppermute(local_weights, "gy", partner_route(gy_count, gy_count, k))
        pieces.append((my_gy ^ k, got))

    local_float = tokens_in.astype(jnp.float32)
    my_gx = lax.axis_index("gx")
    feature_block = tokens_in.shape[1]
    local_gain = lax.dynamic_slice_in_dim(norm_gain, my_gx * feature_block, feature_block, 0)
    local_normed = (local_float * local_gain.astype(jnp.float32)[None, :]).astype(jnp.bfloat16)
    local_squares = jnp.sum(local_float * local_float, axis=1)
    square_parts = [local_squares]
    for k in range(1, gx_count):
        square_parts.append(lax.ppermute(local_squares, "gx", partner_route(gx_count, gx_count, k)))
    square_order = jnp.arange(gx_count, dtype=jnp.int32) ^ my_gx
    squares = jnp.sum(jnp.take(jnp.stack(square_parts), square_order, axis=0), axis=0)
    span_count = gy_count // 4
    marks = segment_ids + 1
    mark_list = [marks]
    for shift_by in range(1, span_count + 1):
        mark_list.insert(0, shifted(marks, "gy", shift_by))
    scaling = 1.0 / jnp.sqrt(squares / D + EPSILON)
    query_cols = head_local * HD
    halves = 1
    half_rows = token_count // halves
    query_halves, kv_halves, head_halves = [], [], []
    for h in range(halves):
        rows_of = slice(h * half_rows, (h + 1) * half_rows)
        normed = lax.all_gather(local_normed[rows_of], "gx", axis=0, tiled=False)
        per_piece = row_block // feature_block
        normed = normed.reshape(gx_count // per_piece, per_piece, half_rows, feature_block)
        if head_halves:
            normed, head_halves[-1] = lax.optimization_barrier((normed, head_halves[-1]))
        products = None
        for source, block in pieces:
            rows = lax.dynamic_index_in_dim(normed, source, 0, keepdims=False)
            weights_of = block.reshape(per_piece, feature_block, block.shape[1])
            part = jnp.einsum("btd,bdc->tc", rows, weights_of, preferred_element_type=jnp.float32)
            products = part if products is None else products + part
        projected = products * scaling[rows_of, None]
        places = positions[rows_of]
        key_half = rope(
            projected[:, query_cols : query_cols + half_cols],
            places,
            half_cols,
            (spot // 2) * quarter,
        ).astype(jnp.bfloat16)
        value_half = projected[:, query_cols + half_cols :].astype(jnp.bfloat16)
        query_halves.append(rope(projected[:, :query_cols], places, HD, 0).astype(jnp.bfloat16))
        half_kv = jnp.stack([key_half, value_half])
        kv_halves.append(lax.dynamic_slice_in_dim(half_kv, (spot % 2) * quarter, quarter, 2))
        low_half = (spot // 2) % 2 == 0
        window_list = [
            joined(half_kv, lax.ppermute(half_kv, "gx", partner_route(gx_count, quarters, 2)), low_half)
        ]
        for shift_by in range(1, span_count + 1):
            route = []
            for i in range(gx_count):
                peer = i - i % quarters + ((i % quarters) ^ 2)
                for j in range(gy_count - shift_by):
                    route.append((i * gy_count + j, peer * gy_count + j + shift_by))
            same = shifted(half_kv, "gy", shift_by)
            other = lax.ppermute(half_kv, ("gx", "gy"), route)
            window_list.insert(0, joined(same, other, low_half))
        held = jnp.concatenate(window_list, axis=1)
        head_halves.append(held.reshape(2, span_count + 1, half_rows, HD))
    queries = jnp.concatenate(query_halves, axis=0)
    own_kv = jnp.concatenate(kv_halves, axis=1)
    key_piece = own_kv[0]
    value_piece = own_kv[1]
    window_kv = jnp.stack(head_halves, axis=2).reshape(2, (span_count + 1) * token_count, HD)
    window_keys = window_kv[0]
    window_values = window_kv[1]
    window_marks = jnp.concatenate(mark_list, axis=0)
    reach_rows = span_count * token_count
    query_rows = (
        queries.reshape(token_count, head_local, HD)
        .transpose(1, 0, 2)
        .reshape(head_local * token_count, HD)
    )
    scores = lax.dot_general(
        query_rows, window_keys, (((1,), (1,)), ((), ())), preferred_element_type=jnp.float32
    ) * HD ** (-0.5)
    query_marks = jnp.tile(segment_ids, head_local)
    query_place = jnp.tile(jnp.arange(token_count, dtype=jnp.int32), head_local)
    key_place = jnp.arange(window_keys.shape[0], dtype=jnp.int32)
    allowed = (window_marks[None, :] == query_marks[:, None] + 1) & (window_marks[None, :] > 0)
    allowed = allowed & (key_place[None, :] <= query_place[:, None] + reach_rows)
    masked = jnp.where(allowed, scores, MASKED)
    highest = jnp.max(masked, axis=1, keepdims=True)
    exponent = jnp.exp(masked - highest)
    totals = jnp.sum(exponent, axis=1)
    weights = exponent.astype(jnp.bfloat16)
    summed = jnp.dot(weights, window_values, preferred_element_type=jnp.float32)
    result = summed / totals[:, None]
    result = jnp.where((query_marks >= 0)[:, None], result, 0.0)
    context = (
        result.reshape(head_local, token_count, HD)
        .transpose(1, 0, 2)
        .reshape(token_count, head_local * HD)
        .astype(jnp.bfloat16)
    )
    owner_count = gy_count
    page_rows = token_count // PAGE
    capacity = max(2, 2 * page_rows // owner_count)
    owner_of = page_owner[:, 0]
    one_hot = (owner_of[:, None] == jnp.arange(owner_count, dtype=jnp.int32)[None, :]).astype(
        jnp.int32
    )
    earlier = jnp.cumsum(one_hot, axis=0) - one_hot
    rank_in = jnp.sum(earlier * one_hot, axis=1)
    slot_of = owner_of * capacity + rank_in
    kv_pages = own_kv.reshape(2, page_rows, PAGE * quarter).transpose(1, 0, 2)
    send_kv = (
        jnp.zeros((owner_count * capacity, 2, PAGE * quarter), jnp.bfloat16)
        .at[slot_of]
        .set(kv_pages)
    )
    send_kv = send_kv.reshape(owner_count, capacity, 2, PAGE * quarter)
    got_kv = lax.all_to_all(send_kv, "gy", split_axis=0, concat_axis=0, tiled=True)
    got_kv = got_kv.reshape(owner_count * capacity, 2, PAGE, quarter)
    key_cache = got_kv[:, 0]
    value_cache = got_kv[:, 1]
    return (context, key_cache, value_cache)


def solution(mesh):
    placed = (
        P("gy", "gx"),
        P(),
        P("gy", "gx"),
        P("gy", "gx"),
        P("gy", "gx"),
        P("gy"),
        P("gy"),
        P("gy", None),
    )
    return jax.shard_map(
        shards,
        mesh=mesh,
        in_specs=placed,
        out_specs=(P("gy", "gx"), P("gy", None, "gx"), P("gy", None, "gx")),
        check_vma=False,
    )
```

```python
import jax
import jax.numpy as jnp
from jax import lax
from jax.sharding import PartitionSpec as P

D = 8192
HD = 128
PAGE = 16


EPSILON = 1e-05
THETA = 500000.0
MASKED = -1e30


def shifted(value, axis, by):
    count = lax.axis_size(axis)
    pairs = [(i, i + by) for i in range(count) if 0 <= i + by < count]
    return lax.ppermute(value, axis, pairs)


def partner_route(count, group, k):
    route = []
    for i in range(count):
        base = i - i % group
        route.append((i, base + ((i % group) ^ k)))
    return route


def rope(matrix, places, width, first_pair):
    cols = jnp.arange(matrix.shape[1], dtype=jnp.int32)
    pair_index = first_pair + (cols % width) // 2
    frequency = jnp.power(THETA, -(2.0 * pair_index.astype(jnp.float32)) / HD)
    angles = places.astype(jnp.float32)[:, None] * frequency[None, :]
    cosine = jnp.cos(angles)
    sine_of = jnp.sin(angles)
    following = jnp.roll(matrix, -1, axis=1)
    preceding = jnp.roll(matrix, 1, axis=1)
    even = (cols % 2 == 0)[None, :]
    return jnp.where(
        even, matrix * cosine - following * sine_of, matrix * cosine + preceding * sine_of
    )


def joined(mine, theirs, mine_first):
    return jnp.where(
        mine_first,
        jnp.concatenate([mine, theirs], axis=-1),
        jnp.concatenate([theirs, mine], axis=-1),
    )


def shards(
    tokens_in, norm_gain, query_weight, key_weight, value_weight, segment_ids, positions, page_owner
):
    token_count = tokens_in.shape[0]
    quarter = key_weight.shape[1]
    head_local = query_weight.shape[1] // HD
    quarters = HD // quarter
    gx_count = lax.axis_size("gx")
    gy_count = lax.axis_size("gy")
    spot = lax.axis_index("gx") % quarters
    my_gy = lax.axis_index("gy")
    row_block = query_weight.shape[0]

    kv_weights = jnp.stack([key_weight, value_weight])
    sibling = lax.ppermute(kv_weights, "gx", partner_route(gx_count, quarters, 1))
    half_weights = joined(kv_weights, sibling, spot % 2 == 0)
    local_weights = jnp.concatenate([query_weight, half_weights[0], half_weights[1]], axis=1)
    half_cols = 2 * quarter
    pieces = [(my_gy, local_weights)]
    for k in range(1, gy_count):
        got = lax.ppermute(local_weights, "gy", partner_route(gy_count, gy_count, k))
        pieces.append((my_gy ^ k, got))

    local_float = tokens_in.astype(jnp.float32)
    my_gx = lax.axis_index("gx")
    feature_block = tokens_in.shape[1]
    local_gain = lax.dynamic_slice_in_dim(norm_gain, my_gx * feature_block, feature_block, 0)
    local_normed = (local_float * local_gain.astype(jnp.float32)[None, :]).astype(jnp.bfloat16)
    local_normed, local_float = lax.optimization_barrier((local_normed, local_float))
    local_squares = jnp.sum(local_float * local_float, axis=1)
    square_parts = [local_squares]
    for k in range(1, gx_count):
        square_parts.append(lax.ppermute(local_squares, "gx", partner_route(gx_count, gx_count, k)))
    square_order = jnp.arange(gx_count, dtype=jnp.int32) ^ my_gx
    squares = jnp.sum(jnp.take(jnp.stack(square_parts), square_order, axis=0), axis=0)
    span_count = gy_count // 4
    marks = segment_ids + 1
    mark_list = [marks]
    for shift_by in range(1, span_count + 1):
        mark_list.insert(0, shifted(marks, "gy", shift_by))
    scaling = 1.0 / jnp.sqrt(squares / D + EPSILON)
    query_cols = head_local * HD
    halves = 1
    half_rows = token_count // halves
    query_halves, kv_halves, head_halves = [], [], []
    for h in range(halves):
        rows_of = slice(h * half_rows, (h + 1) * half_rows)
        normed = lax.all_gather(local_normed[rows_of], "gx", axis=0, tiled=False)
        per_piece = row_block // feature_block
        normed = normed.reshape(gx_count // per_piece, per_piece, half_rows, feature_block)
        if head_halves:
            normed, head_halves[-1] = lax.optimization_barrier((normed, head_halves[-1]))
        products = None
        for source, block in pieces:
            rows = lax.dynamic_index_in_dim(normed, source, 0, keepdims=False)
            weights_of = block.reshape(per_piece, feature_block, block.shape[1])
            part = jnp.einsum("btd,bdc->tc", rows, weights_of, preferred_element_type=jnp.float32)
            products = part if products is None else products + part
        projected = products * scaling[rows_of, None]
        places = positions[rows_of]
        key_half = rope(
            projected[:, query_cols : query_cols + half_cols],
            places,
            half_cols,
            (spot // 2) * quarter,
        ).astype(jnp.bfloat16)
        value_half = projected[:, query_cols + half_cols :].astype(jnp.bfloat16)
        query_halves.append(rope(projected[:, :query_cols], places, HD, 0).astype(jnp.bfloat16))
        half_kv = jnp.stack([key_half, value_half])
        kv_halves.append(lax.dynamic_slice_in_dim(half_kv, (spot % 2) * quarter, quarter, 2))
        low_half = (spot // 2) % 2 == 0
        window_list = [
            joined(half_kv, lax.ppermute(half_kv, "gx", partner_route(gx_count, quarters, 2)), low_half)
        ]
        for shift_by in range(1, span_count + 1):
            route = []
            for i in range(gx_count):
                peer = i - i % quarters + ((i % quarters) ^ 2)
                for j in range(gy_count - shift_by):
                    route.append((i * gy_count + j, peer * gy_count + j + shift_by))
            same = shifted(half_kv, "gy", shift_by)
            other = lax.ppermute(half_kv, ("gx", "gy"), route)
            window_list.insert(0, joined(same, other, low_half))
        held = jnp.concatenate(window_list, axis=1)
        head_halves.append(held.reshape(2, span_count + 1, half_rows, HD))
    queries = jnp.concatenate(query_halves, axis=0)
    own_kv = jnp.concatenate(kv_halves, axis=1)
    key_piece = own_kv[0]
    value_piece = own_kv[1]
    window_kv = jnp.stack(head_halves, axis=2).reshape(2, (span_count + 1) * token_count, HD)
    window_keys = window_kv[0]
    window_values = window_kv[1]
    window_marks = jnp.concatenate(mark_list, axis=0)
    reach_rows = span_count * token_count
    query_rows = (
        queries.reshape(token_count, head_local, HD)
        .transpose(1, 0, 2)
        .reshape(head_local * token_count, HD)
    )
    scores = lax.dot_general(
        query_rows, window_keys, (((1,), (1,)), ((), ())), preferred_element_type=jnp.float32
    ) * HD ** (-0.5)
    query_marks = jnp.tile(segment_ids, head_local)
    query_place = jnp.tile(jnp.arange(token_count, dtype=jnp.int32), head_local)
    key_place = jnp.arange(window_keys.shape[0], dtype=jnp.int32)
    allowed = (window_marks[None, :] == query_marks[:, None] + 1) & (window_marks[None, :] > 0)
    allowed = allowed & (key_place[None, :] <= query_place[:, None] + reach_rows)
    masked = jnp.where(allowed, scores, MASKED)
    highest = jnp.max(masked, axis=1, keepdims=True)
    exponent = jnp.exp(masked - highest)
    totals = jnp.sum(exponent, axis=1)
    weights = exponent.astype(jnp.bfloat16)
    summed = jnp.dot(weights, window_values, preferred_element_type=jnp.float32)
    result = summed / totals[:, None]
    result = jnp.where((query_marks >= 0)[:, None], result, 0.0)
    context = (
        result.reshape(head_local, token_count, HD)
        .transpose(1, 0, 2)
        .reshape(token_count, head_local * HD)
        .astype(jnp.bfloat16)
    )
    owner_count = gy_count
    page_rows = token_count // PAGE
    capacity = max(2, 2 * page_rows // owner_count)
    owner_of = page_owner[:, 0]
    one_hot = (owner_of[:, None] == jnp.arange(owner_count, dtype=jnp.int32)[None, :]).astype(
        jnp.int32
    )
    earlier = jnp.cumsum(one_hot, axis=0) - one_hot
    rank_in = jnp.sum(earlier * one_hot, axis=1)
    slot_of = owner_of * capacity + rank_in
    kv_pages = own_kv.reshape(2, page_rows, PAGE * quarter).transpose(1, 0, 2)
    send_kv = (
        jnp.zeros((owner_count * capacity, 2, PAGE * quarter), jnp.bfloat16)
        .at[slot_of]
        .set(kv_pages)
    )
    send_kv = send_kv.reshape(owner_count, capacity, 2, PAGE * quarter)
    got_kv = lax.all_to_all(send_kv, "gy", split_axis=0, concat_axis=0, tiled=True)
    got_kv = got_kv.reshape(owner_count * capacity, 2, PAGE, quarter)
    key_cache = got_kv[:, 0]
    value_cache = got_kv[:, 1]
    return (context, key_cache, value_cache)


def solution(mesh):
    placed = (
        P("gy", "gx"),
        P(),
        P("gy", "gx"),
        P("gy", "gx"),
        P("gy", "gx"),
        P("gy"),
        P("gy"),
        P("gy", None),
    )
    return jax.shard_map(
        shards,
        mesh=mesh,
        in_specs=placed,
        out_specs=(P("gy", "gx"), P("gy", None, "gx"), P("gy", None, "gx")),
        check_vma=False,
    )
```

```python
import jax
import jax.numpy as jnp
from jax import lax
from jax.sharding import PartitionSpec as P

D = 8192
HD = 128
PAGE = 16


EPSILON = 1e-05
THETA = 500000.0
MASKED = -1e30


def shifted(value, axis, by):
    count = lax.axis_size(axis)
    pairs = [(i, i + by) for i in range(count) if 0 <= i + by < count]
    return lax.ppermute(value, axis, pairs)


def partner_route(count, group, k):
    route = []
    for i in range(count):
        base = i - i % group
        route.append((i, base + ((i % group) ^ k)))
    return route


def rope(matrix, places, width, first_pair):
    cols = jnp.arange(matrix.shape[1], dtype=jnp.int32)
    pair_index = first_pair + (cols % width) // 2
    frequency = jnp.power(THETA, -(2.0 * pair_index.astype(jnp.float32)) / HD)
    angles = places.astype(jnp.float32)[:, None] * frequency[None, :]
    cosine = jnp.cos(angles)
    sine_of = jnp.sin(angles)
    following = jnp.roll(matrix, -1, axis=1)
    preceding = jnp.roll(matrix, 1, axis=1)
    even = (cols % 2 == 0)[None, :]
    return jnp.where(
        even, matrix * cosine - following * sine_of, matrix * cosine + preceding * sine_of
    )


def joined(mine, theirs, mine_first):
    return jnp.where(
        mine_first,
        jnp.concatenate([mine, theirs], axis=-1),
        jnp.concatenate([theirs, mine], axis=-1),
    )


def shards(
    tokens_in, norm_gain, query_weight, key_weight, value_weight, segment_ids, positions, page_owner
):
    token_count = tokens_in.shape[0]
    quarter = key_weight.shape[1]
    head_local = query_weight.shape[1] // HD
    quarters = HD // quarter
    gx_count = lax.axis_size("gx")
    gy_count = lax.axis_size("gy")
    spot = lax.axis_index("gx") % quarters
    my_gy = lax.axis_index("gy")
    row_block = query_weight.shape[0]

    kv_weights = jnp.stack([key_weight, value_weight])
    sibling = lax.ppermute(kv_weights, "gx", partner_route(gx_count, quarters, 1))
    half_weights = joined(kv_weights, sibling, spot % 2 == 0)
    local_weights = jnp.concatenate([query_weight, half_weights[0], half_weights[1]], axis=1)
    half_cols = 2 * quarter
    pieces = [(my_gy, local_weights)]
    for k in range(1, gy_count):
        got = lax.ppermute(local_weights, "gy", partner_route(gy_count, gy_count, k))
        pieces.append((my_gy ^ k, got))

    local_float = tokens_in.astype(jnp.float32)
    my_gx = lax.axis_index("gx")
    feature_block = tokens_in.shape[1]
    local_gain = lax.dynamic_slice_in_dim(norm_gain, my_gx * feature_block, feature_block, 0)
    local_normed = (local_float * local_gain.astype(jnp.float32)[None, :]).astype(jnp.bfloat16)
    local_squares = jnp.sum(local_float * local_float, axis=1)
    square_parts = [local_squares]
    for k in range(1, gx_count):
        square_parts.append(lax.ppermute(local_squares, "gx", partner_route(gx_count, gx_count, k)))
    square_order = jnp.arange(gx_count, dtype=jnp.int32) ^ my_gx
    squares = jnp.sum(jnp.take(jnp.stack(square_parts), square_order, axis=0), axis=0)
    span_count = gy_count // 4
    marks = segment_ids + 1
    mark_list = [marks]
    for shift_by in range(1, span_count + 1):
        mark_list.insert(0, shifted(marks, "gy", shift_by))
    scaling = 1.0 / jnp.sqrt(squares / D + EPSILON)
    query_cols = head_local * HD
    halves = 1
    half_rows = token_count // halves
    query_halves, kv_halves, head_halves = [], [], []
    for h in range(halves):
        rows_of = slice(h * half_rows, (h + 1) * half_rows)
        normed = lax.all_gather(local_normed[rows_of], "gx", axis=0, tiled=False)
        per_piece = row_block // feature_block
        normed = normed.reshape(gx_count // per_piece, per_piece, half_rows, feature_block)
        if head_halves:
            normed, head_halves[-1] = lax.optimization_barrier((normed, head_halves[-1]))
        products = None
        for source, block in pieces:
            rows = lax.dynamic_index_in_dim(normed, source, 0, keepdims=False)
            weights_of = block.reshape(per_piece, feature_block, block.shape[1])
            part = jnp.einsum("btd,bdc->tc", rows, weights_of, preferred_element_type=jnp.float32)
            products = part if products is None else products + part
        projected = products * scaling[rows_of, None]
        places = positions[rows_of]
        key_half = rope(
            projected[:, query_cols : query_cols + half_cols],
            places,
            half_cols,
            (spot // 2) * quarter,
        ).astype(jnp.bfloat16)
        value_half = projected[:, query_cols + half_cols :].astype(jnp.bfloat16)
        query_halves.append(rope(projected[:, :query_cols], places, HD, 0).astype(jnp.bfloat16))
        half_kv = jnp.stack([key_half, value_half])
        kv_halves.append(lax.dynamic_slice_in_dim(half_kv, (spot % 2) * quarter, quarter, 2))
        low_half = (spot // 2) % 2 == 0
        window_list = [
            joined(half_kv, lax.ppermute(half_kv, "gx", partner_route(gx_count, quarters, 2)), low_half)
        ]
        for shift_by in range(1, span_count + 1):
            route = []
            for i in range(gx_count):
                peer = i - i % quarters + ((i % quarters) ^ 2)
                for j in range(gy_count - shift_by):
                    route.append((i * gy_count + j, peer * gy_count + j + shift_by))
            same = shifted(half_kv, "gy", shift_by)
            other = lax.ppermute(half_kv, ("gx", "gy"), route)
            window_list.insert(0, joined(same, other, low_half))
        held = jnp.concatenate(window_list, axis=1)
        head_halves.append(held.reshape(2, span_count + 1, half_rows, HD))
    queries = jnp.concatenate(query_halves, axis=0)
    own_kv = jnp.concatenate(kv_halves, axis=1)
    key_piece = own_kv[0]
    value_piece = own_kv[1]
    window_kv = jnp.stack(head_halves, axis=2).reshape(2, (span_count + 1) * token_count, HD)
    window_keys = window_kv[0]
    window_values = window_kv[1]
    window_marks = jnp.concatenate(mark_list, axis=0)
    reach_rows = span_count * token_count
    query_rows = (
        queries.reshape(token_count, head_local, HD)
        .transpose(1, 0, 2)
        .reshape(head_local * token_count, HD)
    )
    scores = lax.dot_general(
        query_rows, window_keys, (((1,), (1,)), ((), ())), preferred_element_type=jnp.float32
    ) * HD ** (-0.5)
    query_marks = jnp.tile(segment_ids, head_local)
    query_place = jnp.tile(jnp.arange(token_count, dtype=jnp.int32), head_local)
    key_place = jnp.arange(window_keys.shape[0], dtype=jnp.int32)
    allowed = (window_marks[None, :] == query_marks[:, None] + 1) & (window_marks[None, :] > 0)
    allowed = allowed & (key_place[None, :] <= query_place[:, None] + reach_rows)
    masked = jnp.where(allowed, scores, MASKED)
    highest = jnp.max(masked, axis=1, keepdims=True)
    exponent = jnp.exp(masked - highest)
    totals = jnp.sum(exponent, axis=1)
    weights = exponent.astype(jnp.bfloat16)
    summed = jnp.dot(weights, window_values, preferred_element_type=jnp.float32)
    result = summed / totals[:, None]
    result = jnp.where((query_marks >= 0)[:, None], result, 0.0)
    context = (
        result.reshape(head_local, token_count, HD)
        .transpose(1, 0, 2)
        .reshape(token_count, head_local * HD)
        .astype(jnp.bfloat16)
    )
    owner_count = gy_count
    page_rows = token_count // PAGE
    capacity = max(2, 2 * page_rows // owner_count)
    owner_of = page_owner[:, 0]
    one_hot = (owner_of[:, None] == jnp.arange(owner_count, dtype=jnp.int32)[None, :]).astype(
        jnp.int32
    )
    earlier = jnp.cumsum(one_hot, axis=0) - one_hot
    rank_in = jnp.sum(earlier * one_hot, axis=1)
    slot_of = owner_of * capacity + rank_in
    kv_pages = own_kv.reshape(2, page_rows, PAGE * quarter).transpose(1, 0, 2)
    send_kv = (
        jnp.zeros((owner_count * capacity, 2, PAGE * quarter), jnp.bfloat16)
        .at[slot_of]
        .set(kv_pages)
    )
    send_kv = send_kv.reshape(owner_count, capacity, 2, PAGE * quarter)
    gathered = lax.all_gather(send_kv, "gy", axis=0, tiled=False)
    got_kv = lax.dynamic_index_in_dim(gathered, my_gy, 1, keepdims=False)
    got_kv = got_kv.reshape(owner_count * capacity, 2, PAGE, quarter)
    key_cache = got_kv[:, 0]
    value_cache = got_kv[:, 1]
    return (context, key_cache, value_cache)


def solution(mesh):
    placed = (
        P("gy", "gx"),
        P(),
        P("gy", "gx"),
        P("gy", "gx"),
        P("gy", "gx"),
        P("gy"),
        P("gy"),
        P("gy", None),
    )
    return jax.shard_map(
        shards,
        mesh=mesh,
        in_specs=placed,
        out_specs=(P("gy", "gx"), P("gy", None, "gx"), P("gy", None, "gx")),
        check_vma=False,
    )
```

```python
import jax
import jax.numpy as jnp
from jax import lax
from jax.sharding import PartitionSpec as P

D = 8192
HD = 128
PAGE = 16


EPSILON = 1e-05
THETA = 500000.0
MASKED = -1e30


def shifted(value, axis, by):
    count = lax.axis_size(axis)
    pairs = [(i, i + by) for i in range(count) if 0 <= i + by < count]
    return lax.ppermute(value, axis, pairs)


def partner_route(count, group, k):
    route = []
    for i in range(count):
        base = i - i % group
        route.append((i, base + ((i % group) ^ k)))
    return route


def rope(matrix, places, width, first_pair):
    cols = jnp.arange(matrix.shape[1], dtype=jnp.int32)
    pair_index = first_pair + (cols % width) // 2
    frequency = jnp.power(THETA, -(2.0 * pair_index.astype(jnp.float32)) / HD)
    angles = places.astype(jnp.float32)[:, None] * frequency[None, :]
    cosine = jnp.cos(angles)
    sine_of = jnp.sin(angles)
    following = jnp.roll(matrix, -1, axis=1)
    preceding = jnp.roll(matrix, 1, axis=1)
    even = (cols % 2 == 0)[None, :]
    return jnp.where(
        even, matrix * cosine - following * sine_of, matrix * cosine + preceding * sine_of
    )


def joined(mine, theirs, mine_first):
    return jnp.where(
        mine_first,
        jnp.concatenate([mine, theirs], axis=-1),
        jnp.concatenate([theirs, mine], axis=-1),
    )


def shards(
    tokens_in, norm_gain, query_weight, key_weight, value_weight, segment_ids, positions, page_owner
):
    token_count = tokens_in.shape[0]
    quarter = key_weight.shape[1]
    head_local = query_weight.shape[1] // HD
    quarters = HD // quarter
    gx_count = lax.axis_size("gx")
    gy_count = lax.axis_size("gy")
    spot = lax.axis_index("gx") % quarters
    my_gy = lax.axis_index("gy")
    row_block = query_weight.shape[0]

    kv_weights = jnp.stack([key_weight, value_weight])
    sibling = lax.ppermute(kv_weights, "gx", partner_route(gx_count, quarters, 1))
    half_weights = joined(kv_weights, sibling, spot % 2 == 0)
    local_weights = jnp.concatenate([query_weight, half_weights[0], half_weights[1]], axis=1)
    half_cols = 2 * quarter
    pieces = [(my_gy, local_weights)]
    for k in range(1, gy_count):
        got = lax.ppermute(local_weights, "gy", partner_route(gy_count, gy_count, k))
        pieces.append((my_gy ^ k, got))

    local_float = tokens_in.astype(jnp.float32)
    my_gx = lax.axis_index("gx")
    feature_block = tokens_in.shape[1]
    local_gain = lax.dynamic_slice_in_dim(norm_gain, my_gx * feature_block, feature_block, 0)
    local_normed = (local_float * local_gain.astype(jnp.float32)[None, :]).astype(jnp.bfloat16)
    local_squares = jnp.sum(local_float * local_float, axis=1)
    square_parts = [local_squares]
    for k in range(1, gx_count):
        square_parts.append(lax.ppermute(local_squares, "gx", partner_route(gx_count, gx_count, k)))
    square_order = jnp.arange(gx_count, dtype=jnp.int32) ^ my_gx
    squares = jnp.sum(jnp.take(jnp.stack(square_parts), square_order, axis=0), axis=0)
    span_count = gy_count // 4
    marks = segment_ids + 1
    mark_list = [marks]
    for shift_by in range(1, span_count + 1):
        mark_list.insert(0, shifted(marks, "gy", shift_by))
    scaling = 1.0 / jnp.sqrt(squares / D + EPSILON)
    query_cols = head_local * HD
    halves = 1
    half_rows = token_count // halves
    query_halves, kv_halves, head_halves = [], [], []
    for h in range(halves):
        rows_of = slice(h * half_rows, (h + 1) * half_rows)
        normed = lax.all_gather(local_normed[rows_of], "gx", axis=0, tiled=False)
        per_piece = row_block // feature_block
        normed = normed.reshape(gx_count // per_piece, per_piece, half_rows, feature_block)
        if head_halves:
            normed, head_halves[-1] = lax.optimization_barrier((normed, head_halves[-1]))
        products = None
        for source, block in pieces:
            rows = lax.dynamic_index_in_dim(normed, source, 0, keepdims=False)
            weights_of = block.reshape(per_piece, feature_block, block.shape[1])
            part = jnp.einsum("btd,bdc->tc", rows, weights_of, preferred_element_type=jnp.float32)
            products = part if products is None else products + part
        projected = products * scaling[rows_of, None]
        places = positions[rows_of]
        key_half = rope(
            projected[:, query_cols : query_cols + half_cols],
            places,
            half_cols,
            (spot // 2) * quarter,
        ).astype(jnp.bfloat16)
        value_half = projected[:, query_cols + half_cols :].astype(jnp.bfloat16)
        query_halves.append(rope(projected[:, :query_cols], places, HD, 0).astype(jnp.bfloat16))
        half_kv = jnp.stack([key_half, value_half])
        kv_halves.append(lax.dynamic_slice_in_dim(half_kv, (spot % 2) * quarter, quarter, 2))
        low_half = (spot // 2) % 2 == 0
        window_list = [
            joined(half_kv, lax.ppermute(half_kv, "gx", partner_route(gx_count, quarters, 2)), low_half)
        ]
        for shift_by in range(1, span_count + 1):
            route = []
            for i in range(gx_count):
                peer = i - i % quarters + ((i % quarters) ^ 2)
                for j in range(gy_count - shift_by):
                    route.append((i * gy_count + j, peer * gy_count + j + shift_by))
            same = shifted(half_kv, "gy", shift_by)
            other = lax.ppermute(half_kv, ("gx", "gy"), route)
            window_list.insert(0, joined(same, other, low_half))
        held = jnp.concatenate(window_list, axis=1)
        head_halves.append(held.reshape(2, span_count + 1, half_rows, HD))
    queries = jnp.concatenate(query_halves, axis=0)
    own_kv = jnp.concatenate(kv_halves, axis=1)
    key_piece = own_kv[0]
    value_piece = own_kv[1]
    window_kv = jnp.stack(head_halves, axis=2).reshape(2, (span_count + 1) * token_count, HD)
    window_keys = window_kv[0]
    window_values = window_kv[1]
    window_marks = jnp.concatenate(mark_list, axis=0)
    reach_rows = span_count * token_count
    query_rows = (
        queries.reshape(token_count, head_local, HD)
        .transpose(1, 0, 2)
        .reshape(head_local * token_count, HD)
    )
    scores = lax.dot_general(
        query_rows, window_keys, (((1,), (1,)), ((), ())), preferred_element_type=jnp.float32
    ) * HD ** (-0.5)
    query_marks = jnp.tile(segment_ids, head_local)
    query_place = jnp.tile(jnp.arange(token_count, dtype=jnp.int32), head_local)
    key_place = jnp.arange(window_keys.shape[0], dtype=jnp.int32)
    allowed = (window_marks[None, :] == query_marks[:, None] + 1) & (window_marks[None, :] > 0)
    allowed = allowed & (key_place[None, :] <= query_place[:, None] + reach_rows)
    masked = jnp.where(allowed, scores, MASKED)
    highest = jnp.max(masked, axis=1, keepdims=True)
    exponent = jnp.exp(masked - highest)
    totals = jnp.sum(exponent, axis=1)
    weights = exponent.astype(jnp.bfloat16)
    summed = jnp.dot(weights, window_values, preferred_element_type=jnp.float32)
    result = summed / totals[:, None]
    result = jnp.where((query_marks >= 0)[:, None], result, 0.0)
    context = (
        result.reshape(head_local, token_count, HD)
        .transpose(1, 0, 2)
        .reshape(token_count, head_local * HD)
        .astype(jnp.bfloat16)
    )
    owner_count = gy_count
    page_rows = token_count // PAGE
    capacity = max(2, 2 * page_rows // owner_count)
    owner_of = page_owner[:, 0]
    one_hot = (owner_of[:, None] == jnp.arange(owner_count, dtype=jnp.int32)[None, :]).astype(
        jnp.int32
    )
    earlier = jnp.cumsum(one_hot, axis=0) - one_hot
    rank_in = jnp.sum(earlier * one_hot, axis=1)
    slot_of = owner_of * capacity + rank_in
    kv_pages = own_kv.reshape(2, page_rows, PAGE * quarter).transpose(1, 0, 2)
    send_kv = (
        jnp.zeros((owner_count * capacity, 2, PAGE * quarter), jnp.bfloat16)
        .at[slot_of]
        .set(kv_pages)
    )
    send_kv = send_kv.reshape(owner_count, capacity, 2, PAGE * quarter)
    got_kv = lax.all_to_all(send_kv, "gy", split_axis=0, concat_axis=0, tiled=True)
    got_kv, context = lax.optimization_barrier((got_kv, context))
    got_kv = got_kv.reshape(owner_count * capacity, 2, PAGE, quarter)
    key_cache = got_kv[:, 0]
    value_cache = got_kv[:, 1]
    return (context, key_cache, value_cache)


def solution(mesh):
    placed = (
        P("gy", "gx"),
        P(),
        P("gy", "gx"),
        P("gy", "gx"),
        P("gy", "gx"),
        P("gy"),
        P("gy"),
        P("gy", None),
    )
    return jax.shard_map(
        shards,
        mesh=mesh,
        in_specs=placed,
        out_specs=(P("gy", "gx"), P("gy", None, "gx"), P("gy", None, "gx")),
        check_vma=False,
    )
```

```python
import jax
import jax.numpy as jnp
from jax import lax
from jax.sharding import PartitionSpec as P

D = 8192
HD = 128
PAGE = 16


EPSILON = 1e-05
THETA = 500000.0
MASKED = -1e30


def shifted(value, axis, by):
    count = lax.axis_size(axis)
    pairs = [(i, i + by) for i in range(count) if 0 <= i + by < count]
    return lax.ppermute(value, axis, pairs)


def partner_route(count, group, k):
    route = []
    for i in range(count):
        base = i - i % group
        route.append((i, base + ((i % group) ^ k)))
    return route


def rope(matrix, places, width, first_pair):
    cols = jnp.arange(matrix.shape[1], dtype=jnp.int32)
    pair_index = first_pair + (cols % width) // 2
    frequency = jnp.power(THETA, -(2.0 * pair_index.astype(jnp.float32)) / HD)
    angles = places.astype(jnp.float32)[:, None] * frequency[None, :]
    cosine = jnp.cos(angles)
    sine_of = jnp.sin(angles)
    following = jnp.roll(matrix, -1, axis=1)
    preceding = jnp.roll(matrix, 1, axis=1)
    even = (cols % 2 == 0)[None, :]
    return jnp.where(
        even, matrix * cosine - following * sine_of, matrix * cosine + preceding * sine_of
    )


def joined(mine, theirs, mine_first):
    return jnp.where(
        mine_first,
        jnp.concatenate([mine, theirs], axis=-1),
        jnp.concatenate([theirs, mine], axis=-1),
    )


def shards(
    tokens_in, norm_gain, query_weight, key_weight, value_weight, segment_ids, positions, page_owner
):
    token_count = tokens_in.shape[0]
    quarter = key_weight.shape[1]
    head_local = query_weight.shape[1] // HD
    quarters = HD // quarter
    gx_count = lax.axis_size("gx")
    gy_count = lax.axis_size("gy")
    spot = lax.axis_index("gx") % quarters
    my_gy = lax.axis_index("gy")
    row_block = query_weight.shape[0]

    kv_weights = jnp.stack([key_weight, value_weight])
    sibling = lax.ppermute(kv_weights, "gx", partner_route(gx_count, quarters, 1))
    half_weights = joined(kv_weights, sibling, spot % 2 == 0)
    local_weights = jnp.concatenate([query_weight, half_weights[0], half_weights[1]], axis=1)
    half_cols = 2 * quarter
    pieces = [(my_gy, local_weights)]
    for k in range(1, gy_count):
        got = lax.ppermute(local_weights, "gy", partner_route(gy_count, gy_count, k))
        pieces.append((my_gy ^ k, got))

    local_float = tokens_in.astype(jnp.float32)
    my_gx = lax.axis_index("gx")
    feature_block = tokens_in.shape[1]
    local_gain = lax.dynamic_slice_in_dim(norm_gain, my_gx * feature_block, feature_block, 0)
    local_normed = (local_float * local_gain.astype(jnp.float32)[None, :]).astype(jnp.bfloat16)
    local_normed, local_float = lax.optimization_barrier((local_normed, local_float))
    local_squares = jnp.sum(local_float * local_float, axis=1)
    square_parts = [local_squares]
    for k in range(1, gx_count):
        square_parts.append(lax.ppermute(local_squares, "gx", partner_route(gx_count, gx_count, k)))
    square_order = jnp.arange(gx_count, dtype=jnp.int32) ^ my_gx
    squares = jnp.sum(jnp.take(jnp.stack(square_parts), square_order, axis=0), axis=0)
    span_count = gy_count // 4
    marks = segment_ids + 1
    mark_list = [marks]
    for shift_by in range(1, span_count + 1):
        mark_list.insert(0, shifted(marks, "gy", shift_by))
    scaling = 1.0 / jnp.sqrt(squares / D + EPSILON)
    query_cols = head_local * HD
    halves = 1
    half_rows = token_count // halves
    query_halves, kv_halves, head_halves = [], [], []
    for h in range(halves):
        rows_of = slice(h * half_rows, (h + 1) * half_rows)
        normed = lax.all_gather(local_normed[rows_of], "gx", axis=0, tiled=False)
        per_piece = row_block // feature_block
        normed = normed.reshape(gx_count // per_piece, per_piece, half_rows, feature_block)
        if head_halves:
            normed, head_halves[-1] = lax.optimization_barrier((normed, head_halves[-1]))
        products = None
        for source, block in pieces:
            rows = lax.dynamic_index_in_dim(normed, source, 0, keepdims=False)
            weights_of = block.reshape(per_piece, feature_block, block.shape[1])
            part = jnp.einsum("btd,bdc->tc", rows, weights_of, preferred_element_type=jnp.float32)
            products = part if products is None else products + part
        projected = products * scaling[rows_of, None]
        places = positions[rows_of]
        key_half = rope(
            projected[:, query_cols : query_cols + half_cols],
            places,
            half_cols,
            (spot // 2) * quarter,
        ).astype(jnp.bfloat16)
        value_half = projected[:, query_cols + half_cols :].astype(jnp.bfloat16)
        query_halves.append(rope(projected[:, :query_cols], places, HD, 0).astype(jnp.bfloat16))
        half_kv = jnp.stack([key_half, value_half])
        kv_halves.append(lax.dynamic_slice_in_dim(half_kv, (spot % 2) * quarter, quarter, 2))
        low_half = (spot // 2) % 2 == 0
        window_list = [
            joined(half_kv, lax.ppermute(half_kv, "gx", partner_route(gx_count, quarters, 2)), low_half)
        ]
        for shift_by in range(1, span_count + 1):
            route = []
            for i in range(gx_count):
                peer = i - i % quarters + ((i % quarters) ^ 2)
                for j in range(gy_count - shift_by):
                    route.append((i * gy_count + j, peer * gy_count + j + shift_by))
            same = shifted(half_kv, "gy", shift_by)
            other = lax.ppermute(half_kv, ("gx", "gy"), route)
            window_list.insert(0, joined(same, other, low_half))
        held = jnp.concatenate(window_list, axis=1)
        head_halves.append(held.reshape(2, span_count + 1, half_rows, HD))
    queries = jnp.concatenate(query_halves, axis=0)
    own_kv = jnp.concatenate(kv_halves, axis=1)
    key_piece = own_kv[0]
    value_piece = own_kv[1]
    window_kv = jnp.stack(head_halves, axis=2).reshape(2, (span_count + 1) * token_count, HD)
    window_keys = window_kv[0]
    window_values = window_kv[1]
    window_marks = jnp.concatenate(mark_list, axis=0)
    reach_rows = span_count * token_count
    query_rows = (
        queries.reshape(token_count, head_local, HD)
        .transpose(1, 0, 2)
        .reshape(head_local * token_count, HD)
    )
    scores = lax.dot_general(
        query_rows, window_keys, (((1,), (1,)), ((), ())), preferred_element_type=jnp.float32
    ) * HD ** (-0.5)
    query_marks = jnp.tile(segment_ids, head_local)
    query_place = jnp.tile(jnp.arange(token_count, dtype=jnp.int32), head_local)
    key_place = jnp.arange(window_keys.shape[0], dtype=jnp.int32)
    allowed = (window_marks[None, :] == query_marks[:, None] + 1) & (window_marks[None, :] > 0)
    allowed = allowed & (key_place[None, :] <= query_place[:, None] + reach_rows)
    masked = jnp.where(allowed, scores, MASKED)
    highest = jnp.max(masked, axis=1, keepdims=True)
    exponent = jnp.exp(masked - highest)
    totals = jnp.sum(exponent, axis=1)
    weights = exponent.astype(jnp.bfloat16)
    summed = jnp.dot(weights, window_values, preferred_element_type=jnp.float32)
    result = summed / totals[:, None]
    result = jnp.where((query_marks >= 0)[:, None], result, 0.0)
    context = (
        result.reshape(head_local, token_count, HD)
        .transpose(1, 0, 2)
        .reshape(token_count, head_local * HD)
        .astype(jnp.bfloat16)
    )
    owner_count = gy_count
    page_rows = token_count // PAGE
    capacity = max(2, 2 * page_rows // owner_count)
    owner_of = page_owner[:, 0]
    one_hot = (owner_of[:, None] == jnp.arange(owner_count, dtype=jnp.int32)[None, :]).astype(
        jnp.int32
    )
    earlier = jnp.cumsum(one_hot, axis=0) - one_hot
    rank_in = jnp.sum(earlier * one_hot, axis=1)
    slot_of = owner_of * capacity + rank_in
    kv_pages = own_kv.reshape(2, page_rows, PAGE * quarter).transpose(1, 0, 2)
    send_kv = (
        jnp.zeros((owner_count * capacity, 2, PAGE * quarter), jnp.bfloat16)
        .at[slot_of]
        .set(kv_pages)
    )
    send_kv = send_kv.reshape(owner_count, capacity, 2, PAGE * quarter)
    got_kv = lax.all_to_all(send_kv, "gy", split_axis=0, concat_axis=0, tiled=True)
    got_kv, context = lax.optimization_barrier((got_kv, context))
    got_kv = got_kv.reshape(owner_count * capacity, 2, PAGE, quarter)
    key_cache = got_kv[:, 0]
    value_cache = got_kv[:, 1]
    return (context, key_cache, value_cache)


def solution(mesh):
    placed = (
        P("gy", "gx"),
        P(),
        P("gy", "gx"),
        P("gy", "gx"),
        P("gy", "gx"),
        P("gy"),
        P("gy"),
        P("gy", None),
    )
    return jax.shard_map(
        shards,
        mesh=mesh,
        in_specs=placed,
        out_specs=(P("gy", "gx"), P("gy", None, "gx"), P("gy", None, "gx")),
        check_vma=False,
    )
```

```python
import jax
import jax.numpy as jnp
from jax import lax
from jax.sharding import PartitionSpec as P

D = 8192
HD = 128
PAGE = 16


EPSILON = 1e-05
THETA = 500000.0
MASKED = -1e30


def shifted(value, axis, by):
    count = lax.axis_size(axis)
    pairs = [(i, i + by) for i in range(count) if 0 <= i + by < count]
    return lax.ppermute(value, axis, pairs)


def partner_route(count, group, k):
    route = []
    for i in range(count):
        base = i - i % group
        route.append((i, base + ((i % group) ^ k)))
    return route


def rope(matrix, places, width, first_pair):
    cols = jnp.arange(matrix.shape[1], dtype=jnp.int32)
    pair_index = first_pair + (cols % width) // 2
    frequency = jnp.power(THETA, -(2.0 * pair_index.astype(jnp.float32)) / HD)
    angles = places.astype(jnp.float32)[:, None] * frequency[None, :]
    cosine = jnp.cos(angles)
    sine_of = jnp.sin(angles)
    following = jnp.roll(matrix, -1, axis=1)
    preceding = jnp.roll(matrix, 1, axis=1)
    even = (cols % 2 == 0)[None, :]
    return jnp.where(
        even, matrix * cosine - following * sine_of, matrix * cosine + preceding * sine_of
    )


def joined(mine, theirs, mine_first):
    return jnp.where(
        mine_first,
        jnp.concatenate([mine, theirs], axis=-1),
        jnp.concatenate([theirs, mine], axis=-1),
    )


def shards(
    tokens_in, norm_gain, query_weight, key_weight, value_weight, segment_ids, positions, page_owner
):
    token_count = tokens_in.shape[0]
    quarter = key_weight.shape[1]
    head_local = query_weight.shape[1] // HD
    quarters = HD // quarter
    gx_count = lax.axis_size("gx")
    gy_count = lax.axis_size("gy")
    spot = lax.axis_index("gx") % quarters
    my_gy = lax.axis_index("gy")
    row_block = query_weight.shape[0]

    kv_weights = jnp.stack([key_weight, value_weight])
    sibling = lax.ppermute(kv_weights, "gx", partner_route(gx_count, quarters, 1))
    half_weights = joined(kv_weights, sibling, spot % 2 == 0)
    local_weights = jnp.concatenate([query_weight, half_weights[0], half_weights[1]], axis=1)
    half_cols = 2 * quarter
    pieces = [(my_gy, local_weights)]
    for k in range(1, gy_count):
        got = lax.ppermute(local_weights, "gy", partner_route(gy_count, gy_count, k))
        pieces.append((my_gy ^ k, got))

    local_float = tokens_in.astype(jnp.float32)
    my_gx = lax.axis_index("gx")
    feature_block = tokens_in.shape[1]
    local_gain = lax.dynamic_slice_in_dim(norm_gain, my_gx * feature_block, feature_block, 0)
    local_normed = (local_float * local_gain.astype(jnp.float32)[None, :]).astype(jnp.bfloat16)
    local_normed, local_float = lax.optimization_barrier((local_normed, local_float))
    local_squares = jnp.sum(local_float * local_float, axis=1)
    square_parts = [local_squares]
    for k in range(1, gx_count):
        square_parts.append(lax.ppermute(local_squares, "gx", partner_route(gx_count, gx_count, k)))
    square_order = jnp.arange(gx_count, dtype=jnp.int32) ^ my_gx
    squares = jnp.sum(jnp.take(jnp.stack(square_parts), square_order, axis=0), axis=0)
    span_count = gy_count // 4
    marks = segment_ids + 1
    mark_list = [marks]
    for shift_by in range(1, span_count + 1):
        mark_list.insert(0, shifted(marks, "gy", shift_by))
    scaling = 1.0 / jnp.sqrt(squares / D + EPSILON)
    query_cols = head_local * HD
    halves = 1
    half_rows = token_count // halves
    query_halves, kv_halves, head_halves = [], [], []
    for h in range(halves):
        rows_of = slice(h * half_rows, (h + 1) * half_rows)
        normed = lax.all_gather(local_normed[rows_of], "gx", axis=0, tiled=False)
        per_piece = row_block // feature_block
        normed = normed.reshape(gx_count // per_piece, per_piece, half_rows, feature_block)
        if head_halves:
            normed, head_halves[-1] = lax.optimization_barrier((normed, head_halves[-1]))
        products = None
        for source, block in pieces:
            rows = lax.dynamic_index_in_dim(normed, source, 0, keepdims=False)
            weights_of = block.reshape(per_piece, feature_block, block.shape[1])
            part = jnp.einsum("btd,bdc->tc", rows, weights_of, preferred_element_type=jnp.float32)
            products = part if products is None else products + part
        projected = products * scaling[rows_of, None]
        places = positions[rows_of]
        key_half = rope(
            projected[:, query_cols : query_cols + half_cols],
            places,
            half_cols,
            (spot // 2) * quarter,
        ).astype(jnp.bfloat16)
        value_half = projected[:, query_cols + half_cols :].astype(jnp.bfloat16)
        query_halves.append(rope(projected[:, :query_cols], places, HD, 0).astype(jnp.bfloat16))
        half_kv = jnp.stack([key_half, value_half])
        kv_halves.append(lax.dynamic_slice_in_dim(half_kv, (spot % 2) * quarter, quarter, 2))
        low_half = (spot // 2) % 2 == 0
        other_half = lax.ppermute(half_kv, "gx", partner_route(gx_count, quarters, 2))
        head_now = joined(half_kv, other_half, low_half)
        window_list = [head_now]
        for shift_by in range(1, span_count + 1):
            window_list.insert(0, shifted(head_now, "gy", shift_by))
        held = jnp.concatenate(window_list, axis=1)
        head_halves.append(held.reshape(2, span_count + 1, half_rows, HD))
    queries = jnp.concatenate(query_halves, axis=0)
    own_kv = jnp.concatenate(kv_halves, axis=1)
    key_piece = own_kv[0]
    value_piece = own_kv[1]
    window_kv = jnp.stack(head_halves, axis=2).reshape(2, (span_count + 1) * token_count, HD)
    window_keys = window_kv[0]
    window_values = window_kv[1]
    window_marks = jnp.concatenate(mark_list, axis=0)
    reach_rows = span_count * token_count
    query_rows = (
        queries.reshape(token_count, head_local, HD)
        .transpose(1, 0, 2)
        .reshape(head_local * token_count, HD)
    )
    scores = lax.dot_general(
        query_rows, window_keys, (((1,), (1,)), ((), ())), preferred_element_type=jnp.float32
    ) * HD ** (-0.5)
    query_marks = jnp.tile(segment_ids, head_local)
    query_place = jnp.tile(jnp.arange(token_count, dtype=jnp.int32), head_local)
    key_place = jnp.arange(window_keys.shape[0], dtype=jnp.int32)
    allowed = (window_marks[None, :] == query_marks[:, None] + 1) & (window_marks[None, :] > 0)
    allowed = allowed & (key_place[None, :] <= query_place[:, None] + reach_rows)
    masked = jnp.where(allowed, scores, MASKED)
    highest = jnp.max(masked, axis=1, keepdims=True)
    exponent = jnp.exp(masked - highest)
    totals = jnp.sum(exponent, axis=1)
    weights = exponent.astype(jnp.bfloat16)
    summed = jnp.dot(weights, window_values, preferred_element_type=jnp.float32)
    result = summed / totals[:, None]
    result = jnp.where((query_marks >= 0)[:, None], result, 0.0)
    context = (
        result.reshape(head_local, token_count, HD)
        .transpose(1, 0, 2)
        .reshape(token_count, head_local * HD)
        .astype(jnp.bfloat16)
    )
    owner_count = gy_count
    page_rows = token_count // PAGE
    capacity = max(2, 2 * page_rows // owner_count)
    owner_of = page_owner[:, 0]
    one_hot = (owner_of[:, None] == jnp.arange(owner_count, dtype=jnp.int32)[None, :]).astype(
        jnp.int32
    )
    earlier = jnp.cumsum(one_hot, axis=0) - one_hot
    rank_in = jnp.sum(earlier * one_hot, axis=1)
    slot_of = owner_of * capacity + rank_in
    kv_pages = own_kv.reshape(2, page_rows, PAGE * quarter).transpose(1, 0, 2)
    send_kv = (
        jnp.zeros((owner_count * capacity, 2, PAGE * quarter), jnp.bfloat16)
        .at[slot_of]
        .set(kv_pages)
    )
    send_kv = send_kv.reshape(owner_count, capacity, 2, PAGE * quarter)
    got_kv = lax.all_to_all(send_kv, "gy", split_axis=0, concat_axis=0, tiled=True)
    got_kv, context = lax.optimization_barrier((got_kv, context))
    got_kv = got_kv.reshape(owner_count * capacity, 2, PAGE, quarter)
    key_cache = got_kv[:, 0]
    value_cache = got_kv[:, 1]
    return (context, key_cache, value_cache)


def solution(mesh):
    placed = (
        P("gy", "gx"),
        P(),
        P("gy", "gx"),
        P("gy", "gx"),
        P("gy", "gx"),
        P("gy"),
        P("gy"),
        P("gy", None),
    )
    return jax.shard_map(
        shards,
        mesh=mesh,
        in_specs=placed,
        out_specs=(P("gy", "gx"), P("gy", None, "gx"), P("gy", None, "gx")),
        check_vma=False,
    )
```

```python
import jax
import jax.numpy as jnp
from jax import lax
from jax.sharding import PartitionSpec as P

D = 8192
HD = 128
PAGE = 16


EPSILON = 1e-05
THETA = 500000.0
MASKED = -1e30


def shifted(value, axis, by):
    count = lax.axis_size(axis)
    pairs = [(i, i + by) for i in range(count) if 0 <= i + by < count]
    return lax.ppermute(value, axis, pairs)


def partner_route(count, group, k):
    route = []
    for i in range(count):
        base = i - i % group
        route.append((i, base + ((i % group) ^ k)))
    return route


def rope_tables(places, count, width, first_pair):
    cols = jnp.arange(count, dtype=jnp.int32)
    pair_index = first_pair + (cols % width) // 2
    frequency = jnp.power(THETA, -(2.0 * pair_index.astype(jnp.float32)) / HD)
    angles = places.astype(jnp.float32)[:, None] * frequency[None, :]
    return lax.optimization_barrier((jnp.cos(angles), jnp.sin(angles)))


def rope(matrix, tables):
    cosine, sine_of = tables
    cols = jnp.arange(matrix.shape[1], dtype=jnp.int32)
    following = jnp.roll(matrix, -1, axis=1)
    preceding = jnp.roll(matrix, 1, axis=1)
    even = (cols % 2 == 0)[None, :]
    return jnp.where(
        even, matrix * cosine - following * sine_of, matrix * cosine + preceding * sine_of
    )


def joined(mine, theirs, mine_first):
    return jnp.where(
        mine_first,
        jnp.concatenate([mine, theirs], axis=-1),
        jnp.concatenate([theirs, mine], axis=-1),
    )


def shards(
    tokens_in, norm_gain, query_weight, key_weight, value_weight, segment_ids, positions, page_owner
):
    token_count = tokens_in.shape[0]
    quarter = key_weight.shape[1]
    head_local = query_weight.shape[1] // HD
    quarters = HD // quarter
    gx_count = lax.axis_size("gx")
    gy_count = lax.axis_size("gy")
    spot = lax.axis_index("gx") % quarters
    my_gy = lax.axis_index("gy")
    row_block = query_weight.shape[0]

    kv_weights = jnp.stack([key_weight, value_weight])
    sibling = lax.ppermute(kv_weights, "gx", partner_route(gx_count, quarters, 1))
    half_weights = joined(kv_weights, sibling, spot % 2 == 0)
    local_weights = jnp.concatenate([query_weight, half_weights[0], half_weights[1]], axis=1)
    half_cols = 2 * quarter
    pieces = [(my_gy, local_weights)]
    for k in range(1, gy_count):
        got = lax.ppermute(local_weights, "gy", partner_route(gy_count, gy_count, k))
        pieces.append((my_gy ^ k, got))

    local_float = tokens_in.astype(jnp.float32)
    my_gx = lax.axis_index("gx")
    feature_block = tokens_in.shape[1]
    local_gain = lax.dynamic_slice_in_dim(norm_gain, my_gx * feature_block, feature_block, 0)
    local_normed = (local_float * local_gain.astype(jnp.float32)[None, :]).astype(jnp.bfloat16)
    local_normed, local_float = lax.optimization_barrier((local_normed, local_float))
    local_squares = jnp.sum(local_float * local_float, axis=1)
    square_parts = [local_squares]
    for k in range(1, gx_count):
        square_parts.append(lax.ppermute(local_squares, "gx", partner_route(gx_count, gx_count, k)))
    square_order = jnp.arange(gx_count, dtype=jnp.int32) ^ my_gx
    squares = jnp.sum(jnp.take(jnp.stack(square_parts), square_order, axis=0), axis=0)
    span_count = gy_count // 4
    marks = segment_ids + 1
    mark_list = [marks]
    for shift_by in range(1, span_count + 1):
        mark_list.insert(0, shifted(marks, "gy", shift_by))
    scaling = 1.0 / jnp.sqrt(squares / D + EPSILON)
    query_cols = head_local * HD
    halves = 1
    half_rows = token_count // halves
    query_halves, kv_halves, head_halves = [], [], []
    for h in range(halves):
        rows_of = slice(h * half_rows, (h + 1) * half_rows)
        normed = lax.all_gather(local_normed[rows_of], "gx", axis=0, tiled=False)
        per_piece = row_block // feature_block
        normed = normed.reshape(gx_count // per_piece, per_piece, half_rows, feature_block)
        if head_halves:
            normed, head_halves[-1] = lax.optimization_barrier((normed, head_halves[-1]))
        products = None
        for source, block in pieces:
            rows = lax.dynamic_index_in_dim(normed, source, 0, keepdims=False)
            weights_of = block.reshape(per_piece, feature_block, block.shape[1])
            part = jnp.einsum("btd,bdc->tc", rows, weights_of, preferred_element_type=jnp.float32)
            products = part if products is None else products + part
        projected = products * scaling[rows_of, None]
        places = positions[rows_of]
        key_tables = rope_tables(places, half_cols, half_cols, (spot // 2) * quarter)
        key_half = rope(projected[:, query_cols : query_cols + half_cols], key_tables)
        key_half = key_half.astype(jnp.bfloat16)
        value_half = projected[:, query_cols + half_cols :].astype(jnp.bfloat16)
        query_tables = rope_tables(places, query_cols, HD, 0)
        query_halves.append(rope(projected[:, :query_cols], query_tables).astype(jnp.bfloat16))
        half_kv = jnp.stack([key_half, value_half])
        kv_halves.append(lax.dynamic_slice_in_dim(half_kv, (spot % 2) * quarter, quarter, 2))
        low_half = (spot // 2) % 2 == 0
        window_list = [
            joined(half_kv, lax.ppermute(half_kv, "gx", partner_route(gx_count, quarters, 2)), low_half)
        ]
        for shift_by in range(1, span_count + 1):
            route = []
            for i in range(gx_count):
                peer = i - i % quarters + ((i % quarters) ^ 2)
                for j in range(gy_count - shift_by):
                    route.append((i * gy_count + j, peer * gy_count + j + shift_by))
            same = shifted(half_kv, "gy", shift_by)
            other = lax.ppermute(half_kv, ("gx", "gy"), route)
            window_list.insert(0, joined(same, other, low_half))
        held = jnp.concatenate(window_list, axis=1)
        head_halves.append(held.reshape(2, span_count + 1, half_rows, HD))
    queries = jnp.concatenate(query_halves, axis=0)
    own_kv = jnp.concatenate(kv_halves, axis=1)
    key_piece = own_kv[0]
    value_piece = own_kv[1]
    window_kv = jnp.stack(head_halves, axis=2).reshape(2, (span_count + 1) * token_count, HD)
    window_keys = window_kv[0]
    window_values = window_kv[1]
    window_marks = jnp.concatenate(mark_list, axis=0)
    reach_rows = span_count * token_count
    query_rows = (
        queries.reshape(token_count, head_local, HD)
        .transpose(1, 0, 2)
        .reshape(head_local * token_count, HD)
    )
    scores = lax.dot_general(
        query_rows, window_keys, (((1,), (1,)), ((), ())), preferred_element_type=jnp.float32
    ) * HD ** (-0.5)
    query_marks = jnp.tile(segment_ids, head_local)
    query_place = jnp.tile(jnp.arange(token_count, dtype=jnp.int32), head_local)
    key_place = jnp.arange(window_keys.shape[0], dtype=jnp.int32)
    allowed = (window_marks[None, :] == query_marks[:, None] + 1) & (window_marks[None, :] > 0)
    allowed = allowed & (key_place[None, :] <= query_place[:, None] + reach_rows)
    masked = jnp.where(allowed, scores, MASKED)
    highest = jnp.max(masked, axis=1, keepdims=True)
    exponent = jnp.exp(masked - highest)
    totals = jnp.sum(exponent, axis=1)
    weights = exponent.astype(jnp.bfloat16)
    summed = jnp.dot(weights, window_values, preferred_element_type=jnp.float32)
    result = summed / totals[:, None]
    result = jnp.where((query_marks >= 0)[:, None], result, 0.0)
    context = (
        result.reshape(head_local, token_count, HD)
        .transpose(1, 0, 2)
        .reshape(token_count, head_local * HD)
        .astype(jnp.bfloat16)
    )
    owner_count = gy_count
    page_rows = token_count // PAGE
    capacity = max(2, 2 * page_rows // owner_count)
    owner_of = page_owner[:, 0]
    one_hot = (owner_of[:, None] == jnp.arange(owner_count, dtype=jnp.int32)[None, :]).astype(
        jnp.int32
    )
    earlier = jnp.cumsum(one_hot, axis=0) - one_hot
    rank_in = jnp.sum(earlier * one_hot, axis=1)
    slot_of = owner_of * capacity + rank_in
    kv_pages = own_kv.reshape(2, page_rows, PAGE * quarter).transpose(1, 0, 2)
    send_kv = (
        jnp.zeros((owner_count * capacity, 2, PAGE * quarter), jnp.bfloat16)
        .at[slot_of]
        .set(kv_pages)
    )
    send_kv = send_kv.reshape(owner_count, capacity, 2, PAGE * quarter)
    got_kv = lax.all_to_all(send_kv, "gy", split_axis=0, concat_axis=0, tiled=True)
    got_kv, context = lax.optimization_barrier((got_kv, context))
    got_kv = got_kv.reshape(owner_count * capacity, 2, PAGE, quarter)
    key_cache = got_kv[:, 0]
    value_cache = got_kv[:, 1]
    return (context, key_cache, value_cache)


def solution(mesh):
    placed = (
        P("gy", "gx"),
        P(),
        P("gy", "gx"),
        P("gy", "gx"),
        P("gy", "gx"),
        P("gy"),
        P("gy"),
        P("gy", None),
    )
    return jax.shard_map(
        shards,
        mesh=mesh,
        in_specs=placed,
        out_specs=(P("gy", "gx"), P("gy", None, "gx"), P("gy", None, "gx")),
        check_vma=False,
    )
```

```python
import jax
import jax.numpy as jnp
from jax import lax
from jax.sharding import PartitionSpec as P

D = 8192
HD = 128
PAGE = 16


EPSILON = 1e-05
THETA = 500000.0
MASKED = -1e30


def shifted(value, axis, by):
    count = lax.axis_size(axis)
    pairs = [(i, i + by) for i in range(count) if 0 <= i + by < count]
    return lax.ppermute(value, axis, pairs)


def partner_route(count, group, k):
    route = []
    for i in range(count):
        base = i - i % group
        route.append((i, base + ((i % group) ^ k)))
    return route


def rope_tables(places, count, width, first_pair):
    cols = jnp.arange(count, dtype=jnp.int32)
    pair_index = first_pair + (cols % width) // 2
    frequency = jnp.power(THETA, -(2.0 * pair_index.astype(jnp.float32)) / HD)
    angles = places.astype(jnp.float32)[:, None] * frequency[None, :]
    return lax.optimization_barrier((jnp.cos(angles), jnp.sin(angles)))


def rope(matrix, tables):
    cosine, sine_of = tables
    cols = jnp.arange(matrix.shape[1], dtype=jnp.int32)
    following = jnp.roll(matrix, -1, axis=1)
    preceding = jnp.roll(matrix, 1, axis=1)
    even = (cols % 2 == 0)[None, :]
    return jnp.where(
        even, matrix * cosine - following * sine_of, matrix * cosine + preceding * sine_of
    )


def joined(mine, theirs, mine_first):
    return jnp.where(
        mine_first,
        jnp.concatenate([mine, theirs], axis=-1),
        jnp.concatenate([theirs, mine], axis=-1),
    )


def shards(
    tokens_in, norm_gain, query_weight, key_weight, value_weight, segment_ids, positions, page_owner
):
    token_count = tokens_in.shape[0]
    quarter = key_weight.shape[1]
    head_local = query_weight.shape[1] // HD
    quarters = HD // quarter
    gx_count = lax.axis_size("gx")
    gy_count = lax.axis_size("gy")
    spot = lax.axis_index("gx") % quarters
    my_gy = lax.axis_index("gy")
    row_block = query_weight.shape[0]

    kv_weights = jnp.stack([key_weight, value_weight])
    sibling = lax.ppermute(kv_weights, "gx", partner_route(gx_count, quarters, 1))
    half_weights = joined(kv_weights, sibling, spot % 2 == 0)
    local_weights = jnp.concatenate([query_weight, half_weights[0], half_weights[1]], axis=1)
    half_cols = 2 * quarter
    pieces = [(my_gy, local_weights)]
    for k in range(1, gy_count):
        got = lax.ppermute(local_weights, "gy", partner_route(gy_count, gy_count, k))
        pieces.append((my_gy ^ k, got))

    local_float = tokens_in.astype(jnp.float32)
    my_gx = lax.axis_index("gx")
    feature_block = tokens_in.shape[1]
    local_gain = lax.dynamic_slice_in_dim(norm_gain, my_gx * feature_block, feature_block, 0)
    local_normed = (local_float * local_gain.astype(jnp.float32)[None, :]).astype(jnp.bfloat16)
    local_normed, local_float = lax.optimization_barrier((local_normed, local_float))
    local_squares = jnp.sum(local_float * local_float, axis=1)
    square_parts = [local_squares]
    for k in range(1, gx_count):
        square_parts.append(lax.ppermute(local_squares, "gx", partner_route(gx_count, gx_count, k)))
    square_order = jnp.arange(gx_count, dtype=jnp.int32) ^ my_gx
    squares = jnp.sum(jnp.take(jnp.stack(square_parts), square_order, axis=0), axis=0)
    span_count = gy_count // 4
    marks = segment_ids + 1
    mark_list = [marks]
    for shift_by in range(1, span_count + 1):
        mark_list.insert(0, shifted(marks, "gy", shift_by))
    scaling = 1.0 / jnp.sqrt(squares / D + EPSILON)
    query_cols = head_local * HD
    halves = 1
    half_rows = token_count // halves
    query_halves, kv_halves, head_halves = [], [], []
    for h in range(halves):
        rows_of = slice(h * half_rows, (h + 1) * half_rows)
        normed = lax.all_gather(local_normed[rows_of], "gx", axis=0, tiled=False)
        per_piece = row_block // feature_block
        normed = normed.reshape(gx_count // per_piece, per_piece, half_rows, feature_block)
        if head_halves:
            normed, head_halves[-1] = lax.optimization_barrier((normed, head_halves[-1]))
        products = None
        for source, block in pieces:
            rows = lax.dynamic_index_in_dim(normed, source, 0, keepdims=False)
            weights_of = block.reshape(per_piece, feature_block, block.shape[1])
            part = jnp.einsum("btd,bdc->tc", rows, weights_of, preferred_element_type=jnp.float32)
            products = part if products is None else products + part
        projected = products * scaling[rows_of, None]
        places = positions[rows_of]
        key_tables = rope_tables(places, half_cols, half_cols, (spot // 2) * quarter)
        key_half = rope(projected[:, query_cols : query_cols + half_cols], key_tables)
        key_half = key_half.astype(jnp.bfloat16)
        value_half = projected[:, query_cols + half_cols :].astype(jnp.bfloat16)
        query_tables = rope_tables(places, query_cols, HD, 0)
        query_halves.append(rope(projected[:, :query_cols], query_tables).astype(jnp.bfloat16))
        half_kv = jnp.stack([key_half, value_half])
        kv_halves.append(lax.dynamic_slice_in_dim(half_kv, (spot % 2) * quarter, quarter, 2))
        low_half = (spot // 2) % 2 == 0
        window_list = [
            joined(half_kv, lax.ppermute(half_kv, "gx", partner_route(gx_count, quarters, 2)), low_half)
        ]
        for shift_by in range(1, span_count + 1):
            route = []
            for i in range(gx_count):
                peer = i - i % quarters + ((i % quarters) ^ 2)
                for j in range(gy_count - shift_by):
                    route.append((i * gy_count + j, peer * gy_count + j + shift_by))
            same = shifted(half_kv, "gy", shift_by)
            other = lax.ppermute(half_kv, ("gx", "gy"), route)
            window_list.insert(0, joined(same, other, low_half))
        held = jnp.concatenate(window_list, axis=1)
        head_halves.append(held.reshape(2, span_count + 1, half_rows, HD))
    queries = jnp.concatenate(query_halves, axis=0)
    own_kv = jnp.concatenate(kv_halves, axis=1)
    key_piece = own_kv[0]
    value_piece = own_kv[1]
    window_kv = jnp.stack(head_halves, axis=2).reshape(2, (span_count + 1) * token_count, HD)
    window_keys = window_kv[0]
    window_values = window_kv[1]
    window_marks = jnp.concatenate(mark_list, axis=0)
    reach_rows = span_count * token_count
    query_rows = (
        queries.reshape(token_count, head_local, HD)
        .transpose(1, 0, 2)
        .reshape(head_local * token_count, HD)
    )
    scores = lax.dot_general(
        query_rows, window_keys, (((1,), (1,)), ((), ())), preferred_element_type=jnp.float32
    ) * HD ** (-0.5)
    query_marks = jnp.tile(segment_ids, head_local)
    query_place = jnp.tile(jnp.arange(token_count, dtype=jnp.int32), head_local)
    key_place = jnp.arange(window_keys.shape[0], dtype=jnp.int32)
    allowed = (window_marks[None, :] == query_marks[:, None] + 1) & (window_marks[None, :] > 0)
    allowed = allowed & (key_place[None, :] <= query_place[:, None] + reach_rows)
    allowed = lax.optimization_barrier(allowed)
    masked = jnp.where(allowed, scores, MASKED)
    highest = jnp.max(masked, axis=1, keepdims=True)
    exponent = jnp.exp(masked - highest)
    totals = jnp.sum(exponent, axis=1)
    weights = exponent.astype(jnp.bfloat16)
    summed = jnp.dot(weights, window_values, preferred_element_type=jnp.float32)
    result = summed / totals[:, None]
    result = jnp.where((query_marks >= 0)[:, None], result, 0.0)
    context = (
        result.reshape(head_local, token_count, HD)
        .transpose(1, 0, 2)
        .reshape(token_count, head_local * HD)
        .astype(jnp.bfloat16)
    )
    owner_count = gy_count
    page_rows = token_count // PAGE
    capacity = max(2, 2 * page_rows // owner_count)
    owner_of = page_owner[:, 0]
    one_hot = (owner_of[:, None] == jnp.arange(owner_count, dtype=jnp.int32)[None, :]).astype(
        jnp.int32
    )
    earlier = jnp.cumsum(one_hot, axis=0) - one_hot
    rank_in = jnp.sum(earlier * one_hot, axis=1)
    slot_of = owner_of * capacity + rank_in
    kv_pages = own_kv.reshape(2, page_rows, PAGE * quarter).transpose(1, 0, 2)
    send_kv = (
        jnp.zeros((owner_count * capacity, 2, PAGE * quarter), jnp.bfloat16)
        .at[slot_of]
        .set(kv_pages)
    )
    send_kv = send_kv.reshape(owner_count, capacity, 2, PAGE * quarter)
    got_kv = lax.all_to_all(send_kv, "gy", split_axis=0, concat_axis=0, tiled=True)
    got_kv, context = lax.optimization_barrier((got_kv, context))
    got_kv = got_kv.reshape(owner_count * capacity, 2, PAGE, quarter)
    key_cache = got_kv[:, 0]
    value_cache = got_kv[:, 1]
    return (context, key_cache, value_cache)


def solution(mesh):
    placed = (
        P("gy", "gx"),
        P(),
        P("gy", "gx"),
        P("gy", "gx"),
        P("gy", "gx"),
        P("gy"),
        P("gy"),
        P("gy", None),
    )
    return jax.shard_map(
        shards,
        mesh=mesh,
        in_specs=placed,
        out_specs=(P("gy", "gx"), P("gy", None, "gx"), P("gy", None, "gx")),
        check_vma=False,
    )
```

```python
import jax
import jax.numpy as jnp
from jax import lax
from jax.sharding import PartitionSpec as P

D = 8192
HD = 128
PAGE = 16


EPSILON = 1e-05
THETA = 500000.0
MASKED = -1e30


def shifted(value, axis, by):
    count = lax.axis_size(axis)
    pairs = [(i, i + by) for i in range(count) if 0 <= i + by < count]
    return lax.ppermute(value, axis, pairs)


def partner_route(count, group, k):
    route = []
    for i in range(count):
        base = i - i % group
        route.append((i, base + ((i % group) ^ k)))
    return route


def rope_tables(places, count, width, first_pair):
    cols = jnp.arange(count, dtype=jnp.int32)
    pair_index = first_pair + (cols % width) // 2
    frequency = jnp.power(THETA, -(2.0 * pair_index.astype(jnp.float32)) / HD)
    angles = places.astype(jnp.float32)[:, None] * frequency[None, :]
    return lax.optimization_barrier((jnp.cos(angles), jnp.sin(angles)))


def rope(matrix, tables):
    cosine, sine_of = tables
    cols = jnp.arange(matrix.shape[1], dtype=jnp.int32)
    following = jnp.roll(matrix, -1, axis=1)
    preceding = jnp.roll(matrix, 1, axis=1)
    even = (cols % 2 == 0)[None, :]
    return jnp.where(
        even, matrix * cosine - following * sine_of, matrix * cosine + preceding * sine_of
    )


def joined(mine, theirs, mine_first):
    return jnp.where(
        mine_first,
        jnp.concatenate([mine, theirs], axis=-1),
        jnp.concatenate([theirs, mine], axis=-1),
    )


def shards(
    tokens_in, norm_gain, query_weight, key_weight, value_weight, segment_ids, positions, page_owner
):
    token_count = tokens_in.shape[0]
    quarter = key_weight.shape[1]
    head_local = query_weight.shape[1] // HD
    quarters = HD // quarter
    gx_count = lax.axis_size("gx")
    gy_count = lax.axis_size("gy")
    spot = lax.axis_index("gx") % quarters
    my_gy = lax.axis_index("gy")
    row_block = query_weight.shape[0]

    kv_weights = jnp.stack([key_weight, value_weight])
    sibling = lax.ppermute(kv_weights, "gx", partner_route(gx_count, quarters, 1))
    half_weights = joined(kv_weights, sibling, spot % 2 == 0)
    local_weights = jnp.concatenate([query_weight, half_weights[0], half_weights[1]], axis=1)
    half_cols = 2 * quarter
    pieces = [(my_gy, local_weights)]
    for k in range(1, gy_count):
        got = lax.ppermute(local_weights, "gy", partner_route(gy_count, gy_count, k))
        pieces.append((my_gy ^ k, got))

    local_float = tokens_in.astype(jnp.float32)
    my_gx = lax.axis_index("gx")
    feature_block = tokens_in.shape[1]
    local_gain = lax.dynamic_slice_in_dim(norm_gain, my_gx * feature_block, feature_block, 0)
    local_normed = (local_float * local_gain.astype(jnp.float32)[None, :]).astype(jnp.bfloat16)
    local_normed, local_float = lax.optimization_barrier((local_normed, local_float))
    local_squares = jnp.sum(local_float * local_float, axis=1)
    square_parts = [local_squares]
    for k in range(1, gx_count):
        square_parts.append(lax.ppermute(local_squares, "gx", partner_route(gx_count, gx_count, k)))
    square_order = jnp.arange(gx_count, dtype=jnp.int32) ^ my_gx
    squares = jnp.sum(jnp.take(jnp.stack(square_parts), square_order, axis=0), axis=0)
    span_count = gy_count // 4
    marks = segment_ids + 1
    mark_list = [marks]
    for shift_by in range(1, span_count + 1):
        mark_list.insert(0, shifted(marks, "gy", shift_by))
    scaling = 1.0 / jnp.sqrt(squares / D + EPSILON)
    query_cols = head_local * HD
    halves = 1
    half_rows = token_count // halves
    query_halves, kv_halves, head_halves = [], [], []
    for h in range(halves):
        rows_of = slice(h * half_rows, (h + 1) * half_rows)
        normed = lax.all_gather(local_normed[rows_of], "gx", axis=0, tiled=False)
        per_piece = row_block // feature_block
        normed = normed.reshape(gx_count // per_piece, per_piece, half_rows, feature_block)
        if head_halves:
            normed, head_halves[-1] = lax.optimization_barrier((normed, head_halves[-1]))
        products = None
        for source, block in pieces:
            rows = lax.dynamic_index_in_dim(normed, source, 0, keepdims=False)
            weights_of = block.reshape(per_piece, feature_block, block.shape[1])
            part = jnp.einsum("btd,bdc->tc", rows, weights_of, preferred_element_type=jnp.float32)
            products = part if products is None else products + part
        projected = products * scaling[rows_of, None]
        places = positions[rows_of]
        key_tables = rope_tables(places, half_cols, half_cols, (spot // 2) * quarter)
        key_half = rope(projected[:, query_cols : query_cols + half_cols], key_tables)
        key_half = key_half.astype(jnp.bfloat16)
        value_half = projected[:, query_cols + half_cols :].astype(jnp.bfloat16)
        query_tables = rope_tables(places, query_cols, HD, 0)
        query_halves.append(rope(projected[:, :query_cols], query_tables).astype(jnp.bfloat16))
        half_kv = jnp.stack([key_half, value_half])
        kv_halves.append(lax.dynamic_slice_in_dim(half_kv, (spot % 2) * quarter, quarter, 2))
        low_half = (spot // 2) % 2 == 0
        window_list = [
            joined(half_kv, lax.ppermute(half_kv, "gx", partner_route(gx_count, quarters, 2)), low_half)
        ]
        for shift_by in range(1, span_count + 1):
            route = []
            for i in range(gx_count):
                peer = i - i % quarters + ((i % quarters) ^ 2)
                for j in range(gy_count - shift_by):
                    route.append((i * gy_count + j, peer * gy_count + j + shift_by))
            same = shifted(half_kv, "gy", shift_by)
            other = lax.ppermute(half_kv, ("gx", "gy"), route)
            window_list.insert(0, joined(same, other, low_half))
        held = jnp.concatenate(window_list, axis=1)
        head_halves.append(held.reshape(2, span_count + 1, half_rows, HD))
    queries = jnp.concatenate(query_halves, axis=0)
    own_kv = jnp.concatenate(kv_halves, axis=1)
    key_piece = own_kv[0]
    value_piece = own_kv[1]
    window_kv = jnp.stack(head_halves, axis=2).reshape(2, (span_count + 1) * token_count, HD)
    window_keys = window_kv[0]
    window_values = window_kv[1]
    window_marks = jnp.concatenate(mark_list, axis=0)
    reach_rows = span_count * token_count
    query_rows = (
        queries.reshape(token_count, head_local, HD)
        .transpose(1, 0, 2)
        .reshape(head_local * token_count, HD)
    )
    scores = lax.dot_general(
        query_rows, window_keys, (((1,), (1,)), ((), ())), preferred_element_type=jnp.float32
    ) * HD ** (-0.5)
    query_marks = jnp.tile(segment_ids, head_local)
    query_place = jnp.tile(jnp.arange(token_count, dtype=jnp.int32), head_local)
    key_place = jnp.arange(window_keys.shape[0], dtype=jnp.int32)
    allowed = (window_marks[None, :] == query_marks[:, None] + 1) & (window_marks[None, :] > 0)
    allowed = allowed & (key_place[None, :] <= query_place[:, None] + reach_rows)
    allowed = lax.optimization_barrier(allowed)
    masked = jnp.where(allowed, scores, MASKED)
    highest = jnp.max(masked, axis=1, keepdims=True)
    exponent = jnp.exp(masked - highest)
    totals = jnp.sum(exponent, axis=1)
    weights = exponent.astype(jnp.bfloat16)
    summed = jnp.dot(weights, window_values, preferred_element_type=jnp.float32)
    result = summed / totals[:, None]
    result = jnp.where((query_marks >= 0)[:, None], result, 0.0)
    context = (
        result.reshape(head_local, token_count, HD)
        .transpose(1, 0, 2)
        .reshape(token_count, head_local * HD)
        .astype(jnp.bfloat16)
    )
    owner_count = gy_count
    page_rows = token_count // PAGE
    capacity = max(2, 2 * page_rows // owner_count)
    owner_of = page_owner[:, 0]
    one_hot = (owner_of[:, None] == jnp.arange(owner_count, dtype=jnp.int32)[None, :]).astype(
        jnp.int32
    )
    earlier = jnp.cumsum(one_hot, axis=0) - one_hot
    rank_in = jnp.sum(earlier * one_hot, axis=1)
    slot_of = owner_of * capacity + rank_in
    kv_pages = own_kv.reshape(2, page_rows, PAGE * quarter).transpose(1, 0, 2)
    slot_ids = jnp.arange(owner_count * capacity, dtype=jnp.int32)
    placing = (slot_ids[:, None] == slot_of[None, :]).astype(jnp.bfloat16)
    send_kv = jnp.einsum(
        "sp,pkc->skc", placing, kv_pages, preferred_element_type=jnp.float32
    ).astype(jnp.bfloat16)
    send_kv = send_kv.reshape(owner_count, capacity, 2, PAGE * quarter)
    got_kv = lax.all_to_all(send_kv, "gy", split_axis=0, concat_axis=0, tiled=True)
    got_kv, context = lax.optimization_barrier((got_kv, context))
    got_kv = got_kv.reshape(owner_count * capacity, 2, PAGE, quarter)
    key_cache = got_kv[:, 0]
    value_cache = got_kv[:, 1]
    return (context, key_cache, value_cache)


def solution(mesh):
    placed = (
        P("gy", "gx"),
        P(),
        P("gy", "gx"),
        P("gy", "gx"),
        P("gy", "gx"),
        P("gy"),
        P("gy"),
        P("gy", None),
    )
    return jax.shard_map(
        shards,
        mesh=mesh,
        in_specs=placed,
        out_specs=(P("gy", "gx"), P("gy", None, "gx"), P("gy", None, "gx")),
        check_vma=False,
    )
```

```python
import jax
import jax.numpy as jnp
from jax import lax
from jax.sharding import PartitionSpec as P

D = 8192
HD = 128
PAGE = 16


EPSILON = 1e-05
THETA = 500000.0
MASKED = -1e30


def shifted(value, axis, by):
    count = lax.axis_size(axis)
    pairs = [(i, i + by) for i in range(count) if 0 <= i + by < count]
    return lax.ppermute(value, axis, pairs)


def partner_route(count, group, k):
    route = []
    for i in range(count):
        base = i - i % group
        route.append((i, base + ((i % group) ^ k)))
    return route


def rope_tables(places, count, width, first_pair):
    cols = jnp.arange(count, dtype=jnp.int32)
    pair_index = first_pair + (cols % width) // 2
    frequency = jnp.power(THETA, -(2.0 * pair_index.astype(jnp.float32)) / HD)
    angles = places.astype(jnp.float32)[:, None] * frequency[None, :]
    return lax.optimization_barrier((jnp.cos(angles), jnp.sin(angles)))


def rope(matrix, tables):
    cosine, sine_of = tables
    cols = jnp.arange(matrix.shape[1], dtype=jnp.int32)
    following = jnp.roll(matrix, -1, axis=1)
    preceding = jnp.roll(matrix, 1, axis=1)
    even = (cols % 2 == 0)[None, :]
    return jnp.where(
        even, matrix * cosine - following * sine_of, matrix * cosine + preceding * sine_of
    )


def joined(mine, theirs, mine_first):
    return jnp.where(
        mine_first,
        jnp.concatenate([mine, theirs], axis=-1),
        jnp.concatenate([theirs, mine], axis=-1),
    )


def shards(
    tokens_in, norm_gain, query_weight, key_weight, value_weight, segment_ids, positions, page_owner
):
    token_count = tokens_in.shape[0]
    quarter = key_weight.shape[1]
    head_local = query_weight.shape[1] // HD
    quarters = HD // quarter
    gx_count = lax.axis_size("gx")
    gy_count = lax.axis_size("gy")
    spot = lax.axis_index("gx") % quarters
    my_gy = lax.axis_index("gy")
    row_block = query_weight.shape[0]

    kv_weights = jnp.stack([key_weight, value_weight])
    sibling = lax.ppermute(kv_weights, "gx", partner_route(gx_count, quarters, 1))
    half_weights = joined(kv_weights, sibling, spot % 2 == 0)
    local_weights = jnp.concatenate([query_weight, half_weights[0], half_weights[1]], axis=1)
    half_cols = 2 * quarter
    pieces = [(my_gy, local_weights)]
    for k in range(1, gy_count):
        got = lax.ppermute(local_weights, "gy", partner_route(gy_count, gy_count, k))
        pieces.append((my_gy ^ k, got))

    local_float = tokens_in.astype(jnp.float32)
    my_gx = lax.axis_index("gx")
    feature_block = tokens_in.shape[1]
    gain_rows = norm_gain.reshape(gx_count, feature_block)
    local_gain = lax.dynamic_index_in_dim(gain_rows, my_gx, 0, keepdims=False)
    local_normed = (local_float * local_gain.astype(jnp.float32)[None, :]).astype(jnp.bfloat16)
    local_normed, local_float = lax.optimization_barrier((local_normed, local_float))
    local_squares = jnp.sum(local_float * local_float, axis=1)
    square_parts = [local_squares]
    for k in range(1, gx_count):
        square_parts.append(lax.ppermute(local_squares, "gx", partner_route(gx_count, gx_count, k)))
    square_order = jnp.arange(gx_count, dtype=jnp.int32) ^ my_gx
    squares = jnp.sum(jnp.take(jnp.stack(square_parts), square_order, axis=0), axis=0)
    span_count = gy_count // 4
    marks = segment_ids + 1
    mark_list = [marks]
    for shift_by in range(1, span_count + 1):
        mark_list.insert(0, shifted(marks, "gy", shift_by))
    scaling = 1.0 / jnp.sqrt(squares / D + EPSILON)
    query_cols = head_local * HD
    halves = 1
    half_rows = token_count // halves
    query_halves, kv_halves, head_halves = [], [], []
    for h in range(halves):
        rows_of = slice(h * half_rows, (h + 1) * half_rows)
        normed = lax.all_gather(local_normed[rows_of], "gx", axis=0, tiled=False)
        per_piece = row_block // feature_block
        normed = normed.reshape(gx_count // per_piece, per_piece, half_rows, feature_block)
        if head_halves:
            normed, head_halves[-1] = lax.optimization_barrier((normed, head_halves[-1]))
        products = None
        for source, block in pieces:
            rows = lax.dynamic_index_in_dim(normed, source, 0, keepdims=False)
            weights_of = block.reshape(per_piece, feature_block, block.shape[1])
            part = jnp.einsum("btd,bdc->tc", rows, weights_of, preferred_element_type=jnp.float32)
            products = part if products is None else products + part
        projected = products * scaling[rows_of, None]
        places = positions[rows_of]
        key_tables = rope_tables(places, half_cols, half_cols, (spot // 2) * quarter)
        key_half = rope(projected[:, query_cols : query_cols + half_cols], key_tables)
        key_half = key_half.astype(jnp.bfloat16)
        value_half = projected[:, query_cols + half_cols :].astype(jnp.bfloat16)
        query_tables = rope_tables(places, query_cols, HD, 0)
        query_halves.append(rope(projected[:, :query_cols], query_tables).astype(jnp.bfloat16))
        half_kv = jnp.stack([key_half, value_half])
        kv_halves.append(lax.dynamic_slice_in_dim(half_kv, (spot % 2) * quarter, quarter, 2))
        low_half = (spot // 2) % 2 == 0
        window_list = [
            joined(half_kv, lax.ppermute(half_kv, "gx", partner_route(gx_count, quarters, 2)), low_half)
        ]
        for shift_by in range(1, span_count + 1):
            route = []
            for i in range(gx_count):
                peer = i - i % quarters + ((i % quarters) ^ 2)
                for j in range(gy_count - shift_by):
                    route.append((i * gy_count + j, peer * gy_count + j + shift_by))
            same = shifted(half_kv, "gy", shift_by)
            other = lax.ppermute(half_kv, ("gx", "gy"), route)
            window_list.insert(0, joined(same, other, low_half))
        held = jnp.concatenate(window_list, axis=1)
        head_halves.append(held.reshape(2, span_count + 1, half_rows, HD))
    queries = jnp.concatenate(query_halves, axis=0)
    own_kv = jnp.concatenate(kv_halves, axis=1)
    key_piece = own_kv[0]
    value_piece = own_kv[1]
    window_kv = jnp.stack(head_halves, axis=2).reshape(2, (span_count + 1) * token_count, HD)
    window_keys = window_kv[0]
    window_values = window_kv[1]
    window_marks = jnp.concatenate(mark_list, axis=0)
    reach_rows = span_count * token_count
    query_rows = (
        queries.reshape(token_count, head_local, HD)
        .transpose(1, 0, 2)
        .reshape(head_local * token_count, HD)
    )
    scores = lax.dot_general(
        query_rows, window_keys, (((1,), (1,)), ((), ())), preferred_element_type=jnp.float32
    ) * HD ** (-0.5)
    query_marks = jnp.tile(segment_ids, head_local)
    query_place = jnp.tile(jnp.arange(token_count, dtype=jnp.int32), head_local)
    key_place = jnp.arange(window_keys.shape[0], dtype=jnp.int32)
    allowed = (window_marks[None, :] == query_marks[:, None] + 1) & (window_marks[None, :] > 0)
    allowed = allowed & (key_place[None, :] <= query_place[:, None] + reach_rows)
    allowed = lax.optimization_barrier(allowed)
    masked = jnp.where(allowed, scores, MASKED)
    highest = jnp.max(masked, axis=1, keepdims=True)
    exponent = jnp.exp(masked - highest)
    totals = jnp.sum(exponent, axis=1)
    weights = exponent.astype(jnp.bfloat16)
    summed = jnp.dot(weights, window_values, preferred_element_type=jnp.float32)
    result = summed / totals[:, None]
    result = jnp.where((query_marks >= 0)[:, None], result, 0.0)
    context = (
        result.reshape(head_local, token_count, HD)
        .transpose(1, 0, 2)
        .reshape(token_count, head_local * HD)
        .astype(jnp.bfloat16)
    )
    owner_count = gy_count
    page_rows = token_count // PAGE
    capacity = max(2, 2 * page_rows // owner_count)
    owner_of = page_owner[:, 0]
    one_hot = (owner_of[:, None] == jnp.arange(owner_count, dtype=jnp.int32)[None, :]).astype(
        jnp.int32
    )
    earlier = jnp.cumsum(one_hot, axis=0) - one_hot
    rank_in = jnp.sum(earlier * one_hot, axis=1)
    slot_of = owner_of * capacity + rank_in
    kv_pages = own_kv.reshape(2, page_rows, PAGE * quarter).transpose(1, 0, 2)
    send_kv = (
        jnp.zeros((owner_count * capacity, 2, PAGE * quarter), jnp.bfloat16)
        .at[slot_of]
        .set(kv_pages)
    )
    send_kv = send_kv.reshape(owner_count, capacity, 2, PAGE * quarter)
    got_kv = lax.all_to_all(send_kv, "gy", split_axis=0, concat_axis=0, tiled=True)
    got_kv, context = lax.optimization_barrier((got_kv, context))
    got_kv = got_kv.reshape(owner_count * capacity, 2, PAGE, quarter)
    key_cache = got_kv[:, 0]
    value_cache = got_kv[:, 1]
    return (context, key_cache, value_cache)


def solution(mesh):
    placed = (
        P("gy", "gx"),
        P(),
        P("gy", "gx"),
        P("gy", "gx"),
        P("gy", "gx"),
        P("gy"),
        P("gy"),
        P("gy", None),
    )
    return jax.shard_map(
        shards,
        mesh=mesh,
        in_specs=placed,
        out_specs=(P("gy", "gx"), P("gy", None, "gx"), P("gy", None, "gx")),
        check_vma=False,
    )
```

```python
import jax
import jax.numpy as jnp
from jax import lax
from jax.sharding import PartitionSpec as P

D = 8192
HD = 128
PAGE = 16


EPSILON = 1e-05
THETA = 500000.0
MASKED = -1e30


def shifted(value, axis, by):
    count = lax.axis_size(axis)
    pairs = [(i, i + by) for i in range(count) if 0 <= i + by < count]
    return lax.ppermute(value, axis, pairs)


def partner_route(count, group, k):
    route = []
    for i in range(count):
        base = i - i % group
        route.append((i, base + ((i % group) ^ k)))
    return route


def rope_tables(places, count, width, first_pair):
    cols = jnp.arange(count, dtype=jnp.int32)
    pair_index = first_pair + (cols % width) // 2
    frequency = jnp.power(THETA, -(2.0 * pair_index.astype(jnp.float32)) / HD)
    angles = places.astype(jnp.float32)[:, None] * frequency[None, :]
    return lax.optimization_barrier((jnp.cos(angles), jnp.sin(angles)))


def rope(matrix, tables):
    cosine, sine_of = tables
    cols = jnp.arange(matrix.shape[1], dtype=jnp.int32)
    following = jnp.roll(matrix, -1, axis=1)
    preceding = jnp.roll(matrix, 1, axis=1)
    even = (cols % 2 == 0)[None, :]
    return jnp.where(
        even, matrix * cosine - following * sine_of, matrix * cosine + preceding * sine_of
    )


def joined(mine, theirs, mine_first):
    return jnp.where(
        mine_first,
        jnp.concatenate([mine, theirs], axis=-1),
        jnp.concatenate([theirs, mine], axis=-1),
    )


def shards(
    tokens_in, norm_gain, query_weight, key_weight, value_weight, segment_ids, positions, page_owner
):
    token_count = tokens_in.shape[0]
    quarter = key_weight.shape[1]
    head_local = query_weight.shape[1] // HD
    quarters = HD // quarter
    gx_count = lax.axis_size("gx")
    gy_count = lax.axis_size("gy")
    spot = lax.axis_index("gx") % quarters
    my_gy = lax.axis_index("gy")
    row_block = query_weight.shape[0]

    kv_weights = jnp.stack([key_weight, value_weight])
    sibling = lax.ppermute(kv_weights, "gx", partner_route(gx_count, quarters, 1))
    half_weights = joined(kv_weights, sibling, spot % 2 == 0)
    local_weights = jnp.concatenate([query_weight, half_weights[0], half_weights[1]], axis=1)
    half_cols = 2 * quarter
    pieces = [(my_gy, local_weights)]
    for k in range(1, gy_count):
        got = lax.ppermute(local_weights, "gy", partner_route(gy_count, gy_count, k))
        pieces.append((my_gy ^ k, got))

    local_float = tokens_in.astype(jnp.float32)
    my_gx = lax.axis_index("gx")
    feature_block = tokens_in.shape[1]
    local_gain = lax.dynamic_slice_in_dim(norm_gain, my_gx * feature_block, feature_block, 0)
    local_normed = (local_float * local_gain.astype(jnp.float32)[None, :]).astype(jnp.bfloat16)
    local_normed, local_float = lax.optimization_barrier((local_normed, local_float))
    local_squares = jnp.sum(local_float * local_float, axis=1)
    square_parts = [local_squares]
    for k in range(1, gx_count):
        square_parts.append(lax.ppermute(local_squares, "gx", partner_route(gx_count, gx_count, k)))
    square_order = jnp.arange(gx_count, dtype=jnp.int32) ^ my_gx
    squares = jnp.sum(jnp.take(jnp.stack(square_parts), square_order, axis=0), axis=0)
    span_count = gy_count // 4
    marks = segment_ids + 1
    mark_list = [marks]
    for shift_by in range(1, span_count + 1):
        mark_list.insert(0, shifted(marks, "gy", shift_by))
    scaling = 1.0 / jnp.sqrt(squares / D + EPSILON)
    query_cols = head_local * HD
    halves = 1
    half_rows = token_count // halves
    query_halves, kv_halves, head_halves = [], [], []
    for h in range(halves):
        rows_of = slice(h * half_rows, (h + 1) * half_rows)
        normed = lax.all_gather(local_normed[rows_of], "gx", axis=0, tiled=False)
        per_piece = row_block // feature_block
        normed = normed.reshape(gx_count // per_piece, per_piece, half_rows, feature_block)
        if head_halves:
            normed, head_halves[-1] = lax.optimization_barrier((normed, head_halves[-1]))
        products = None
        for source, block in pieces:
            rows = lax.dynamic_index_in_dim(normed, source, 0, keepdims=False)
            weights_of = block.reshape(per_piece, feature_block, block.shape[1])
            part = jnp.einsum("btd,bdc->tc", rows, weights_of, preferred_element_type=jnp.float32)
            products = part if products is None else products + part
        projected = products * scaling[rows_of, None]
        places = positions[rows_of]
        key_tables = rope_tables(places, half_cols, half_cols, (spot // 2) * quarter)
        key_half = rope(projected[:, query_cols : query_cols + half_cols], key_tables)
        key_half = key_half.astype(jnp.bfloat16)
        value_half = projected[:, query_cols + half_cols :].astype(jnp.bfloat16)
        query_tables = rope_tables(places, query_cols, HD, 0)
        query_halves.append(rope(projected[:, :query_cols], query_tables).astype(jnp.bfloat16))
        half_kv = jnp.stack([key_half, value_half])
        kv_halves.append(lax.dynamic_slice_in_dim(half_kv, (spot % 2) * quarter, quarter, 2))
        low_half = (spot // 2) % 2 == 0
        window_list = [
            joined(half_kv, lax.ppermute(half_kv, "gx", partner_route(gx_count, quarters, 2)), low_half)
        ]
        for shift_by in range(1, span_count + 1):
            route = []
            for i in range(gx_count):
                peer = i - i % quarters + ((i % quarters) ^ 2)
                for j in range(gy_count - shift_by):
                    route.append((i * gy_count + j, peer * gy_count + j + shift_by))
            same = shifted(half_kv, "gy", shift_by)
            other = lax.ppermute(half_kv, ("gx", "gy"), route)
            window_list.insert(0, joined(same, other, low_half))
        held = jnp.concatenate(window_list, axis=1)
        head_halves.append(held.reshape(2, span_count + 1, half_rows, HD))
    queries = jnp.concatenate(query_halves, axis=0)
    own_kv = jnp.concatenate(kv_halves, axis=1)
    key_piece = own_kv[0]
    value_piece = own_kv[1]
    window_kv = jnp.stack(head_halves, axis=2).reshape(2, (span_count + 1) * token_count, HD)
    window_keys = window_kv[0]
    window_rows = window_keys.shape[0]
    window_values = window_kv[1]
    window_marks = jnp.concatenate(mark_list, axis=0)
    reach_rows = span_count * token_count
    scores = jnp.einsum(
        "thd,ud->htu",
        queries.reshape(token_count, head_local, HD),
        window_keys,
        preferred_element_type=jnp.float32,
    ).reshape(head_local * token_count, window_rows) * HD ** (-0.5)
    query_marks = jnp.tile(segment_ids, head_local)
    query_place = jnp.tile(jnp.arange(token_count, dtype=jnp.int32), head_local)
    key_place = jnp.arange(window_keys.shape[0], dtype=jnp.int32)
    allowed = (window_marks[None, :] == query_marks[:, None] + 1) & (window_marks[None, :] > 0)
    allowed = allowed & (key_place[None, :] <= query_place[:, None] + reach_rows)
    allowed = lax.optimization_barrier(allowed)
    masked = jnp.where(allowed, scores, MASKED)
    highest = jnp.max(masked, axis=1, keepdims=True)
    exponent = jnp.exp(masked - highest)
    totals = jnp.sum(exponent, axis=1)
    weights = exponent.astype(jnp.bfloat16)
    summed = jnp.dot(weights, window_values, preferred_element_type=jnp.float32)
    result = summed / totals[:, None]
    result = jnp.where((query_marks >= 0)[:, None], result, 0.0)
    context = (
        result.reshape(head_local, token_count, HD)
        .transpose(1, 0, 2)
        .reshape(token_count, head_local * HD)
        .astype(jnp.bfloat16)
    )
    owner_count = gy_count
    page_rows = token_count // PAGE
    capacity = max(2, 2 * page_rows // owner_count)
    owner_of = page_owner[:, 0]
    one_hot = (owner_of[:, None] == jnp.arange(owner_count, dtype=jnp.int32)[None, :]).astype(
        jnp.int32
    )
    earlier = jnp.cumsum(one_hot, axis=0) - one_hot
    rank_in = jnp.sum(earlier * one_hot, axis=1)
    slot_of = owner_of * capacity + rank_in
    kv_pages = own_kv.reshape(2, page_rows, PAGE * quarter).transpose(1, 0, 2)
    send_kv = (
        jnp.zeros((owner_count * capacity, 2, PAGE * quarter), jnp.bfloat16)
        .at[slot_of]
        .set(kv_pages)
    )
    send_kv = send_kv.reshape(owner_count, capacity, 2, PAGE * quarter)
    got_kv = lax.all_to_all(send_kv, "gy", split_axis=0, concat_axis=0, tiled=True)
    got_kv, context = lax.optimization_barrier((got_kv, context))
    got_kv = got_kv.reshape(owner_count * capacity, 2, PAGE, quarter)
    key_cache = got_kv[:, 0]
    value_cache = got_kv[:, 1]
    return (context, key_cache, value_cache)


def solution(mesh):
    placed = (
        P("gy", "gx"),
        P(),
        P("gy", "gx"),
        P("gy", "gx"),
        P("gy", "gx"),
        P("gy"),
        P("gy"),
        P("gy", None),
    )
    return jax.shard_map(
        shards,
        mesh=mesh,
        in_specs=placed,
        out_specs=(P("gy", "gx"), P("gy", None, "gx"), P("gy", None, "gx")),
        check_vma=False,
    )
```

```python
import jax
import jax.numpy as jnp
from jax import lax
from jax.sharding import PartitionSpec as P

D = 8192
HD = 128
PAGE = 16


EPSILON = 1e-05
THETA = 500000.0
MASKED = -1e30


def shifted(value, axis, by):
    count = lax.axis_size(axis)
    pairs = [(i, i + by) for i in range(count) if 0 <= i + by < count]
    return lax.ppermute(value, axis, pairs)


def partner_route(count, group, k):
    route = []
    for i in range(count):
        base = i - i % group
        route.append((i, base + ((i % group) ^ k)))
    return route


def rope_tables(places, count, width, first_pair):
    cols = jnp.arange(count, dtype=jnp.int32)
    pair_index = first_pair + (cols % width) // 2
    frequency = jnp.power(THETA, -(2.0 * pair_index.astype(jnp.float32)) / HD)
    angles = places.astype(jnp.float32)[:, None] * frequency[None, :]
    return lax.optimization_barrier((jnp.cos(angles), jnp.sin(angles)))


def rope(matrix, tables):
    cosine, sine_of = tables
    cols = jnp.arange(matrix.shape[1], dtype=jnp.int32)
    following = jnp.roll(matrix, -1, axis=1)
    preceding = jnp.roll(matrix, 1, axis=1)
    even = (cols % 2 == 0)[None, :]
    return jnp.where(
        even, matrix * cosine - following * sine_of, matrix * cosine + preceding * sine_of
    )


def joined(mine, theirs, mine_first):
    return jnp.where(
        mine_first,
        jnp.concatenate([mine, theirs], axis=-1),
        jnp.concatenate([theirs, mine], axis=-1),
    )


def shards(
    tokens_in, norm_gain, query_weight, key_weight, value_weight, segment_ids, positions, page_owner
):
    token_count = tokens_in.shape[0]
    quarter = key_weight.shape[1]
    head_local = query_weight.shape[1] // HD
    quarters = HD // quarter
    gx_count = lax.axis_size("gx")
    gy_count = lax.axis_size("gy")
    spot = lax.axis_index("gx") % quarters
    my_gy = lax.axis_index("gy")
    row_block = query_weight.shape[0]

    kv_weights = jnp.stack([key_weight, value_weight])
    sibling = lax.ppermute(kv_weights, "gx", partner_route(gx_count, quarters, 1))
    half_weights = joined(kv_weights, sibling, spot % 2 == 0)
    local_weights = jnp.concatenate([query_weight, half_weights[0], half_weights[1]], axis=1)
    half_cols = 2 * quarter
    pieces = [(my_gy, local_weights)]
    for k in range(1, gy_count):
        got = lax.ppermute(local_weights, "gy", partner_route(gy_count, gy_count, k))
        pieces.append((my_gy ^ k, got))

    local_float = tokens_in.astype(jnp.float32)
    my_gx = lax.axis_index("gx")
    feature_block = tokens_in.shape[1]
    local_gain = lax.dynamic_slice_in_dim(norm_gain, my_gx * feature_block, feature_block, 0)
    local_normed = (local_float * local_gain.astype(jnp.float32)[None, :]).astype(jnp.bfloat16)
    local_normed, local_float = lax.optimization_barrier((local_normed, local_float))
    local_squares = jnp.sum(local_float * local_float, axis=1)
    square_parts = [local_squares]
    for k in range(1, gx_count):
        square_parts.append(lax.ppermute(local_squares, "gx", partner_route(gx_count, gx_count, k)))
    square_order = jnp.arange(gx_count, dtype=jnp.int32) ^ my_gx
    squares = jnp.sum(jnp.take(jnp.stack(square_parts), square_order, axis=0), axis=0)
    span_count = gy_count // 4
    marks = segment_ids + 1
    mark_list = [marks]
    for shift_by in range(1, span_count + 1):
        mark_list.insert(0, shifted(marks, "gy", shift_by))
    scaling = 1.0 / jnp.sqrt(squares / D + EPSILON)
    scaling = lax.optimization_barrier(scaling)
    query_cols = head_local * HD
    halves = 1
    half_rows = token_count // halves
    query_halves, kv_halves, head_halves = [], [], []
    for h in range(halves):
        rows_of = slice(h * half_rows, (h + 1) * half_rows)
        normed = lax.all_gather(local_normed[rows_of], "gx", axis=0, tiled=False)
        per_piece = row_block // feature_block
        normed = normed.reshape(gx_count // per_piece, per_piece, half_rows, feature_block)
        if head_halves:
            normed, head_halves[-1] = lax.optimization_barrier((normed, head_halves[-1]))
        products = None
        for source, block in pieces:
            rows = lax.dynamic_index_in_dim(normed, source, 0, keepdims=False)
            weights_of = block.reshape(per_piece, feature_block, block.shape[1])
            part = jnp.einsum("btd,bdc->tc", rows, weights_of, preferred_element_type=jnp.float32)
            products = part if products is None else products + part
        projected = products * scaling[rows_of, None]
        places = positions[rows_of]
        key_tables = rope_tables(places, half_cols, half_cols, (spot // 2) * quarter)
        key_half = rope(projected[:, query_cols : query_cols + half_cols], key_tables)
        key_half = key_half.astype(jnp.bfloat16)
        value_half = projected[:, query_cols + half_cols :].astype(jnp.bfloat16)
        query_tables = rope_tables(places, query_cols, HD, 0)
        query_halves.append(rope(projected[:, :query_cols], query_tables).astype(jnp.bfloat16))
        half_kv = jnp.stack([key_half, value_half])
        kv_halves.append(lax.dynamic_slice_in_dim(half_kv, (spot % 2) * quarter, quarter, 2))
        low_half = (spot // 2) % 2 == 0
        window_list = [
            joined(half_kv, lax.ppermute(half_kv, "gx", partner_route(gx_count, quarters, 2)), low_half)
        ]
        for shift_by in range(1, span_count + 1):
            route = []
            for i in range(gx_count):
                peer = i - i % quarters + ((i % quarters) ^ 2)
                for j in range(gy_count - shift_by):
                    route.append((i * gy_count + j, peer * gy_count + j + shift_by))
            same = shifted(half_kv, "gy", shift_by)
            other = lax.ppermute(half_kv, ("gx", "gy"), route)
            window_list.insert(0, joined(same, other, low_half))
        held = jnp.concatenate(window_list, axis=1)
        head_halves.append(held.reshape(2, span_count + 1, half_rows, HD))
    queries = jnp.concatenate(query_halves, axis=0)
    own_kv = jnp.concatenate(kv_halves, axis=1)
    key_piece = own_kv[0]
    value_piece = own_kv[1]
    window_kv = jnp.stack(head_halves, axis=2).reshape(2, (span_count + 1) * token_count, HD)
    window_keys = window_kv[0]
    window_values = window_kv[1]
    window_marks = jnp.concatenate(mark_list, axis=0)
    reach_rows = span_count * token_count
    query_rows = (
        queries.reshape(token_count, head_local, HD)
        .transpose(1, 0, 2)
        .reshape(head_local * token_count, HD)
    )
    scores = lax.dot_general(
        query_rows, window_keys, (((1,), (1,)), ((), ())), preferred_element_type=jnp.float32
    ) * HD ** (-0.5)
    query_marks = jnp.tile(segment_ids, head_local)
    query_place = jnp.tile(jnp.arange(token_count, dtype=jnp.int32), head_local)
    key_place = jnp.arange(window_keys.shape[0], dtype=jnp.int32)
    allowed = (window_marks[None, :] == query_marks[:, None] + 1) & (window_marks[None, :] > 0)
    allowed = allowed & (key_place[None, :] <= query_place[:, None] + reach_rows)
    allowed = lax.optimization_barrier(allowed)
    masked = jnp.where(allowed, scores, MASKED)
    highest = jnp.max(masked, axis=1, keepdims=True)
    exponent = jnp.exp(masked - highest)
    totals = jnp.sum(exponent, axis=1)
    weights = exponent.astype(jnp.bfloat16)
    summed = jnp.dot(weights, window_values, preferred_element_type=jnp.float32)
    result = summed / totals[:, None]
    result = jnp.where((query_marks >= 0)[:, None], result, 0.0)
    context = (
        result.reshape(head_local, token_count, HD)
        .transpose(1, 0, 2)
        .reshape(token_count, head_local * HD)
        .astype(jnp.bfloat16)
    )
    owner_count = gy_count
    page_rows = token_count // PAGE
    capacity = max(2, 2 * page_rows // owner_count)
    owner_of = page_owner[:, 0]
    one_hot = (owner_of[:, None] == jnp.arange(owner_count, dtype=jnp.int32)[None, :]).astype(
        jnp.int32
    )
    earlier = jnp.cumsum(one_hot, axis=0) - one_hot
    rank_in = jnp.sum(earlier * one_hot, axis=1)
    slot_of = owner_of * capacity + rank_in
    kv_pages = own_kv.reshape(2, page_rows, PAGE * quarter).transpose(1, 0, 2)
    send_kv = (
        jnp.zeros((owner_count * capacity, 2, PAGE * quarter), jnp.bfloat16)
        .at[slot_of]
        .set(kv_pages)
    )
    send_kv = send_kv.reshape(owner_count, capacity, 2, PAGE * quarter)
    got_kv = lax.all_to_all(send_kv, "gy", split_axis=0, concat_axis=0, tiled=True)
    got_kv, context = lax.optimization_barrier((got_kv, context))
    got_kv = got_kv.reshape(owner_count * capacity, 2, PAGE, quarter)
    key_cache = got_kv[:, 0]
    value_cache = got_kv[:, 1]
    return (context, key_cache, value_cache)


def solution(mesh):
    placed = (
        P("gy", "gx"),
        P(),
        P("gy", "gx"),
        P("gy", "gx"),
        P("gy", "gx"),
        P("gy"),
        P("gy"),
        P("gy", None),
    )
    return jax.shard_map(
        shards,
        mesh=mesh,
        in_specs=placed,
        out_specs=(P("gy", "gx"), P("gy", None, "gx"), P("gy", None, "gx")),
        check_vma=False,
    )
```
